32 devices in a mesh: tm: 4 (over x, core), space: 8 (over z, y).
Axes of the slice: x: 2, y: 2, z: 4, core: 2. Of those that a mesh axis runs over, the one named last changes fastest.
Arguments:
- age_field: float32 [8, 32, 24, 512], P('tm', 'space'), may hold values from -6 to 6
- source_term: float32 [8, 32, 24, 512], P('tm', 'space'), may hold values from -6 to 6
- conductivity: float32 [32, 24, 512], P('space'), may hold values from 0.2 to 2
- memory_weights: float32 [8], replicated, may hold values from 0 to 2.5, as said below
- eigenvalues: float32 [2, 8], replicated, may hold values from 0.25 to 1.5
Outputs:
- updated_age: float32 [8, 32, 24, 512], P('tm', 'space')
The draws below stay inside these ranges and needn't reach their ends.
Inputs may be any that keep to these rules, and one draw needn't show every extreme that they name: `memory_weights`: every weight is positive.
All inputs are finite; a program needn't handle non-finite values.
Results may differ from the reference program's by a relative error of at most 0.0003.
Values sent between devices are 32-bit elements; how exact they have to be, the bound alone decides.
No kernel may reach another device: no remote copies, remote signals or barrier semaphores. Data moves between devices by JAX's collectives and lax.ppermute only.
A program may use at most 64 MiB of HBM per device.

```python
import math
import jax
import jax.numpy as jnp
from jax import lax

NZ = 24
NY = 512
SWEEPS = 4
NT = 8
NX = 32


def draw_memory_weights(key, part):
    first_key, second_key = jax.random.split(jax.random.fold_in(key, 17))
    lag_values = jnp.arange(NT).astype(jnp.float32)
    factor = jax.random.uniform(first_key, (NT,), jnp.float32, 0.5, 1.5)
    present = jax.random.uniform(second_key, (), jnp.float32, 1.5, 2.5)
    tail_values = 0.3 * factor / jnp.sqrt(jnp.maximum(lag_values, 1.0))
    return jnp.where(lag_values > 0.5, tail_values, present).astype(jnp.float32)


def level_of(rng, extent, shards, least, high):
    factor_of, own = 1.0, jax.random.fold_in(rng, 6)
    for axis_at, shards_of in shards:
        draws = jnp.exp(jax.random.uniform(jax.random.fold_in(own, axis_at), (shards_of,), jnp.float32, least / len(shards), high / len(shards)))
        factor_of = factor_of * jnp.repeat(draws, extent[axis_at] // shards_of).reshape([-1 if axis == axis_at else 1 for axis in range(len(extent))])
    return factor_of


def gaussian(stream_key, dims, scale, most, shards=(), kind=jnp.bfloat16):
    values = jax.random.normal(stream_key, dims, jnp.float32) * scale
    if len(shards) > 0:
        values = level_of(stream_key, dims, shards, -0.22, 0.18) * values
    return jnp.clip(values, min=-most, max=most).astype(kind)


def setup_inputs(seed: int = 0) -> dict:
    splits = jax.random.split(jax.random.key(seed), 6)
    age_field = gaussian(splits[0], (NT, NX, NZ, NY), 1.0, 6.0, ((0, 4), (1, 8)), jnp.float32)
    source_term = gaussian(splits[1], (NT, NX, NZ, NY), 1.0, 6.0, ((0, 4), (1, 8)), jnp.float32)
    conductivity = jnp.clip(jnp.exp(math.log(2.0) - 2.3025851 * jax.random.uniform(splits[2], (NX, NZ, NY), jnp.float32) ** level_of(splits[2], (NX, NZ, NY), ((0, 8),), -0.2, 0.2)), 0.2, 2.0)
    memory_weights = draw_memory_weights(jax.random.fold_in(splits[5], 71), 0)
    eigenvalues = jnp.clip(jax.random.uniform(splits[4], (2, NT), jnp.float32, 0.25, 1.5), 0.25, 1.5)
    return {"age_field": age_field, "source_term": source_term, "conductivity": conductivity, "memory_weights": memory_weights, "eigenvalues": eigenvalues}


HIGHEST_PRECISION = lax.Precision.HIGHEST


def face_values(conductivity):
    padded = jnp.pad(conductivity, 1)
    centre = padded[1:-1, 1:-1, 1:-1]
    others = (padded[:-2, 1:-1, 1:-1], padded[2:, 1:-1, 1:-1], padded[1:-1, :-2, 1:-1],
              padded[1:-1, 2:, 1:-1], padded[1:-1, 1:-1, :-2], padded[1:-1, 1:-1, 2:])
    return tuple(0.5 * (centre + other_cell) for other_cell in others)


def face_sum(face_list):
    result = face_list[0]
    for one_face in face_list[1:]:
        result = result + one_face
    return result


def neighbour_sum(field, face_list):
    widths = [(0, 0)] * (field.ndim - 3) + [(1, 1)] * 3
    padded = jnp.pad(field, widths)
    shifted = (padded[..., :-2, 1:-1, 1:-1], padded[..., 2:, 1:-1, 1:-1], padded[..., 1:-1, :-2, 1:-1],
               padded[..., 1:-1, 2:, 1:-1], padded[..., 1:-1, 1:-1, :-2], padded[..., 1:-1, 1:-1, 2:])
    result = face_list[0] * shifted[0]
    for one_face, moved_field in zip(face_list[1:], shifted[1:]):
        result = result + one_face * moved_field
    return result


def transform_tables(count):
    index_values = jnp.arange(count, dtype=jnp.int32)
    products = (index_values[:, None] * index_values[None, :]) % count
    angles = (2.0 * math.pi / count) * products.astype(jnp.float32)
    return jnp.cos(angles), jnp.sin(angles)


def reference(age_field, source_term, conductivity, memory_weights, eigenvalues):
    face_list = face_values(conductivity)
    face_total = face_sum(face_list)
    steps_all = age_field.shape[0]
    spread = neighbour_sum(age_field, face_list) - face_total * age_field
    step_index = jnp.arange(steps_all, dtype=jnp.int32)
    lag_table = (step_index[:, None] - step_index[None, :]) % steps_all
    kernel = memory_weights[lag_table]
    held_memory = jnp.einsum("nj,jxzy->nxzy", kernel, age_field, precision=HIGHEST_PRECISION)
    residual = source_term + spread - held_memory
    cosine, sine_of = transform_tables(steps_all)
    spectrum_real = jnp.einsum("kn,nxzy->kxzy", cosine, residual, precision=HIGHEST_PRECISION)
    spectrum_imag = -jnp.einsum("kn,nxzy->kxzy", sine_of, residual, precision=HIGHEST_PRECISION)

    def solve_one(item_tuple):
        source_real, source_imag, eigen_real, eigen_imag = item_tuple
        shifted_real = eigen_real + face_total
        squared = shifted_real * shifted_real + eigen_imag * eigen_imag
        ratio_real = shifted_real / squared
        ratio_imag = eigen_imag / squared
        correction_real = jnp.zeros_like(source_real)
        correction_imag = jnp.zeros_like(source_imag)
        for sweep_number in range(SWEEPS):
            summed_real = source_real + neighbour_sum(correction_real, face_list)
            summed_imag = source_imag + neighbour_sum(correction_imag, face_list)
            correction_real = summed_real * ratio_real + summed_imag * ratio_imag
            correction_imag = summed_imag * ratio_real - summed_real * ratio_imag
        return correction_real, correction_imag

    solved_real, solved_imag = lax.map(solve_one, (spectrum_real, spectrum_imag, eigenvalues[0], eigenvalues[1]))
    rebuilt = (jnp.einsum("nk,kxzy->nxzy", cosine, solved_real, precision=HIGHEST_PRECISION)
               - jnp.einsum("nk,kxzy->nxzy", sine_of, solved_imag, precision=HIGHEST_PRECISION))
    return age_field + rebuilt / steps_all
```

```python
import math

import jax
import jax.numpy as jnp
from jax import lax
from jax.sharding import PartitionSpec as P

SWEEPS = 4


HIGHEST_PRECISION = lax.Precision.HIGHEST


def shift_pairs(count, step):
    return [(i, i + step) for i in range(count) if 0 <= i + step < count]


def halos(array, axis, dim):
    count = lax.axis_size(axis)
    length = array.shape[dim]
    last = lax.slice_in_dim(array, length - 1, length, axis=dim)
    first = lax.slice_in_dim(array, 0, 1, axis=dim)
    before = lax.ppermute(last, axis, shift_pairs(count, 1))
    after = lax.ppermute(first, axis, shift_pairs(count, -1))
    return before, after


def column_halos(array, axis):
    count = lax.axis_size(axis)
    lead = array.shape[:-1]
    size = math.prod(lead)
    flat = (size // 128, 128) if size % 128 == 0 else (size,)
    last = array[..., -1].reshape(flat)
    first = array[..., 0].reshape(flat)
    before = lax.ppermute(last, axis, shift_pairs(count, 1))
    after = lax.ppermute(first, axis, shift_pairs(count, -1))
    return before.reshape(lead + (1,)), after.reshape(lead + (1,))


def shifted_pair(field, before, after, dim):
    length = field.shape[dim]
    low = jnp.concatenate([before, lax.slice_in_dim(field, 0, length - 1, axis=dim)], axis=dim)
    high = jnp.concatenate([lax.slice_in_dim(field, 1, length, axis=dim), after], axis=dim)
    return low, high


def zero_shifted(field, dim):
    edge_shape = list(field.shape)
    edge_shape[dim] = 1
    zero = jnp.zeros(edge_shape, field.dtype)
    return shifted_pair(field, zero, zero, dim)


def neighbour_sum(field, faces, x_halo, y_halo):
    nd = field.ndim
    xm, xp = shifted_pair(field, x_halo[0], x_halo[1], nd - 3)
    zm, zp = zero_shifted(field, nd - 2)
    if y_halo is None:
        ym, yp = zero_shifted(field, nd - 1)
    else:
        ym, yp = shifted_pair(field, y_halo[0], y_halo[1], nd - 1)
    moved = (xm, xp, zm, zp, ym, yp)
    result = faces[0] * moved[0]
    for one_face, one_moved in zip(faces[1:], moved[1:]):
        result = result + one_face * one_moved
    return result


def shards(age_field, source_term, conductivity, memory_weights, eigenvalues):
    groups = lax.axis_size("tm")
    position = lax.axis_index("tm")
    steps_local, width_x, depth_z, length_y = age_field.shape
    total_steps = steps_local * groups
    chunk = length_y // groups

    cond_halo = halos(conductivity, "space", 0)
    age_halo = halos(age_field, "space", 1)

    c_low, c_high = shifted_pair(conductivity, cond_halo[0], cond_halo[1], 0)
    z_low, z_high = zero_shifted(conductivity, 1)
    y_low, y_high = zero_shifted(conductivity, 2)
    faces = tuple(0.5 * (conductivity + other) for other in (c_low, c_high, z_low, z_high, y_low, y_high))
    face_total = faces[0]
    for one_face in faces[1:]:
        face_total = face_total + one_face

    spread = neighbour_sum(age_field, faces, age_halo, None) - face_total * age_field
    partial = source_term + spread

    stacked = jnp.stack([partial, age_field])
    gathered = lax.all_to_all(stacked, "tm", 4, 1, tiled=True)
    gathered = gathered.reshape((2 * total_steps, width_x, depth_z, chunk))

    index_values = jnp.arange(total_steps, dtype=jnp.int32)
    products = index_values[:, None] * index_values[None, :] % total_steps
    angles = 2.0 * math.pi / total_steps * products.astype(jnp.float32)
    cosine = jnp.cos(angles)
    sine_of = jnp.sin(angles)
    forward = jnp.concatenate([cosine, -sine_of], axis=0)
    lag_table = (index_values[:, None] - index_values[None, :]) % total_steps
    circulant = memory_weights[lag_table]
    held_part = jnp.einsum("kn,nj->kj", forward, circulant, precision=HIGHEST_PRECISION)
    mixing = jnp.concatenate([forward, -held_part], axis=1)
    spectrum = jnp.einsum("km,mxzy->kxzy", mixing, gathered, precision=HIGHEST_PRECISION)
    spectrum = spectrum.reshape((2, total_steps, width_x, depth_z, chunk))

    start = position * chunk
    faces_y = tuple(lax.dynamic_slice_in_dim(one_face, start, chunk, axis=2) for one_face in faces)
    total_y = lax.dynamic_slice_in_dim(face_total, start, chunk, axis=2)
    shifted_real = eigenvalues[0][:, None, None, None] + total_y[None]
    eigen_imag = eigenvalues[1][:, None, None, None]
    squared = shifted_real * shifted_real + eigen_imag * eigen_imag
    ratio_real = shifted_real / squared
    ratio_imag = eigen_imag / squared

    summed = spectrum
    correction = None
    for sweep_number in range(SWEEPS):
        if sweep_number > 0:
            x_halo = halos(correction, "space", 2)
            y_halo = column_halos(correction, "tm")
            summed = spectrum + neighbour_sum(correction, faces_y, x_halo, y_halo)
        correction = jnp.stack(
            [
                summed[0] * ratio_real + summed[1] * ratio_imag,
                summed[1] * ratio_real - summed[0] * ratio_imag,
            ]
        )

    inverse = jnp.concatenate([cosine, -sine_of], axis=1) / total_steps
    flat_correction = correction.reshape((2 * total_steps, width_x, depth_z, chunk))
    update = jnp.einsum("nk,kxzy->nxzy", inverse, flat_correction, precision=HIGHEST_PRECISION)
    result_y = gathered[total_steps:] + update
    return lax.all_to_all(result_y, "tm", 0, 3, tiled=True)


def solution(mesh):
    in_specs = (
        P("tm", "space", None, None),
        P("tm", "space", None, None),
        P("space", None, None),
        P(),
        P(),
    )
    out_specs = P("tm", "space", None, None)
    return jax.shard_map(shards, mesh=mesh, in_specs=in_specs, out_specs=out_specs, check_vma=False)
```

```python
import math

import jax
import jax.numpy as jnp
from jax import lax
from jax.sharding import PartitionSpec as P

SWEEPS = 4


HIGHEST_PRECISION = lax.Precision.HIGHEST


def shift_pairs(count, step):
    return [(i, i + step) for i in range(count) if 0 <= i + step < count]


def halos(array, axis, dim):
    count = lax.axis_size(axis)
    length = array.shape[dim]
    last = lax.slice_in_dim(array, length - 1, length, axis=dim)
    first = lax.slice_in_dim(array, 0, 1, axis=dim)
    before = lax.ppermute(last, axis, shift_pairs(count, 1))
    after = lax.ppermute(first, axis, shift_pairs(count, -1))
    return before, after


def column_halos(array, axis):
    count = lax.axis_size(axis)
    before = lax.ppermute(array[..., -1], axis, shift_pairs(count, 1))
    after = lax.ppermute(array[..., 0], axis, shift_pairs(count, -1))
    return before[..., None], after[..., None]


def ring_pairs(count, step):
    return [(i, (i + step) % count) for i in range(count)]


def shifted_pair(field, before, after, dim):
    length = field.shape[dim]
    low = jnp.concatenate([before, lax.slice_in_dim(field, 0, length - 1, axis=dim)], axis=dim)
    high = jnp.concatenate([lax.slice_in_dim(field, 1, length, axis=dim), after], axis=dim)
    return low, high


def zero_shifted(field, dim):
    edge_shape = list(field.shape)
    edge_shape[dim] = 1
    zero = jnp.zeros(edge_shape, field.dtype)
    return shifted_pair(field, zero, zero, dim)


def neighbour_sum(field, faces, x_halo, y_halo):
    nd = field.ndim
    xm, xp = shifted_pair(field, x_halo[0], x_halo[1], nd - 3)
    zm, zp = zero_shifted(field, nd - 2)
    if y_halo is None:
        ym, yp = zero_shifted(field, nd - 1)
    else:
        ym, yp = shifted_pair(field, y_halo[0], y_halo[1], nd - 1)
    moved = (xm, xp, zm, zp, ym, yp)
    result = faces[0] * moved[0]
    for one_face, one_moved in zip(faces[1:], moved[1:]):
        result = result + one_face * one_moved
    return result


def shards(age_field, source_term, conductivity, memory_weights, eigenvalues):
    groups = lax.axis_size("tm")
    position = lax.axis_index("tm")
    steps_local, width_x, depth_z, length_y = age_field.shape
    total_steps = steps_local * groups
    chunk = length_y // groups

    cond_halo = halos(conductivity, "space", 0)
    age_halo = halos(age_field, "space", 1)

    c_low, c_high = shifted_pair(conductivity, cond_halo[0], cond_halo[1], 0)
    z_low, z_high = zero_shifted(conductivity, 1)
    y_low, y_high = zero_shifted(conductivity, 2)
    faces = tuple(0.5 * (conductivity + other) for other in (c_low, c_high, z_low, z_high, y_low, y_high))
    face_total = faces[0]
    for one_face in faces[1:]:
        face_total = face_total + one_face

    spread = neighbour_sum(age_field, faces, age_halo, None) - face_total * age_field
    partial = source_term + spread

    stacked = jnp.stack([partial, age_field])
    pieces = []
    for step in range(groups):
        target = (position + step) % groups
        piece = lax.dynamic_slice_in_dim(stacked, target * chunk, chunk, axis=4)
        if step > 0:
            piece = lax.ppermute(piece, "tm", ring_pairs(groups, step))
        pieces.append(piece)

    index_values = jnp.arange(total_steps, dtype=jnp.int32)
    products = index_values[:, None] * index_values[None, :] % total_steps
    angles = 2.0 * math.pi / total_steps * products.astype(jnp.float32)
    cosine = jnp.cos(angles)
    sine_of = jnp.sin(angles)
    forward = jnp.concatenate([cosine, -sine_of], axis=0)
    lag_table = (index_values[:, None] - index_values[None, :]) % total_steps
    circulant = memory_weights[lag_table]
    held_part = jnp.einsum("kn,nj->kj", forward, circulant, precision=HIGHEST_PRECISION)
    mixing = jnp.stack([forward, -held_part], axis=1).reshape(2 * total_steps, 2, groups, steps_local)
    spectrum = None
    for step in range(groups):
        source_device = (position - step) % groups
        columns = lax.dynamic_index_in_dim(mixing, source_device, axis=2, keepdims=False)
        term = jnp.einsum("kfl,flxzy->kxzy", columns, pieces[step], precision=HIGHEST_PRECISION)
        spectrum = term if spectrum is None else spectrum + term
    spectrum = spectrum.reshape((2, total_steps, width_x, depth_z, chunk))

    start = position * chunk
    faces_y = tuple(lax.dynamic_slice_in_dim(one_face, start, chunk, axis=2) for one_face in faces)
    total_y = lax.dynamic_slice_in_dim(face_total, start, chunk, axis=2)
    shifted_real = eigenvalues[0][:, None, None, None] + total_y[None]
    eigen_imag = eigenvalues[1][:, None, None, None]
    squared = shifted_real * shifted_real + eigen_imag * eigen_imag
    ratio_real, ratio_imag = lax.optimization_barrier((shifted_real / squared, eigen_imag / squared))

    summed = spectrum
    correction = None
    for sweep_number in range(SWEEPS):
        if sweep_number > 0:
            x_halo = halos(correction, "space", 2)
            y_halo = column_halos(correction, "tm")
            summed = spectrum + neighbour_sum(correction, faces_y, x_halo, y_halo)
        correction = jnp.stack(
            [
                summed[0] * ratio_real + summed[1] * ratio_imag,
                summed[1] * ratio_real - summed[0] * ratio_imag,
            ]
        )

    inverse = jnp.concatenate([cosine, -sine_of], axis=1) / total_steps
    inverse = inverse.reshape(groups, steps_local, 2, total_steps)
    back = []
    for step in range(groups):
        target = (position + step) % groups
        rows = lax.dynamic_index_in_dim(inverse, target, axis=0, keepdims=False)
        piece = jnp.einsum("lfk,fkxzy->lxzy", rows, correction, precision=HIGHEST_PRECISION)
        if step > 0:
            piece = lax.ppermute(piece, "tm", ring_pairs(groups, step))
        back.append(piece)
    arrived = jnp.stack(back)
    update = jnp.concatenate(
        [lax.dynamic_index_in_dim(arrived, (position - j) % groups, axis=0, keepdims=False) for j in range(groups)],
        axis=3,
    )
    return age_field + update


def solution(mesh):
    in_specs = (
        P("tm", "space", None, None),
        P("tm", "space", None, None),
        P("space", None, None),
        P(),
        P(),
    )
    out_specs = P("tm", "space", None, None)
    return jax.shard_map(shards, mesh=mesh, in_specs=in_specs, out_specs=out_specs, check_vma=False)
```

```python
import math

import jax
import jax.numpy as jnp
from jax import lax
from jax.sharding import PartitionSpec as P

SWEEPS = 4


HIGHEST_PRECISION = lax.Precision.HIGHEST


def shift_pairs(count, step):
    return [(i, i + step) for i in range(count) if 0 <= i + step < count]


def halos(array, axis, dim):
    count = lax.axis_size(axis)
    length = array.shape[dim]
    last = lax.slice_in_dim(array, length - 1, length, axis=dim)
    first = lax.slice_in_dim(array, 0, 1, axis=dim)
    before = lax.ppermute(last, axis, shift_pairs(count, 1))
    after = lax.ppermute(first, axis, shift_pairs(count, -1))
    return before, after


def column_halos(array, axis):
    count = lax.axis_size(axis)
    before = lax.ppermute(array[..., -1], axis, shift_pairs(count, 1))
    after = lax.ppermute(array[..., 0], axis, shift_pairs(count, -1))
    return before[..., None], after[..., None]


def ring_pairs(count, step):
    return [(i, (i + step) % count) for i in range(count)]


def shifted_pair(field, before, after, dim):
    length = field.shape[dim]
    low = jnp.concatenate([before, lax.slice_in_dim(field, 0, length - 1, axis=dim)], axis=dim)
    high = jnp.concatenate([lax.slice_in_dim(field, 1, length, axis=dim), after], axis=dim)
    return low, high


def zero_shifted(field, dim):
    edge_shape = list(field.shape)
    edge_shape[dim] = 1
    zero = jnp.zeros(edge_shape, field.dtype)
    return shifted_pair(field, zero, zero, dim)


def neighbour_sum(field, faces, x_halo, y_halo):
    nd = field.ndim
    xm, xp = shifted_pair(field, x_halo[0], x_halo[1], nd - 3)
    zm, zp = zero_shifted(field, nd - 2)
    if y_halo is None:
        ym, yp = zero_shifted(field, nd - 1)
    else:
        ym, yp = shifted_pair(field, y_halo[0], y_halo[1], nd - 1)
    moved = (xm, xp, zm, zp, ym, yp)
    result = faces[0] * moved[0]
    for one_face, one_moved in zip(faces[1:], moved[1:]):
        result = result + one_face * one_moved
    return result


def shards(age_field, source_term, conductivity, memory_weights, eigenvalues):
    groups = lax.axis_size("tm")
    position = lax.axis_index("tm")
    steps_local, width_x, depth_z, length_y = age_field.shape
    total_steps = steps_local * groups
    chunk = length_y // groups

    cond_halo = halos(conductivity, "space", 0)
    age_halo = halos(age_field, "space", 1)

    c_low, c_high = shifted_pair(conductivity, cond_halo[0], cond_halo[1], 0)
    z_low, z_high = zero_shifted(conductivity, 1)
    y_low, y_high = zero_shifted(conductivity, 2)
    faces = tuple(0.5 * (conductivity + other) for other in (c_low, c_high, z_low, z_high, y_low, y_high))
    face_total = faces[0]
    for one_face in faces[1:]:
        face_total = face_total + one_face

    spread = neighbour_sum(age_field, faces, age_halo, None) - face_total * age_field
    partial = source_term + spread

    stacked = jnp.stack([partial, age_field])
    index_values = jnp.arange(total_steps, dtype=jnp.int32)
    products = index_values[:, None] * index_values[None, :] % total_steps
    angles = 2.0 * math.pi / total_steps * products.astype(jnp.float32)
    cosine = jnp.cos(angles)
    sine_of = jnp.sin(angles)
    forward = jnp.concatenate([cosine, -sine_of], axis=0)
    lag_table = (index_values[:, None] - index_values[None, :]) % total_steps
    circulant = memory_weights[lag_table]
    held_part = jnp.einsum("kn,nj->kj", forward, circulant, precision=HIGHEST_PRECISION)
    mixing = jnp.stack([forward, -held_part], axis=1).reshape(2 * total_steps, 2, groups, steps_local)
    inverse = jnp.concatenate([cosine, -sine_of], axis=1) / total_steps
    inverse = inverse.reshape(groups, steps_local, 2, total_steps)
    common = (stacked, mixing, inverse, faces, face_total, eigenvalues, age_field)
    if depth_z % groups == 0:
        return z_split(*common)
    return y_split(*common)


def z_split(stacked, mixing, inverse, faces, face_total, eigenvalues, age_field):
    groups = lax.axis_size("tm")
    position = lax.axis_index("tm")
    _, steps_local, width_x, depth_z, length_y = stacked.shape
    total_steps = steps_local * groups
    rows = depth_z // groups

    pieces = []
    for step in range(groups):
        target = (position + step) % groups
        piece = lax.dynamic_slice_in_dim(stacked, target * rows, rows, axis=3)
        if step > 0:
            piece = lax.ppermute(piece, "tm", ring_pairs(groups, step))
        pieces.append(piece)

    mixing = mixing.reshape(2, total_steps, 2, groups, steps_local)
    spectrum = None
    for step in range(groups):
        source_device = (position - step) % groups
        columns = lax.dynamic_index_in_dim(mixing, source_device, axis=3, keepdims=False)
        for field in range(2):
            for local in range(steps_local):
                weight = columns[:, :, field, local][:, None, None, :, None]
                term = weight * pieces[step][field, local][None, :, :, None, :]
                spectrum = term if spectrum is None else spectrum + term

    start = position * rows
    faces_z = tuple(lax.dynamic_slice_in_dim(one_face, start, rows, axis=1)[:, :, None, :] for one_face in faces)
    total_z = lax.dynamic_slice_in_dim(face_total, start, rows, axis=1)[:, :, None, :]
    shifted_real = eigenvalues[0][None, None, :, None] + total_z
    eigen_imag = eigenvalues[1][None, None, :, None]
    squared = shifted_real * shifted_real + eigen_imag * eigen_imag
    ratio_real, ratio_imag = lax.optimization_barrier((shifted_real / squared, eigen_imag / squared))

    summed = spectrum
    correction = None
    for sweep_number in range(SWEEPS):
        if sweep_number > 0:
            x_low, x_high = halos(correction, "space", 1)
            z_low, z_high = halos(correction, "tm", 2)
            xm, xp = shifted_pair(correction, x_low, x_high, 1)
            zm, zp = shifted_pair(correction, z_low, z_high, 2)
            ym, yp = zero_shifted(correction, 4)
            moved = (xm, xp, zm, zp, ym, yp)
            total = faces_z[0] * moved[0]
            for one_face, one_moved in zip(faces_z[1:], moved[1:]):
                total = total + one_face * one_moved
            summed = spectrum + total
        correction = jnp.stack(
            [
                summed[0] * ratio_real + summed[1] * ratio_imag,
                summed[1] * ratio_real - summed[0] * ratio_imag,
            ]
        )

    back = []
    for step in range(groups):
        target = (position + step) % groups
        weights = lax.dynamic_index_in_dim(inverse, target, axis=0, keepdims=False)
        piece = jnp.einsum("lfk,fxzky->lxzy", weights, correction, precision=HIGHEST_PRECISION)
        if step > 0:
            piece = lax.ppermute(piece, "tm", ring_pairs(groups, step))
        back.append(piece)
    arrived = jnp.stack(back)
    update = jnp.concatenate(
        [lax.dynamic_index_in_dim(arrived, (position - j) % groups, axis=0, keepdims=False) for j in range(groups)],
        axis=2,
    )
    return age_field + update


def y_split(stacked, mixing, inverse, faces, face_total, eigenvalues, age_field):
    groups = lax.axis_size("tm")
    position = lax.axis_index("tm")
    _, steps_local, width_x, depth_z, length_y = stacked.shape
    total_steps = steps_local * groups
    chunk = length_y // groups

    pieces = []
    for step in range(groups):
        target = (position + step) % groups
        piece = lax.dynamic_slice_in_dim(stacked, target * chunk, chunk, axis=4)
        if step > 0:
            piece = lax.ppermute(piece, "tm", ring_pairs(groups, step))
        pieces.append(piece)

    spectrum = None
    for step in range(groups):
        source_device = (position - step) % groups
        columns = lax.dynamic_index_in_dim(mixing, source_device, axis=2, keepdims=False)
        term = jnp.einsum("kfl,flxzy->kxzy", columns, pieces[step], precision=HIGHEST_PRECISION)
        spectrum = term if spectrum is None else spectrum + term
    spectrum = spectrum.reshape((2, total_steps, width_x, depth_z, chunk))

    start = position * chunk
    faces_y = tuple(lax.dynamic_slice_in_dim(one_face, start, chunk, axis=2) for one_face in faces)
    total_y = lax.dynamic_slice_in_dim(face_total, start, chunk, axis=2)
    shifted_real = eigenvalues[0][:, None, None, None] + total_y[None]
    eigen_imag = eigenvalues[1][:, None, None, None]
    squared = shifted_real * shifted_real + eigen_imag * eigen_imag
    ratio_real, ratio_imag = lax.optimization_barrier((shifted_real / squared, eigen_imag / squared))

    summed = spectrum
    correction = None
    for sweep_number in range(SWEEPS):
        if sweep_number > 0:
            x_halo = halos(correction, "space", 2)
            y_halo = column_halos(correction, "tm")
            summed = spectrum + neighbour_sum(correction, faces_y, x_halo, y_halo)
        correction = jnp.stack(
            [
                summed[0] * ratio_real + summed[1] * ratio_imag,
                summed[1] * ratio_real - summed[0] * ratio_imag,
            ]
        )

    back = []
    for step in range(groups):
        target = (position + step) % groups
        rows = lax.dynamic_index_in_dim(inverse, target, axis=0, keepdims=False)
        piece = jnp.einsum("lfk,fkxzy->lxzy", rows, correction, precision=HIGHEST_PRECISION)
        if step > 0:
            piece = lax.ppermute(piece, "tm", ring_pairs(groups, step))
        back.append(piece)
    arrived = jnp.stack(back)
    update = jnp.concatenate(
        [lax.dynamic_index_in_dim(arrived, (position - j) % groups, axis=0, keepdims=False) for j in range(groups)],
        axis=3,
    )
    return age_field + update


def solution(mesh):
    in_specs = (
        P("tm", "space", None, None),
        P("tm", "space", None, None),
        P("space", None, None),
        P(),
        P(),
    )
    out_specs = P("tm", "space", None, None)
    return jax.shard_map(shards, mesh=mesh, in_specs=in_specs, out_specs=out_specs, check_vma=False)
```

```python
import math

import jax
import jax.numpy as jnp
from jax import lax
from jax.sharding import PartitionSpec as P

SWEEPS = 4


HIGHEST_PRECISION = lax.Precision.HIGHEST


def shift_pairs(count, step):
    return [(i, i + step) for i in range(count) if 0 <= i + step < count]


def halos(array, axis, dim):
    count = lax.axis_size(axis)
    length = array.shape[dim]
    last = lax.slice_in_dim(array, length - 1, length, axis=dim)
    first = lax.slice_in_dim(array, 0, 1, axis=dim)
    before = lax.ppermute(last, axis, shift_pairs(count, 1))
    after = lax.ppermute(first, axis, shift_pairs(count, -1))
    return before, after


def column_halos(array, axis):
    count = lax.axis_size(axis)
    before = lax.ppermute(array[..., -1], axis, shift_pairs(count, 1))
    after = lax.ppermute(array[..., 0], axis, shift_pairs(count, -1))
    return before[..., None], after[..., None]


def ring_pairs(count, step):
    return [(i, (i + step) % count) for i in range(count)]


def shifted_pair(field, before, after, dim):
    length = field.shape[dim]
    low = jnp.concatenate([before, lax.slice_in_dim(field, 0, length - 1, axis=dim)], axis=dim)
    high = jnp.concatenate([lax.slice_in_dim(field, 1, length, axis=dim), after], axis=dim)
    return low, high


def zero_shifted(field, dim):
    edge_shape = list(field.shape)
    edge_shape[dim] = 1
    zero = jnp.zeros(edge_shape, field.dtype)
    return shifted_pair(field, zero, zero, dim)


def neighbour_sum(field, faces, x_halo, y_halo):
    nd = field.ndim
    xm, xp = shifted_pair(field, x_halo[0], x_halo[1], nd - 3)
    zm, zp = zero_shifted(field, nd - 2)
    if y_halo is None:
        ym, yp = zero_shifted(field, nd - 1)
    else:
        ym, yp = shifted_pair(field, y_halo[0], y_halo[1], nd - 1)
    moved = (xm, xp, zm, zp, ym, yp)
    result = faces[0] * moved[0]
    for one_face, one_moved in zip(faces[1:], moved[1:]):
        result = result + one_face * one_moved
    return result


def face_halos(conductivity, age_field):
    count = lax.axis_size("space")
    width = conductivity.shape[0]
    last = jnp.concatenate([conductivity[width - 1 :][None], age_field[:, width - 1 :]], axis=0)
    first = jnp.concatenate([conductivity[:1][None], age_field[:, :1]], axis=0)
    before = lax.ppermute(last, "space", shift_pairs(count, 1))
    after = lax.ppermute(first, "space", shift_pairs(count, -1))
    return (before[0], after[0]), (before[1:], after[1:])


def phase_tables(products, count):
    angles = 2.0 * math.pi / count * (products % count).astype(jnp.float32)
    return jnp.cos(angles), jnp.sin(angles)


def shards(age_field, source_term, conductivity, memory_weights, eigenvalues):
    groups = lax.axis_size("tm")
    position = lax.axis_index("tm")
    steps_local, width_x, depth_z, length_y = age_field.shape
    total_steps = steps_local * groups

    cond_halo, age_halo = face_halos(conductivity, age_field)

    c_low, c_high = shifted_pair(conductivity, cond_halo[0], cond_halo[1], 0)
    z_low, z_high = zero_shifted(conductivity, 1)
    y_low, y_high = zero_shifted(conductivity, 2)
    faces = tuple(0.5 * (conductivity + other) for other in (c_low, c_high, z_low, z_high, y_low, y_high))
    face_total = faces[0]
    for one_face in faces[1:]:
        face_total = face_total + one_face

    spread = neighbour_sum(age_field, faces, age_halo, None) - face_total * age_field
    partial = source_term + spread
    stacked = jnp.stack([partial, age_field])

    frequency = jnp.arange(total_steps, dtype=jnp.int32)
    lag = jnp.arange(total_steps, dtype=jnp.int32)
    cos_w, sin_w = phase_tables(frequency[:, None] * lag[None, :], total_steps)
    weight_real = jnp.sum(memory_weights[None, :] * cos_w, axis=1)[:, None, None]
    weight_imag = -jnp.sum(memory_weights[None, :] * sin_w, axis=1)[:, None, None]
    piece = jnp.arange(groups, dtype=jnp.int32)[None, :, None]
    local = jnp.arange(steps_local, dtype=jnp.int32)[None, None, :]
    step_of = ((position - piece) % groups) * steps_local + local
    cos_f, sin_f = phase_tables(frequency[:, None, None] * step_of, total_steps)
    forward = (
        (cos_f, -sin_f),
        (-(weight_real * cos_f + weight_imag * sin_f), weight_real * sin_f - weight_imag * cos_f),
    )
    step_to = ((position + piece[0, :, :, None]) % groups) * steps_local + local[0, :, :, None]
    cos_i, sin_i = phase_tables(step_to * frequency[None, None, :], total_steps)
    inverse = jnp.stack([cos_i, -sin_i], axis=2) / total_steps

    common = (stacked, forward, inverse, faces, face_total, eigenvalues, age_field)
    if depth_z % groups == 0:
        return z_split(*common)
    return y_split(*common)


def z_split(stacked, forward, inverse, faces, face_total, eigenvalues, age_field):
    groups = lax.axis_size("tm")
    position = lax.axis_index("tm")
    _, steps_local, width_x, depth_z, length_y = stacked.shape
    total_steps = steps_local * groups
    rows = depth_z // groups

    pieces = []
    for step in range(groups):
        target = (position + step) % groups
        piece = lax.dynamic_slice_in_dim(stacked, target * rows, rows, axis=3)
        if step > 0:
            piece = lax.ppermute(piece, "tm", ring_pairs(groups, step))
        pieces.append(piece)

    halves = []
    for part in range(2):
        total = None
        for step in range(groups):
            for field in range(2):
                for local in range(steps_local):
                    weight = forward[field][part][:, step, local][None, None, :, None]
                    term = weight * pieces[step][field, local][:, :, None, :]
                    total = term if total is None else total + term
        halves.append(total)
    spectrum = jnp.stack(halves)

    start = position * rows
    faces_z = tuple(lax.dynamic_slice_in_dim(one_face, start, rows, axis=1)[:, :, None, :] for one_face in faces)
    total_z = lax.dynamic_slice_in_dim(face_total, start, rows, axis=1)[:, :, None, :]
    shifted_real = eigenvalues[0][None, None, :, None] + total_z
    eigen_imag = eigenvalues[1][None, None, :, None]
    squared = shifted_real * shifted_real + eigen_imag * eigen_imag
    ratio_real, ratio_imag = lax.optimization_barrier((shifted_real / squared, eigen_imag / squared))

    summed = spectrum
    correction = None
    for sweep_number in range(SWEEPS):
        if sweep_number > 0:
            x_low, x_high = halos(correction, "space", 1)
            z_low, z_high = halos(correction, "tm", 2)
            xm, xp = shifted_pair(correction, x_low, x_high, 1)
            zm, zp = shifted_pair(correction, z_low, z_high, 2)
            ym, yp = zero_shifted(correction, 4)
            moved = (xm, xp, zm, zp, ym, yp)
            total = faces_z[0] * moved[0]
            for one_face, one_moved in zip(faces_z[1:], moved[1:]):
                total = total + one_face * one_moved
            summed = spectrum + total
        correction = jnp.stack(
            [
                summed[0] * ratio_real + summed[1] * ratio_imag,
                summed[1] * ratio_real - summed[0] * ratio_imag,
            ]
        )

    back = []
    for step in range(groups):
        target = (position + step) % groups
        piece = jnp.einsum("lfk,fxzky->lxzy", inverse[step], correction, precision=HIGHEST_PRECISION)
        if step > 0:
            piece = lax.ppermute(piece, "tm", ring_pairs(groups, step))
        back.append(piece)
    arrived = jnp.stack(back)
    update = jnp.concatenate(
        [lax.dynamic_index_in_dim(arrived, (position - j) % groups, axis=0, keepdims=False) for j in range(groups)],
        axis=2,
    )
    return age_field + update


def y_split(stacked, forward, inverse, faces, face_total, eigenvalues, age_field):
    groups = lax.axis_size("tm")
    position = lax.axis_index("tm")
    _, steps_local, width_x, depth_z, length_y = stacked.shape
    total_steps = steps_local * groups
    chunk = length_y // groups

    pieces = []
    for step in range(groups):
        target = (position + step) % groups
        piece = lax.dynamic_slice_in_dim(stacked, target * chunk, chunk, axis=4)
        if step > 0:
            piece = lax.ppermute(piece, "tm", ring_pairs(groups, step))
        pieces.append(piece)

    halves = []
    for part in range(2):
        total = None
        for step in range(groups):
            for field in range(2):
                for local in range(steps_local):
                    weight = forward[field][part][:, step, local][:, None, None, None]
                    term = weight * pieces[step][field, local][None]
                    total = term if total is None else total + term
        halves.append(total)
    spectrum = jnp.stack(halves)


    start = position * chunk
    faces_y = tuple(lax.dynamic_slice_in_dim(one_face, start, chunk, axis=2) for one_face in faces)
    total_y = lax.dynamic_slice_in_dim(face_total, start, chunk, axis=2)
    shifted_real = eigenvalues[0][:, None, None, None] + total_y[None]
    eigen_imag = eigenvalues[1][:, None, None, None]
    squared = shifted_real * shifted_real + eigen_imag * eigen_imag
    ratio_real, ratio_imag = lax.optimization_barrier((shifted_real / squared, eigen_imag / squared))

    summed = spectrum
    correction = None
    for sweep_number in range(SWEEPS):
        if sweep_number > 0:
            x_halo = halos(correction, "space", 2)
            y_halo = column_halos(correction, "tm")
            summed = spectrum + neighbour_sum(correction, faces_y, x_halo, y_halo)
        correction = jnp.stack(
            [
                summed[0] * ratio_real + summed[1] * ratio_imag,
                summed[1] * ratio_real - summed[0] * ratio_imag,
            ]
        )

    back = []
    for step in range(groups):
        target = (position + step) % groups
        piece = jnp.einsum("lfk,fkxzy->lxzy", inverse[step], correction, precision=HIGHEST_PRECISION)
        if step > 0:
            piece = lax.ppermute(piece, "tm", ring_pairs(groups, step))
        back.append(piece)
    arrived = jnp.stack(back)
    update = jnp.concatenate(
        [lax.dynamic_index_in_dim(arrived, (position - j) % groups, axis=0, keepdims=False) for j in range(groups)],
        axis=3,
    )
    return age_field + update


def solution(mesh):
    in_specs = (
        P("tm", "space", None, None),
        P("tm", "space", None, None),
        P("space", None, None),
        P(),
        P(),
    )
    out_specs = P("tm", "space", None, None)
    return jax.shard_map(shards, mesh=mesh, in_specs=in_specs, out_specs=out_specs, check_vma=False)
```

```python
import math

import jax
import jax.numpy as jnp
from jax import lax
from jax.sharding import PartitionSpec as P

SWEEPS = 4


HIGHEST_PRECISION = lax.Precision.HIGHEST


def shift_pairs(count, step):
    return [(i, i + step) for i in range(count) if 0 <= i + step < count]


def halos(array, axis, dim):
    count = lax.axis_size(axis)
    length = array.shape[dim]
    last = lax.slice_in_dim(array, length - 1, length, axis=dim)
    first = lax.slice_in_dim(array, 0, 1, axis=dim)
    if count % 2 == 1 or count < 4:
        before = lax.ppermute(last, axis, shift_pairs(count, 1))
        after = lax.ppermute(first, axis, shift_pairs(count, -1))
        return before, after
    index = lax.axis_index(axis)
    even = index % 2 == 0
    even_groups = [[i, i + 1] for i in range(0, count, 2)]
    odd_groups = [[i, (i + 1) % count] for i in range(1, count, 2)]
    got_even = lax.all_gather(jnp.where(even, last, first), axis, axis_index_groups=even_groups)
    got_odd = lax.all_gather(jnp.where(even, first, last), axis, axis_index_groups=odd_groups)
    before = jnp.where(even, got_odd[0], got_even[0])
    after = jnp.where(even, got_even[1], got_odd[1])
    before = jnp.where(index == 0, jnp.zeros_like(before), before)
    after = jnp.where(index == count - 1, jnp.zeros_like(after), after)
    return before, after


def column_halos(array, axis):
    count = lax.axis_size(axis)
    before = lax.ppermute(array[..., -1], axis, shift_pairs(count, 1))
    after = lax.ppermute(array[..., 0], axis, shift_pairs(count, -1))
    return before[..., None], after[..., None]


def ring_pairs(count, step):
    return [(i, (i + step) % count) for i in range(count)]


def shifted_pair(field, before, after, dim):
    length = field.shape[dim]
    low = jnp.concatenate([before, lax.slice_in_dim(field, 0, length - 1, axis=dim)], axis=dim)
    high = jnp.concatenate([lax.slice_in_dim(field, 1, length, axis=dim), after], axis=dim)
    return low, high


def zero_shifted(field, dim):
    edge_shape = list(field.shape)
    edge_shape[dim] = 1
    zero = jnp.zeros(edge_shape, field.dtype)
    return shifted_pair(field, zero, zero, dim)


def neighbour_sum(field, faces, x_halo, y_halo):
    nd = field.ndim
    xm, xp = shifted_pair(field, x_halo[0], x_halo[1], nd - 3)
    zm, zp = zero_shifted(field, nd - 2)
    if y_halo is None:
        ym, yp = zero_shifted(field, nd - 1)
    else:
        ym, yp = shifted_pair(field, y_halo[0], y_halo[1], nd - 1)
    moved = (xm, xp, zm, zp, ym, yp)
    result = faces[0] * moved[0]
    for one_face, one_moved in zip(faces[1:], moved[1:]):
        result = result + one_face * one_moved
    return result


def face_halos(conductivity, age_field):
    count = lax.axis_size("space")
    width = conductivity.shape[0]
    last = jnp.concatenate([conductivity[width - 1 :][None], age_field[:, width - 1 :]], axis=0)
    first = jnp.concatenate([conductivity[:1][None], age_field[:, :1]], axis=0)
    before = lax.ppermute(last, "space", shift_pairs(count, 1))
    after = lax.ppermute(first, "space", shift_pairs(count, -1))
    return (before[0], after[0]), (before[1:], after[1:])


def phase_tables(products, count):
    angles = 2.0 * math.pi / count * (products % count).astype(jnp.float32)
    return jnp.cos(angles), jnp.sin(angles)


def shards(age_field, source_term, conductivity, memory_weights, eigenvalues):
    groups = lax.axis_size("tm")
    position = lax.axis_index("tm")
    steps_local, width_x, depth_z, length_y = age_field.shape
    total_steps = steps_local * groups

    cond_halo, age_halo = face_halos(conductivity, age_field)

    c_low, c_high = shifted_pair(conductivity, cond_halo[0], cond_halo[1], 0)
    z_low, z_high = zero_shifted(conductivity, 1)
    y_low, y_high = zero_shifted(conductivity, 2)
    faces = tuple(0.5 * (conductivity + other) for other in (c_low, c_high, z_low, z_high, y_low, y_high))
    face_total = faces[0]
    for one_face in faces[1:]:
        face_total = face_total + one_face

    spread = neighbour_sum(age_field, faces, age_halo, None) - face_total * age_field
    partial = source_term + spread
    stacked = jnp.stack([partial, age_field])

    frequency = jnp.arange(total_steps, dtype=jnp.int32)
    lag = jnp.arange(total_steps, dtype=jnp.int32)
    cos_w, sin_w = phase_tables(frequency[:, None] * lag[None, :], total_steps)
    weight_real = jnp.sum(memory_weights[None, :] * cos_w, axis=1)[:, None, None]
    weight_imag = -jnp.sum(memory_weights[None, :] * sin_w, axis=1)[:, None, None]
    piece = jnp.arange(groups, dtype=jnp.int32)[None, :, None]
    local = jnp.arange(steps_local, dtype=jnp.int32)[None, None, :]
    step_of = ((position - piece) % groups) * steps_local + local
    cos_f, sin_f = phase_tables(frequency[:, None, None] * step_of, total_steps)
    forward = (
        (cos_f, -sin_f),
        (-(weight_real * cos_f + weight_imag * sin_f), weight_real * sin_f - weight_imag * cos_f),
    )
    step_to = ((position + piece[0, :, :, None]) % groups) * steps_local + local[0, :, :, None]
    cos_i, sin_i = phase_tables(step_to * frequency[None, None, :], total_steps)
    inverse = jnp.stack([cos_i, -sin_i], axis=2) / total_steps

    common = (stacked, forward, inverse, faces, face_total, eigenvalues, age_field)
    if depth_z % groups == 0:
        return z_split(*common)
    return y_split(*common)


def z_split(stacked, forward, inverse, faces, face_total, eigenvalues, age_field):
    groups = lax.axis_size("tm")
    position = lax.axis_index("tm")
    _, steps_local, width_x, depth_z, length_y = stacked.shape
    total_steps = steps_local * groups
    rows = depth_z // groups

    pieces = []
    for step in range(groups):
        target = (position + step) % groups
        piece = lax.dynamic_slice_in_dim(stacked, target * rows, rows, axis=3)
        if step > 0:
            piece = lax.ppermute(piece, "tm", ring_pairs(groups, step))
        pieces.append(piece)

    halves = []
    for part in range(2):
        total = None
        for step in range(groups):
            for field in range(2):
                for local in range(steps_local):
                    weight = forward[field][part][:, step, local][None, None, :, None]
                    term = weight * pieces[step][field, local][:, :, None, :]
                    total = term if total is None else total + term
        halves.append(total)
    spectrum = jnp.stack(halves)

    start = position * rows
    faces_z = tuple(lax.dynamic_slice_in_dim(one_face, start, rows, axis=1)[:, :, None, :] for one_face in faces)
    total_z = lax.dynamic_slice_in_dim(face_total, start, rows, axis=1)[:, :, None, :]
    shifted_real = eigenvalues[0][None, None, :, None] + total_z
    eigen_imag = eigenvalues[1][None, None, :, None]
    squared = shifted_real * shifted_real + eigen_imag * eigen_imag
    ratio_real, ratio_imag = lax.optimization_barrier((shifted_real / squared, eigen_imag / squared))

    summed = spectrum
    correction = None
    for sweep_number in range(SWEEPS):
        if sweep_number > 0:
            x_low, x_high = halos(correction, "space", 1)
            z_low, z_high = halos(correction, "tm", 2)
            xm, xp = shifted_pair(correction, x_low, x_high, 1)
            zm, zp = shifted_pair(correction, z_low, z_high, 2)
            ym, yp = zero_shifted(correction, 4)
            moved = (xm, xp, zm, zp, ym, yp)
            total = faces_z[0] * moved[0]
            for one_face, one_moved in zip(faces_z[1:], moved[1:]):
                total = total + one_face * one_moved
            summed = spectrum + total
        correction = jnp.stack(
            [
                summed[0] * ratio_real + summed[1] * ratio_imag,
                summed[1] * ratio_real - summed[0] * ratio_imag,
            ]
        )

    back = []
    for step in range(groups):
        target = (position + step) % groups
        piece = jnp.einsum("lfk,fxzky->lxzy", inverse[step], correction, precision=HIGHEST_PRECISION)
        if step > 0:
            piece = lax.ppermute(piece, "tm", ring_pairs(groups, step))
        back.append(piece)
    arrived = jnp.stack(back)
    update = jnp.concatenate(
        [lax.dynamic_index_in_dim(arrived, (position - j) % groups, axis=0, keepdims=False) for j in range(groups)],
        axis=2,
    )
    return age_field + update


def y_split(stacked, forward, inverse, faces, face_total, eigenvalues, age_field):
    groups = lax.axis_size("tm")
    position = lax.axis_index("tm")
    _, steps_local, width_x, depth_z, length_y = stacked.shape
    total_steps = steps_local * groups
    chunk = length_y // groups

    pieces = []
    for step in range(groups):
        target = (position + step) % groups
        piece = lax.dynamic_slice_in_dim(stacked, target * chunk, chunk, axis=4)
        if step > 0:
            piece = lax.ppermute(piece, "tm", ring_pairs(groups, step))
        pieces.append(piece)

    halves = []
    for part in range(2):
        total = None
        for step in range(groups):
            for field in range(2):
                for local in range(steps_local):
                    weight = forward[field][part][:, step, local][:, None, None, None]
                    term = weight * pieces[step][field, local][None]
                    total = term if total is None else total + term
        halves.append(total)
    spectrum = jnp.stack(halves)


    start = position * chunk
    faces_y = tuple(lax.dynamic_slice_in_dim(one_face, start, chunk, axis=2) for one_face in faces)
    total_y = lax.dynamic_slice_in_dim(face_total, start, chunk, axis=2)
    shifted_real = eigenvalues[0][:, None, None, None] + total_y[None]
    eigen_imag = eigenvalues[1][:, None, None, None]
    squared = shifted_real * shifted_real + eigen_imag * eigen_imag
    ratio_real, ratio_imag = lax.optimization_barrier((shifted_real / squared, eigen_imag / squared))

    summed = spectrum
    correction = None
    for sweep_number in range(SWEEPS):
        if sweep_number > 0:
            x_halo = halos(correction, "space", 2)
            y_halo = column_halos(correction, "tm")
            summed = spectrum + neighbour_sum(correction, faces_y, x_halo, y_halo)
        correction = jnp.stack(
            [
                summed[0] * ratio_real + summed[1] * ratio_imag,
                summed[1] * ratio_real - summed[0] * ratio_imag,
            ]
        )

    back = []
    for step in range(groups):
        target = (position + step) % groups
        piece = jnp.einsum("lfk,fkxzy->lxzy", inverse[step], correction, precision=HIGHEST_PRECISION)
        if step > 0:
            piece = lax.ppermute(piece, "tm", ring_pairs(groups, step))
        back.append(piece)
    arrived = jnp.stack(back)
    update = jnp.concatenate(
        [lax.dynamic_index_in_dim(arrived, (position - j) % groups, axis=0, keepdims=False) for j in range(groups)],
        axis=3,
    )
    return age_field + update


def solution(mesh):
    in_specs = (
        P("tm", "space", None, None),
        P("tm", "space", None, None),
        P("space", None, None),
        P(),
        P(),
    )
    out_specs = P("tm", "space", None, None)
    return jax.shard_map(shards, mesh=mesh, in_specs=in_specs, out_specs=out_specs, check_vma=False)
```

```python
import math

import jax
import jax.numpy as jnp
from jax import lax
from jax.sharding import PartitionSpec as P

SWEEPS = 4


HIGHEST_PRECISION = lax.Precision.HIGHEST


def shift_pairs(count, step):
    return [(i, i + step) for i in range(count) if 0 <= i + step < count]


def halos(array, axis, dim):
    count = lax.axis_size(axis)
    length = array.shape[dim]
    last = lax.slice_in_dim(array, length - 1, length, axis=dim)
    first = lax.slice_in_dim(array, 0, 1, axis=dim)
    index = lax.axis_index(axis)
    before = lax.ppermute(last, axis, ring_pairs(count, 1))
    after = lax.ppermute(first, axis, ring_pairs(count, -1))
    before = jnp.where(index == 0, jnp.zeros_like(before), before)
    after = jnp.where(index == count - 1, jnp.zeros_like(after), after)
    return before, after


def column_halos(array, axis):
    count = lax.axis_size(axis)
    before = lax.ppermute(array[..., -1], axis, shift_pairs(count, 1))
    after = lax.ppermute(array[..., 0], axis, shift_pairs(count, -1))
    return before[..., None], after[..., None]


def ring_pairs(count, step):
    return [(i, (i + step) % count) for i in range(count)]


def shifted_pair(field, before, after, dim):
    length = field.shape[dim]
    low = jnp.concatenate([before, lax.slice_in_dim(field, 0, length - 1, axis=dim)], axis=dim)
    high = jnp.concatenate([lax.slice_in_dim(field, 1, length, axis=dim), after], axis=dim)
    return low, high


def zero_shifted(field, dim):
    edge_shape = list(field.shape)
    edge_shape[dim] = 1
    zero = jnp.zeros(edge_shape, field.dtype)
    return shifted_pair(field, zero, zero, dim)


def neighbour_sum(field, faces, x_halo, y_halo):
    nd = field.ndim
    xm, xp = shifted_pair(field, x_halo[0], x_halo[1], nd - 3)
    zm, zp = zero_shifted(field, nd - 2)
    if y_halo is None:
        ym, yp = zero_shifted(field, nd - 1)
    else:
        ym, yp = shifted_pair(field, y_halo[0], y_halo[1], nd - 1)
    moved = (xm, xp, zm, zp, ym, yp)
    result = faces[0] * moved[0]
    for one_face, one_moved in zip(faces[1:], moved[1:]):
        result = result + one_face * one_moved
    return result


def face_halos(conductivity, age_field):
    count = lax.axis_size("space")
    width = conductivity.shape[0]
    last = jnp.concatenate([conductivity[width - 1 :][None], age_field[:, width - 1 :]], axis=0)
    first = jnp.concatenate([conductivity[:1][None], age_field[:, :1]], axis=0)
    before = lax.ppermute(last, "space", shift_pairs(count, 1))
    after = lax.ppermute(first, "space", shift_pairs(count, -1))
    return (before[0], after[0]), (before[1:], after[1:])


def phase_tables(products, count):
    angles = 2.0 * math.pi / count * (products % count).astype(jnp.float32)
    return jnp.cos(angles), jnp.sin(angles)


def shards(age_field, source_term, conductivity, memory_weights, eigenvalues):
    groups = lax.axis_size("tm")
    position = lax.axis_index("tm")
    steps_local, width_x, depth_z, length_y = age_field.shape
    total_steps = steps_local * groups

    cond_halo, age_halo = face_halos(conductivity, age_field)

    c_low, c_high = shifted_pair(conductivity, cond_halo[0], cond_halo[1], 0)
    z_low, z_high = zero_shifted(conductivity, 1)
    y_low, y_high = zero_shifted(conductivity, 2)
    faces = tuple(0.5 * (conductivity + other) for other in (c_low, c_high, z_low, z_high, y_low, y_high))
    face_total = faces[0]
    for one_face in faces[1:]:
        face_total = face_total + one_face

    spread = neighbour_sum(age_field, faces, age_halo, None) - face_total * age_field
    partial = source_term + spread
    stacked = jnp.stack([partial, age_field])

    frequency = jnp.arange(total_steps, dtype=jnp.int32)
    lag = jnp.arange(total_steps, dtype=jnp.int32)
    cos_w, sin_w = phase_tables(frequency[:, None] * lag[None, :], total_steps)
    weight_real = jnp.sum(memory_weights[None, :] * cos_w, axis=1)[:, None, None]
    weight_imag = -jnp.sum(memory_weights[None, :] * sin_w, axis=1)[:, None, None]
    piece = jnp.arange(groups, dtype=jnp.int32)[None, :, None]
    local = jnp.arange(steps_local, dtype=jnp.int32)[None, None, :]
    step_of = ((position - piece) % groups) * steps_local + local
    cos_f, sin_f = phase_tables(frequency[:, None, None] * step_of, total_steps)
    forward = (
        (cos_f, -sin_f),
        (-(weight_real * cos_f + weight_imag * sin_f), weight_real * sin_f - weight_imag * cos_f),
    )
    step_to = ((position + piece[0, :, :, None]) % groups) * steps_local + local[0, :, :, None]
    cos_i, sin_i = phase_tables(step_to * frequency[None, None, :], total_steps)
    inverse = jnp.stack([cos_i, -sin_i], axis=2) / total_steps

    common = (stacked, forward, inverse, faces, face_total, eigenvalues, age_field)
    if depth_z % groups == 0:
        return z_split(*common)
    return y_split(*common)


def z_split(stacked, forward, inverse, faces, face_total, eigenvalues, age_field):
    groups = lax.axis_size("tm")
    position = lax.axis_index("tm")
    _, steps_local, width_x, depth_z, length_y = stacked.shape
    total_steps = steps_local * groups
    rows = depth_z // groups

    pieces = []
    for step in range(groups):
        target = (position + step) % groups
        piece = lax.dynamic_slice_in_dim(stacked, target * rows, rows, axis=3)
        if step > 0:
            piece = lax.ppermute(piece, "tm", ring_pairs(groups, step))
        pieces.append(piece)

    halves = []
    for part in range(2):
        total = None
        for step in range(groups):
            for field in range(2):
                for local in range(steps_local):
                    weight = forward[field][part][:, step, local][None, None, :, None]
                    term = weight * pieces[step][field, local][:, :, None, :]
                    total = term if total is None else total + term
        halves.append(total)
    spectrum = jnp.stack(halves)

    start = position * rows
    faces_z = tuple(lax.dynamic_slice_in_dim(one_face, start, rows, axis=1)[:, :, None, :] for one_face in faces)
    total_z = lax.dynamic_slice_in_dim(face_total, start, rows, axis=1)[:, :, None, :]
    shifted_real = eigenvalues[0][None, None, :, None] + total_z
    eigen_imag = eigenvalues[1][None, None, :, None]
    squared = shifted_real * shifted_real + eigen_imag * eigen_imag
    ratio_real, ratio_imag = lax.optimization_barrier((shifted_real / squared, eigen_imag / squared))

    summed = spectrum
    correction = None
    for sweep_number in range(SWEEPS):
        if sweep_number > 0:
            x_low, x_high = halos(correction, "space", 1)
            z_low, z_high = halos(correction, "tm", 2)
            xm, xp = shifted_pair(correction, x_low, x_high, 1)
            zm, zp = shifted_pair(correction, z_low, z_high, 2)
            ym, yp = zero_shifted(correction, 4)
            moved = (xm, xp, zm, zp, ym, yp)
            total = faces_z[0] * moved[0]
            for one_face, one_moved in zip(faces_z[1:], moved[1:]):
                total = total + one_face * one_moved
            summed = spectrum + total
        correction = jnp.stack(
            [
                summed[0] * ratio_real + summed[1] * ratio_imag,
                summed[1] * ratio_real - summed[0] * ratio_imag,
            ]
        )

    back = []
    for step in range(groups):
        target = (position + step) % groups
        piece = jnp.einsum("lfk,fxzky->lxzy", inverse[step], correction, precision=HIGHEST_PRECISION)
        if step > 0:
            piece = lax.ppermute(piece, "tm", ring_pairs(groups, step))
        back.append(piece)
    arrived = jnp.stack(back)
    update = jnp.concatenate(
        [lax.dynamic_index_in_dim(arrived, (position - j) % groups, axis=0, keepdims=False) for j in range(groups)],
        axis=2,
    )
    return age_field + update


def y_split(stacked, forward, inverse, faces, face_total, eigenvalues, age_field):
    groups = lax.axis_size("tm")
    position = lax.axis_index("tm")
    _, steps_local, width_x, depth_z, length_y = stacked.shape
    total_steps = steps_local * groups
    chunk = length_y // groups

    pieces = []
    for step in range(groups):
        target = (position + step) % groups
        piece = lax.dynamic_slice_in_dim(stacked, target * chunk, chunk, axis=4)
        if step > 0:
            piece = lax.ppermute(piece, "tm", ring_pairs(groups, step))
        pieces.append(piece)

    halves = []
    for part in range(2):
        total = None
        for step in range(groups):
            for field in range(2):
                for local in range(steps_local):
                    weight = forward[field][part][:, step, local][:, None, None, None]
                    term = weight * pieces[step][field, local][None]
                    total = term if total is None else total + term
        halves.append(total)
    spectrum = jnp.stack(halves)


    start = position * chunk
    faces_y = tuple(lax.dynamic_slice_in_dim(one_face, start, chunk, axis=2) for one_face in faces)
    total_y = lax.dynamic_slice_in_dim(face_total, start, chunk, axis=2)
    shifted_real = eigenvalues[0][:, None, None, None] + total_y[None]
    eigen_imag = eigenvalues[1][:, None, None, None]
    squared = shifted_real * shifted_real + eigen_imag * eigen_imag
    ratio_real, ratio_imag = lax.optimization_barrier((shifted_real / squared, eigen_imag / squared))

    summed = spectrum
    correction = None
    for sweep_number in range(SWEEPS):
        if sweep_number > 0:
            x_halo = halos(correction, "space", 2)
            y_halo = column_halos(correction, "tm")
            summed = spectrum + neighbour_sum(correction, faces_y, x_halo, y_halo)
        correction = jnp.stack(
            [
                summed[0] * ratio_real + summed[1] * ratio_imag,
                summed[1] * ratio_real - summed[0] * ratio_imag,
            ]
        )

    back = []
    for step in range(groups):
        target = (position + step) % groups
        piece = jnp.einsum("lfk,fkxzy->lxzy", inverse[step], correction, precision=HIGHEST_PRECISION)
        if step > 0:
            piece = lax.ppermute(piece, "tm", ring_pairs(groups, step))
        back.append(piece)
    arrived = jnp.stack(back)
    update = jnp.concatenate(
        [lax.dynamic_index_in_dim(arrived, (position - j) % groups, axis=0, keepdims=False) for j in range(groups)],
        axis=3,
    )
    return age_field + update


def solution(mesh):
    in_specs = (
        P("tm", "space", None, None),
        P("tm", "space", None, None),
        P("space", None, None),
        P(),
        P(),
    )
    out_specs = P("tm", "space", None, None)
    return jax.shard_map(shards, mesh=mesh, in_specs=in_specs, out_specs=out_specs, check_vma=False)
```

```python
import math

import jax
import jax.numpy as jnp
from jax import lax
from jax.sharding import PartitionSpec as P

SWEEPS = 4


HIGHEST_PRECISION = lax.Precision.HIGHEST


def shift_pairs(count, step):
    return [(i, i + step) for i in range(count) if 0 <= i + step < count]


def halos(array, axis, dim):
    count = lax.axis_size(axis)
    length = array.shape[dim]
    last = lax.slice_in_dim(array, length - 1, length, axis=dim)
    first = lax.slice_in_dim(array, 0, 1, axis=dim)
    index = lax.axis_index(axis)
    before = lax.ppermute(last, axis, ring_pairs(count, 1))
    after = lax.ppermute(first, axis, ring_pairs(count, -1))
    before = jnp.where(index == 0, jnp.zeros_like(before), before)
    after = jnp.where(index == count - 1, jnp.zeros_like(after), after)
    return before, after


def column_halos(array, axis):
    count = lax.axis_size(axis)
    before = lax.ppermute(array[..., -1], axis, shift_pairs(count, 1))
    after = lax.ppermute(array[..., 0], axis, shift_pairs(count, -1))
    return before[..., None], after[..., None]


def ring_pairs(count, step):
    return [(i, (i + step) % count) for i in range(count)]


def shifted_pair(field, before, after, dim):
    length = field.shape[dim]
    low = jnp.concatenate([before, lax.slice_in_dim(field, 0, length - 1, axis=dim)], axis=dim)
    high = jnp.concatenate([lax.slice_in_dim(field, 1, length, axis=dim), after], axis=dim)
    return low, high


def zero_shifted(field, dim):
    edge_shape = list(field.shape)
    edge_shape[dim] = 1
    zero = jnp.zeros(edge_shape, field.dtype)
    return shifted_pair(field, zero, zero, dim)


def neighbour_sum(field, faces, x_halo, y_halo):
    nd = field.ndim
    xm, xp = shifted_pair(field, x_halo[0], x_halo[1], nd - 3)
    zm, zp = zero_shifted(field, nd - 2)
    if y_halo is None:
        ym, yp = zero_shifted(field, nd - 1)
    else:
        ym, yp = shifted_pair(field, y_halo[0], y_halo[1], nd - 1)
    moved = (xm, xp, zm, zp, ym, yp)
    result = faces[0] * moved[0]
    for one_face, one_moved in zip(faces[1:], moved[1:]):
        result = result + one_face * one_moved
    return result


def face_halos(conductivity, age_field, depth):
    count = lax.axis_size("space")
    width = conductivity.shape[0]
    last = jnp.concatenate([conductivity[width - depth :], age_field[:, width - 1]], axis=0)
    first = jnp.concatenate([conductivity[:depth], age_field[:, 0]], axis=0)
    before = lax.ppermute(last, "space", shift_pairs(count, 1))
    after = lax.ppermute(first, "space", shift_pairs(count, -1))
    return (before[:depth], after[:depth]), (before[depth:][:, None], after[depth:][:, None])


def face_set(conductivity, cond_halo, rim):
    depth = rim + 1
    count = lax.axis_size("space")
    width, rows, _ = conductivity.shape
    wide = jnp.concatenate([cond_halo[0], conductivity, cond_halo[1]], axis=0)
    wide = jnp.pad(wide, ((0, 0), (depth, depth), (0, 0)))
    centre = wide[1:-1, 1:-1]
    y_low, y_high = zero_shifted(centre, 2)
    others = (wide[:-2, 1:-1], wide[2:, 1:-1], wide[1:-1, :-2], wide[1:-1, 2:], y_low, y_high)
    faces = tuple(0.5 * (centre + other) for other in others)
    if rim > 0:
        at_x = lax.axis_index("space") * width - rim + jnp.arange(width + 2 * rim, dtype=jnp.int32)
        at_z = jnp.arange(rows + 2 * rim, dtype=jnp.int32) - rim
        inside = ((at_x >= 0) & (at_x < width * count))[:, None, None] & ((at_z >= 0) & (at_z < rows))[None, :, None]
        faces = tuple(jnp.where(inside, one_face, 0.0) for one_face in faces)
    face_total = faces[0]
    for one_face in faces[1:]:
        face_total = face_total + one_face
    return faces, face_total


def phase_tables(products, count):
    angles = 2.0 * math.pi / count * (products % count).astype(jnp.float32)
    return jnp.cos(angles), jnp.sin(angles)


def shards(age_field, source_term, conductivity, memory_weights, eigenvalues):
    groups = lax.axis_size("tm")
    position = lax.axis_index("tm")
    steps_local, width_x, depth_z, length_y = age_field.shape
    total_steps = steps_local * groups

    z_path = depth_z % groups == 0 and width_x > SWEEPS - 1
    rim = SWEEPS - 1 if z_path else 0
    cond_halo, age_halo = face_halos(conductivity, age_field, rim + 1)
    faces_wide, total_wide = face_set(conductivity, cond_halo, rim)
    faces = tuple(one_face[rim : rim + width_x, rim : rim + depth_z] for one_face in faces_wide)
    face_total = total_wide[rim : rim + width_x, rim : rim + depth_z]

    spread = neighbour_sum(age_field, faces, age_halo, None) - face_total * age_field
    partial = source_term + spread
    stacked = jnp.stack([partial, age_field])

    frequency = jnp.arange(total_steps, dtype=jnp.int32)
    lag = jnp.arange(total_steps, dtype=jnp.int32)
    cos_w, sin_w = phase_tables(frequency[:, None] * lag[None, :], total_steps)
    weight_real = jnp.sum(memory_weights[None, :] * cos_w, axis=1)[:, None, None]
    weight_imag = -jnp.sum(memory_weights[None, :] * sin_w, axis=1)[:, None, None]
    piece = jnp.arange(groups, dtype=jnp.int32)[None, :, None]
    local = jnp.arange(steps_local, dtype=jnp.int32)[None, None, :]
    step_of = ((position - piece) % groups) * steps_local + local
    cos_f, sin_f = phase_tables(frequency[:, None, None] * step_of, total_steps)
    forward = (
        (cos_f, -sin_f),
        (-(weight_real * cos_f + weight_imag * sin_f), weight_real * sin_f - weight_imag * cos_f),
    )
    step_to = ((position + piece[0, :, :, None]) % groups) * steps_local + local[0, :, :, None]
    cos_i, sin_i = phase_tables(step_to * frequency[None, None, :], total_steps)
    inverse = jnp.stack([cos_i, -sin_i], axis=2) / total_steps

    if z_path:
        return z_split(stacked, forward, inverse, faces_wide, total_wide, eigenvalues, age_field, rim)
    return y_split(stacked, forward, inverse, faces, face_total, eigenvalues, age_field)


def z_split(stacked, forward, inverse, faces, face_total, eigenvalues, age_field, rim):
    groups = lax.axis_size("tm")
    position = lax.axis_index("tm")
    _, steps_local, width_x, depth_z, length_y = stacked.shape
    total_steps = steps_local * groups
    rows = depth_z // groups
    tall = rows + 2 * rim

    padded = jnp.pad(stacked, ((0, 0), (0, 0), (0, 0), (rim, rim), (0, 0)))
    pieces = []
    for step in range(groups):
        target = (position + step) % groups
        piece = lax.dynamic_slice_in_dim(padded, target * rows, tall, axis=3)
        if step > 0:
            piece = lax.ppermute(piece, "tm", ring_pairs(groups, step))
        pieces.append(piece)

    halves = []
    for part in range(2):
        total = None
        for step in range(groups):
            for field in range(2):
                for local in range(steps_local):
                    weight = forward[field][part][:, step, local][None, None, :, None]
                    term = weight * pieces[step][field, local][:, :, None, :]
                    total = term if total is None else total + term
        halves.append(total)
    spectrum = jnp.stack(halves)

    count = lax.axis_size("space")
    before = lax.ppermute(spectrum[:, width_x - rim :], "space", shift_pairs(count, 1))
    after = lax.ppermute(spectrum[:, :rim], "space", shift_pairs(count, -1))
    spectrum = jnp.concatenate([before, spectrum, after], axis=1)

    start = position * rows
    faces_z = tuple(lax.dynamic_slice_in_dim(one_face, start, tall, axis=1)[:, :, None, :] for one_face in faces)
    total_z = lax.dynamic_slice_in_dim(face_total, start, tall, axis=1)[:, :, None, :]
    shifted_real = eigenvalues[0][None, None, :, None] + total_z
    eigen_imag = eigenvalues[1][None, None, :, None]
    squared = shifted_real * shifted_real + eigen_imag * eigen_imag
    ratio_real = shifted_real / squared
    ratio_imag = eigen_imag / squared

    summed = spectrum
    correction = None
    for sweep_number in range(SWEEPS):
        edge = sweep_number
        cut = (slice(None), slice(edge, spectrum.shape[1] - edge), slice(edge, spectrum.shape[2] - edge))
        if sweep_number > 0:
            inner = correction[:, 1:-1, 1:-1]
            ym, yp = zero_shifted(inner, 4)
            moved = (
                correction[:, :-2, 1:-1],
                correction[:, 2:, 1:-1],
                correction[:, 1:-1, :-2],
                correction[:, 1:-1, 2:],
                ym,
                yp,
            )
            region = (slice(edge, faces_z[0].shape[0] - edge), slice(edge, faces_z[0].shape[1] - edge))
            total = faces_z[0][region] * moved[0]
            for one_face, one_moved in zip(faces_z[1:], moved[1:]):
                total = total + one_face[region] * one_moved
            summed = spectrum[cut] + total
            rr = ratio_real[region]
            ri = ratio_imag[region]
        else:
            rr = ratio_real
            ri = ratio_imag
        correction = jnp.stack([summed[0] * rr + summed[1] * ri, summed[1] * rr - summed[0] * ri])

    back = []
    for step in range(groups):
        piece = jnp.einsum("lfk,fxzky->lxzy", inverse[step], correction, precision=HIGHEST_PRECISION)
        if step > 0:
            piece = lax.ppermute(piece, "tm", ring_pairs(groups, step))
        back.append(piece)
    arrived = jnp.stack(back)
    update = jnp.concatenate(
        [lax.dynamic_index_in_dim(arrived, (position - j) % groups, axis=0, keepdims=False) for j in range(groups)],
        axis=2,
    )
    return age_field + update


def y_split(stacked, forward, inverse, faces, face_total, eigenvalues, age_field):
    groups = lax.axis_size("tm")
    position = lax.axis_index("tm")
    _, steps_local, width_x, depth_z, length_y = stacked.shape
    total_steps = steps_local * groups
    chunk = length_y // groups

    pieces = []
    for step in range(groups):
        target = (position + step) % groups
        piece = lax.dynamic_slice_in_dim(stacked, target * chunk, chunk, axis=4)
        if step > 0:
            piece = lax.ppermute(piece, "tm", ring_pairs(groups, step))
        pieces.append(piece)

    halves = []
    for part in range(2):
        total = None
        for step in range(groups):
            for field in range(2):
                for local in range(steps_local):
                    weight = forward[field][part][:, step, local][:, None, None, None]
                    term = weight * pieces[step][field, local][None]
                    total = term if total is None else total + term
        halves.append(total)
    spectrum = jnp.stack(halves)


    start = position * chunk
    faces_y = tuple(lax.dynamic_slice_in_dim(one_face, start, chunk, axis=2) for one_face in faces)
    total_y = lax.dynamic_slice_in_dim(face_total, start, chunk, axis=2)
    shifted_real = eigenvalues[0][:, None, None, None] + total_y[None]
    eigen_imag = eigenvalues[1][:, None, None, None]
    squared = shifted_real * shifted_real + eigen_imag * eigen_imag
    ratio_real, ratio_imag = lax.optimization_barrier((shifted_real / squared, eigen_imag / squared))

    summed = spectrum
    correction = None
    for sweep_number in range(SWEEPS):
        if sweep_number > 0:
            x_halo = halos(correction, "space", 2)
            y_halo = column_halos(correction, "tm")
            summed = spectrum + neighbour_sum(correction, faces_y, x_halo, y_halo)
        correction = jnp.stack(
            [
                summed[0] * ratio_real + summed[1] * ratio_imag,
                summed[1] * ratio_real - summed[0] * ratio_imag,
            ]
        )

    back = []
    for step in range(groups):
        target = (position + step) % groups
        piece = jnp.einsum("lfk,fkxzy->lxzy", inverse[step], correction, precision=HIGHEST_PRECISION)
        if step > 0:
            piece = lax.ppermute(piece, "tm", ring_pairs(groups, step))
        back.append(piece)
    arrived = jnp.stack(back)
    update = jnp.concatenate(
        [lax.dynamic_index_in_dim(arrived, (position - j) % groups, axis=0, keepdims=False) for j in range(groups)],
        axis=3,
    )
    return age_field + update


def solution(mesh):
    in_specs = (
        P("tm", "space", None, None),
        P("tm", "space", None, None),
        P("space", None, None),
        P(),
        P(),
    )
    out_specs = P("tm", "space", None, None)
    return jax.shard_map(shards, mesh=mesh, in_specs=in_specs, out_specs=out_specs, check_vma=False)
```

```python
import math

import jax
import jax.numpy as jnp
from jax import lax
from jax.sharding import PartitionSpec as P

SWEEPS = 4


HIGHEST_PRECISION = lax.Precision.HIGHEST


def shift_pairs(count, step):
    return [(i, i + step) for i in range(count) if 0 <= i + step < count]


def halos(array, axis, dim):
    count = lax.axis_size(axis)
    length = array.shape[dim]
    last = lax.slice_in_dim(array, length - 1, length, axis=dim)
    first = lax.slice_in_dim(array, 0, 1, axis=dim)
    if axis == "space":
        before = lax.ppermute(last, axis, shift_pairs(count, 1))
        after = lax.ppermute(first, axis, shift_pairs(count, -1))
        return before, after
    index = lax.axis_index(axis)
    before = lax.ppermute(last, axis, ring_pairs(count, 1))
    after = lax.ppermute(first, axis, ring_pairs(count, -1))
    before = jnp.where(index == 0, jnp.zeros_like(before), before)
    after = jnp.where(index == count - 1, jnp.zeros_like(after), after)
    return before, after


def column_halos(array, axis):
    count = lax.axis_size(axis)
    before = lax.ppermute(array[..., -1], axis, shift_pairs(count, 1))
    after = lax.ppermute(array[..., 0], axis, shift_pairs(count, -1))
    return before[..., None], after[..., None]


def ring_pairs(count, step):
    return [(i, (i + step) % count) for i in range(count)]


def shifted_pair(field, before, after, dim):
    length = field.shape[dim]
    low = jnp.concatenate([before, lax.slice_in_dim(field, 0, length - 1, axis=dim)], axis=dim)
    high = jnp.concatenate([lax.slice_in_dim(field, 1, length, axis=dim), after], axis=dim)
    return low, high


def zero_shifted(field, dim):
    edge_shape = list(field.shape)
    edge_shape[dim] = 1
    zero = jnp.zeros(edge_shape, field.dtype)
    return shifted_pair(field, zero, zero, dim)


def neighbour_sum(field, faces, x_halo, y_halo):
    nd = field.ndim
    xm, xp = shifted_pair(field, x_halo[0], x_halo[1], nd - 3)
    zm, zp = zero_shifted(field, nd - 2)
    if y_halo is None:
        ym, yp = zero_shifted(field, nd - 1)
    else:
        ym, yp = shifted_pair(field, y_halo[0], y_halo[1], nd - 1)
    moved = (xm, xp, zm, zp, ym, yp)
    result = faces[0] * moved[0]
    for one_face, one_moved in zip(faces[1:], moved[1:]):
        result = result + one_face * one_moved
    return result


def face_halos(conductivity, age_field):
    count = lax.axis_size("space")
    width = conductivity.shape[0]
    last = jnp.concatenate([conductivity[width - 1 :][None], age_field[:, width - 1 :]], axis=0)
    first = jnp.concatenate([conductivity[:1][None], age_field[:, :1]], axis=0)
    before = lax.ppermute(last, "space", shift_pairs(count, 1))
    after = lax.ppermute(first, "space", shift_pairs(count, -1))
    return (before[0], after[0]), (before[1:], after[1:])


def phase_tables(products, count):
    angles = 2.0 * math.pi / count * (products % count).astype(jnp.float32)
    return jnp.cos(angles), jnp.sin(angles)


def shards(age_field, source_term, conductivity, memory_weights, eigenvalues):
    groups = lax.axis_size("tm")
    position = lax.axis_index("tm")
    steps_local, width_x, depth_z, length_y = age_field.shape
    total_steps = steps_local * groups

    cond_halo, age_halo = face_halos(conductivity, age_field)

    c_low, c_high = shifted_pair(conductivity, cond_halo[0], cond_halo[1], 0)
    z_low, z_high = zero_shifted(conductivity, 1)
    y_low, y_high = zero_shifted(conductivity, 2)
    faces = tuple(0.5 * (conductivity + other) for other in (c_low, c_high, z_low, z_high, y_low, y_high))
    face_total = faces[0]
    for one_face in faces[1:]:
        face_total = face_total + one_face

    spread = neighbour_sum(age_field, faces, age_halo, None) - face_total * age_field
    partial = source_term + spread
    stacked = jnp.stack([partial, age_field])

    frequency = jnp.arange(total_steps, dtype=jnp.int32)
    lag = jnp.arange(total_steps, dtype=jnp.int32)
    cos_w, sin_w = phase_tables(frequency[:, None] * lag[None, :], total_steps)
    weight_real = jnp.sum(memory_weights[None, :] * cos_w, axis=1)[:, None, None]
    weight_imag = -jnp.sum(memory_weights[None, :] * sin_w, axis=1)[:, None, None]
    piece = jnp.arange(groups, dtype=jnp.int32)[None, :, None]
    local = jnp.arange(steps_local, dtype=jnp.int32)[None, None, :]
    step_of = ((position - piece) % groups) * steps_local + local
    cos_f, sin_f = phase_tables(frequency[:, None, None] * step_of, total_steps)
    forward = (
        (cos_f, -sin_f),
        (-(weight_real * cos_f + weight_imag * sin_f), weight_real * sin_f - weight_imag * cos_f),
    )
    step_to = ((position + piece[0, :, :, None]) % groups) * steps_local + local[0, :, :, None]
    cos_i, sin_i = phase_tables(step_to * frequency[None, None, :], total_steps)
    inverse = jnp.stack([cos_i, -sin_i], axis=2) / total_steps

    common = (stacked, forward, inverse, faces, face_total, eigenvalues, age_field)
    if depth_z % groups == 0:
        return z_split(*common)
    return y_split(*common)


def z_split(stacked, forward, inverse, faces, face_total, eigenvalues, age_field):
    groups = lax.axis_size("tm")
    position = lax.axis_index("tm")
    _, steps_local, width_x, depth_z, length_y = stacked.shape
    total_steps = steps_local * groups
    rows = depth_z // groups

    pieces = []
    for step in range(groups):
        target = (position + step) % groups
        piece = lax.dynamic_slice_in_dim(stacked, target * rows, rows, axis=3)
        if step > 0:
            piece = lax.ppermute(piece, "tm", ring_pairs(groups, step))
        pieces.append(piece)

    halves = []
    for part in range(2):
        total = None
        for step in range(groups):
            for field in range(2):
                for local in range(steps_local):
                    weight = forward[field][part][:, step, local][None, None, :, None]
                    term = weight * pieces[step][field, local][:, :, None, :]
                    total = term if total is None else total + term
        halves.append(total)
    spectrum = jnp.stack(halves)

    start = position * rows
    faces_z = tuple(lax.dynamic_slice_in_dim(one_face, start, rows, axis=1)[:, :, None, :] for one_face in faces)
    total_z = lax.dynamic_slice_in_dim(face_total, start, rows, axis=1)[:, :, None, :]
    shifted_real = eigenvalues[0][None, None, :, None] + total_z
    eigen_imag = eigenvalues[1][None, None, :, None]
    squared = shifted_real * shifted_real + eigen_imag * eigen_imag
    ratio_real, ratio_imag = lax.optimization_barrier((shifted_real / squared, eigen_imag / squared))

    summed = spectrum
    correction = None
    for sweep_number in range(SWEEPS):
        if sweep_number > 0:
            x_low, x_high = halos(correction, "space", 1)
            z_low, z_high = halos(correction, "tm", 2)
            xm, xp = shifted_pair(correction, x_low, x_high, 1)
            zm, zp = shifted_pair(correction, z_low, z_high, 2)
            ym, yp = zero_shifted(correction, 4)
            moved = (xm, xp, zm, zp, ym, yp)
            total = faces_z[0] * moved[0]
            for one_face, one_moved in zip(faces_z[1:], moved[1:]):
                total = total + one_face * one_moved
            summed = spectrum + total
        correction = jnp.stack(
            [
                summed[0] * ratio_real + summed[1] * ratio_imag,
                summed[1] * ratio_real - summed[0] * ratio_imag,
            ]
        )

    back = []
    for step in range(groups):
        target = (position + step) % groups
        piece = jnp.einsum("lfk,fxzky->lxzy", inverse[step], correction, precision=HIGHEST_PRECISION)
        if step > 0:
            piece = lax.ppermute(piece, "tm", ring_pairs(groups, step))
        back.append(piece)
    arrived = jnp.stack(back)
    update = jnp.concatenate(
        [lax.dynamic_index_in_dim(arrived, (position - j) % groups, axis=0, keepdims=False) for j in range(groups)],
        axis=2,
    )
    return age_field + update


def y_split(stacked, forward, inverse, faces, face_total, eigenvalues, age_field):
    groups = lax.axis_size("tm")
    position = lax.axis_index("tm")
    _, steps_local, width_x, depth_z, length_y = stacked.shape
    total_steps = steps_local * groups
    chunk = length_y // groups

    pieces = []
    for step in range(groups):
        target = (position + step) % groups
        piece = lax.dynamic_slice_in_dim(stacked, target * chunk, chunk, axis=4)
        if step > 0:
            piece = lax.ppermute(piece, "tm", ring_pairs(groups, step))
        pieces.append(piece)

    halves = []
    for part in range(2):
        total = None
        for step in range(groups):
            for field in range(2):
                for local in range(steps_local):
                    weight = forward[field][part][:, step, local][:, None, None, None]
                    term = weight * pieces[step][field, local][None]
                    total = term if total is None else total + term
        halves.append(total)
    spectrum = jnp.stack(halves)


    start = position * chunk
    faces_y = tuple(lax.dynamic_slice_in_dim(one_face, start, chunk, axis=2) for one_face in faces)
    total_y = lax.dynamic_slice_in_dim(face_total, start, chunk, axis=2)
    shifted_real = eigenvalues[0][:, None, None, None] + total_y[None]
    eigen_imag = eigenvalues[1][:, None, None, None]
    squared = shifted_real * shifted_real + eigen_imag * eigen_imag
    ratio_real, ratio_imag = lax.optimization_barrier((shifted_real / squared, eigen_imag / squared))

    summed = spectrum
    correction = None
    for sweep_number in range(SWEEPS):
        if sweep_number > 0:
            x_halo = halos(correction, "space", 2)
            y_halo = column_halos(correction, "tm")
            summed = spectrum + neighbour_sum(correction, faces_y, x_halo, y_halo)
        correction = jnp.stack(
            [
                summed[0] * ratio_real + summed[1] * ratio_imag,
                summed[1] * ratio_real - summed[0] * ratio_imag,
            ]
        )

    back = []
    for step in range(groups):
        target = (position + step) % groups
        piece = jnp.einsum("lfk,fkxzy->lxzy", inverse[step], correction, precision=HIGHEST_PRECISION)
        if step > 0:
            piece = lax.ppermute(piece, "tm", ring_pairs(groups, step))
        back.append(piece)
    arrived = jnp.stack(back)
    update = jnp.concatenate(
        [lax.dynamic_index_in_dim(arrived, (position - j) % groups, axis=0, keepdims=False) for j in range(groups)],
        axis=3,
    )
    return age_field + update


def solution(mesh):
    in_specs = (
        P("tm", "space", None, None),
        P("tm", "space", None, None),
        P("space", None, None),
        P(),
        P(),
    )
    out_specs = P("tm", "space", None, None)
    return jax.shard_map(shards, mesh=mesh, in_specs=in_specs, out_specs=out_specs, check_vma=False)
```

```python
import math

import jax
import jax.numpy as jnp
from jax import lax
from jax.sharding import PartitionSpec as P

SWEEPS = 4


HIGHEST_PRECISION = lax.Precision.HIGHEST


def shift_pairs(count, step):
    return [(i, i + step) for i in range(count) if 0 <= i + step < count]


def halos(array, axis, dim):
    count = lax.axis_size(axis)
    length = array.shape[dim]
    last = lax.slice_in_dim(array, length - 1, length, axis=dim)
    first = lax.slice_in_dim(array, 0, 1, axis=dim)
    index = lax.axis_index(axis)
    before = lax.ppermute(last, axis, ring_pairs(count, 1))
    after = lax.ppermute(first, axis, ring_pairs(count, -1))
    before = jnp.where(index == 0, jnp.zeros_like(before), before)
    after = jnp.where(index == count - 1, jnp.zeros_like(after), after)
    return before, after


def column_halos(array, axis):
    count = lax.axis_size(axis)
    before = lax.ppermute(array[..., -1], axis, shift_pairs(count, 1))
    after = lax.ppermute(array[..., 0], axis, shift_pairs(count, -1))
    return before[..., None], after[..., None]


def ring_pairs(count, step):
    return [(i, (i + step) % count) for i in range(count)]


def shifted_pair(field, before, after, dim):
    length = field.shape[dim]
    low = jnp.concatenate([before, lax.slice_in_dim(field, 0, length - 1, axis=dim)], axis=dim)
    high = jnp.concatenate([lax.slice_in_dim(field, 1, length, axis=dim), after], axis=dim)
    return low, high


def zero_shifted(field, dim):
    edge_shape = list(field.shape)
    edge_shape[dim] = 1
    zero = jnp.zeros(edge_shape, field.dtype)
    return shifted_pair(field, zero, zero, dim)


def neighbour_sum(field, faces, x_halo, y_halo):
    nd = field.ndim
    xm, xp = shifted_pair(field, x_halo[0], x_halo[1], nd - 3)
    zm, zp = zero_shifted(field, nd - 2)
    if y_halo is None:
        ym, yp = zero_shifted(field, nd - 1)
    else:
        ym, yp = shifted_pair(field, y_halo[0], y_halo[1], nd - 1)
    moved = (xm, xp, zm, zp, ym, yp)
    result = faces[0] * moved[0]
    for one_face, one_moved in zip(faces[1:], moved[1:]):
        result = result + one_face * one_moved
    return result


def face_halos(conductivity, age_field):
    count = lax.axis_size("space")
    width = conductivity.shape[0]
    last = jnp.concatenate([conductivity[width - 1 :][None], age_field[:, width - 1 :]], axis=0)
    first = jnp.concatenate([conductivity[:1][None], age_field[:, :1]], axis=0)
    index = lax.axis_index("space")
    before = lax.ppermute(last, "space", ring_pairs(count, 1))
    after = lax.ppermute(first, "space", ring_pairs(count, -1))
    before = jnp.where(index == 0, jnp.zeros_like(before), before)
    after = jnp.where(index == count - 1, jnp.zeros_like(after), after)
    return (before[0], after[0]), (before[1:], after[1:])


def phase_tables(products, count):
    angles = 2.0 * math.pi / count * (products % count).astype(jnp.float32)
    return jnp.cos(angles), jnp.sin(angles)


def shards(age_field, source_term, conductivity, memory_weights, eigenvalues):
    groups = lax.axis_size("tm")
    position = lax.axis_index("tm")
    steps_local, width_x, depth_z, length_y = age_field.shape
    total_steps = steps_local * groups

    cond_halo, age_halo = face_halos(conductivity, age_field)

    c_low, c_high = shifted_pair(conductivity, cond_halo[0], cond_halo[1], 0)
    z_low, z_high = zero_shifted(conductivity, 1)
    y_low, y_high = zero_shifted(conductivity, 2)
    faces = tuple(0.5 * (conductivity + other) for other in (c_low, c_high, z_low, z_high, y_low, y_high))
    face_total = faces[0]
    for one_face in faces[1:]:
        face_total = face_total + one_face

    spread = neighbour_sum(age_field, faces, age_halo, None) - face_total * age_field
    partial = source_term + spread
    stacked = jnp.stack([partial, age_field])

    frequency = jnp.arange(total_steps, dtype=jnp.int32)
    lag = jnp.arange(total_steps, dtype=jnp.int32)
    cos_w, sin_w = phase_tables(frequency[:, None] * lag[None, :], total_steps)
    weight_real = jnp.sum(memory_weights[None, :] * cos_w, axis=1)[:, None, None]
    weight_imag = -jnp.sum(memory_weights[None, :] * sin_w, axis=1)[:, None, None]
    piece = jnp.arange(groups, dtype=jnp.int32)[None, :, None]
    local = jnp.arange(steps_local, dtype=jnp.int32)[None, None, :]
    step_of = ((position - piece) % groups) * steps_local + local
    cos_f, sin_f = phase_tables(frequency[:, None, None] * step_of, total_steps)
    forward = (
        (cos_f, -sin_f),
        (-(weight_real * cos_f + weight_imag * sin_f), weight_real * sin_f - weight_imag * cos_f),
    )
    step_to = ((position + piece[0, :, :, None]) % groups) * steps_local + local[0, :, :, None]
    cos_i, sin_i = phase_tables(step_to * frequency[None, None, :], total_steps)
    inverse = jnp.stack([cos_i, -sin_i], axis=2) / total_steps

    common = (stacked, forward, inverse, faces, face_total, eigenvalues, age_field)
    if depth_z % groups == 0:
        return z_split(*common)
    return y_split(*common)


def z_split(stacked, forward, inverse, faces, face_total, eigenvalues, age_field):
    groups = lax.axis_size("tm")
    position = lax.axis_index("tm")
    _, steps_local, width_x, depth_z, length_y = stacked.shape
    total_steps = steps_local * groups
    rows = depth_z // groups

    pieces = []
    for step in range(groups):
        target = (position + step) % groups
        piece = lax.dynamic_slice_in_dim(stacked, target * rows, rows, axis=3)
        if step > 0:
            piece = lax.ppermute(piece, "tm", ring_pairs(groups, step))
        pieces.append(piece)

    halves = []
    for part in range(2):
        total = None
        for step in range(groups):
            for field in range(2):
                for local in range(steps_local):
                    weight = forward[field][part][:, step, local][None, None, :, None]
                    term = weight * pieces[step][field, local][:, :, None, :]
                    total = term if total is None else total + term
        halves.append(total)
    spectrum = jnp.stack(halves)

    start = position * rows
    faces_z = tuple(lax.dynamic_slice_in_dim(one_face, start, rows, axis=1)[:, :, None, :] for one_face in faces)
    total_z = lax.dynamic_slice_in_dim(face_total, start, rows, axis=1)[:, :, None, :]
    shifted_real = eigenvalues[0][None, None, :, None] + total_z
    eigen_imag = eigenvalues[1][None, None, :, None]
    squared = shifted_real * shifted_real + eigen_imag * eigen_imag
    ratio_real, ratio_imag = lax.optimization_barrier((shifted_real / squared, eigen_imag / squared))

    summed = spectrum
    correction = None
    for sweep_number in range(SWEEPS):
        if sweep_number > 0:
            x_low, x_high = halos(correction, "space", 1)
            z_low, z_high = halos(correction, "tm", 2)
            xm, xp = shifted_pair(correction, x_low, x_high, 1)
            zm, zp = shifted_pair(correction, z_low, z_high, 2)
            ym, yp = zero_shifted(correction, 4)
            moved = (xm, xp, zm, zp, ym, yp)
            total = faces_z[0] * moved[0]
            for one_face, one_moved in zip(faces_z[1:], moved[1:]):
                total = total + one_face * one_moved
            summed = spectrum + total
        correction = jnp.stack(
            [
                summed[0] * ratio_real + summed[1] * ratio_imag,
                summed[1] * ratio_real - summed[0] * ratio_imag,
            ]
        )

    back = []
    for step in range(groups):
        target = (position + step) % groups
        piece = jnp.einsum("lfk,fxzky->lxzy", inverse[step], correction, precision=HIGHEST_PRECISION)
        if step > 0:
            piece = lax.ppermute(piece, "tm", ring_pairs(groups, step))
        back.append(piece)
    arrived = jnp.stack(back)
    update = jnp.concatenate(
        [lax.dynamic_index_in_dim(arrived, (position - j) % groups, axis=0, keepdims=False) for j in range(groups)],
        axis=2,
    )
    return age_field + update


def y_split(stacked, forward, inverse, faces, face_total, eigenvalues, age_field):
    groups = lax.axis_size("tm")
    position = lax.axis_index("tm")
    _, steps_local, width_x, depth_z, length_y = stacked.shape
    total_steps = steps_local * groups
    chunk = length_y // groups

    pieces = []
    for step in range(groups):
        target = (position + step) % groups
        piece = lax.dynamic_slice_in_dim(stacked, target * chunk, chunk, axis=4)
        if step > 0:
            piece = lax.ppermute(piece, "tm", ring_pairs(groups, step))
        pieces.append(piece)

    halves = []
    for part in range(2):
        total = None
        for step in range(groups):
            for field in range(2):
                for local in range(steps_local):
                    weight = forward[field][part][:, step, local][:, None, None, None]
                    term = weight * pieces[step][field, local][None]
                    total = term if total is None else total + term
        halves.append(total)
    spectrum = jnp.stack(halves)


    start = position * chunk
    faces_y = tuple(lax.dynamic_slice_in_dim(one_face, start, chunk, axis=2) for one_face in faces)
    total_y = lax.dynamic_slice_in_dim(face_total, start, chunk, axis=2)
    shifted_real = eigenvalues[0][:, None, None, None] + total_y[None]
    eigen_imag = eigenvalues[1][:, None, None, None]
    squared = shifted_real * shifted_real + eigen_imag * eigen_imag
    ratio_real, ratio_imag = lax.optimization_barrier((shifted_real / squared, eigen_imag / squared))

    summed = spectrum
    correction = None
    for sweep_number in range(SWEEPS):
        if sweep_number > 0:
            x_halo = halos(correction, "space", 2)
            y_halo = column_halos(correction, "tm")
            summed = spectrum + neighbour_sum(correction, faces_y, x_halo, y_halo)
        correction = jnp.stack(
            [
                summed[0] * ratio_real + summed[1] * ratio_imag,
                summed[1] * ratio_real - summed[0] * ratio_imag,
            ]
        )

    back = []
    for step in range(groups):
        target = (position + step) % groups
        piece = jnp.einsum("lfk,fkxzy->lxzy", inverse[step], correction, precision=HIGHEST_PRECISION)
        if step > 0:
            piece = lax.ppermute(piece, "tm", ring_pairs(groups, step))
        back.append(piece)
    arrived = jnp.stack(back)
    update = jnp.concatenate(
        [lax.dynamic_index_in_dim(arrived, (position - j) % groups, axis=0, keepdims=False) for j in range(groups)],
        axis=3,
    )
    return age_field + update


def solution(mesh):
    in_specs = (
        P("tm", "space", None, None),
        P("tm", "space", None, None),
        P("space", None, None),
        P(),
        P(),
    )
    out_specs = P("tm", "space", None, None)
    return jax.shard_map(shards, mesh=mesh, in_specs=in_specs, out_specs=out_specs, check_vma=False)
```

```python
import math

import jax
import jax.numpy as jnp
from jax import lax
from jax.sharding import PartitionSpec as P

SWEEPS = 4


HIGHEST_PRECISION = lax.Precision.HIGHEST


def shift_pairs(count, step):
    return [(i, i + step) for i in range(count) if 0 <= i + step < count]


def halos(array, axis, dim, parts=1):
    count = lax.axis_size(axis)
    index = lax.axis_index(axis)
    length = array.shape[dim]
    last = lax.slice_in_dim(array, length - 1, length, axis=dim)
    first = lax.slice_in_dim(array, 0, 1, axis=dim)
    last = jnp.where(index == count - 1, jnp.zeros_like(last), last)
    first = jnp.where(index == 0, jnp.zeros_like(first), first)
    size = array.shape[0] // parts
    before = [lax.ppermute(last[i * size : (i + 1) * size], axis, ring_pairs(count, 1)) for i in range(parts)]
    after = [lax.ppermute(first[i * size : (i + 1) * size], axis, ring_pairs(count, -1)) for i in range(parts)]
    if parts == 1:
        return before[0], after[0]
    return jnp.concatenate(before, axis=0), jnp.concatenate(after, axis=0)


def column_halos(array, axis):
    count = lax.axis_size(axis)
    before = lax.ppermute(array[..., -1], axis, shift_pairs(count, 1))
    after = lax.ppermute(array[..., 0], axis, shift_pairs(count, -1))
    return before[..., None], after[..., None]


def ring_pairs(count, step):
    return [(i, (i + step) % count) for i in range(count)]


def shifted_pair(field, before, after, dim):
    length = field.shape[dim]
    low = jnp.concatenate([before, lax.slice_in_dim(field, 0, length - 1, axis=dim)], axis=dim)
    high = jnp.concatenate([lax.slice_in_dim(field, 1, length, axis=dim), after], axis=dim)
    return low, high


def zero_shifted(field, dim):
    edge_shape = list(field.shape)
    edge_shape[dim] = 1
    zero = jnp.zeros(edge_shape, field.dtype)
    return shifted_pair(field, zero, zero, dim)


def neighbour_sum(field, faces, x_halo, y_halo):
    nd = field.ndim
    xm, xp = shifted_pair(field, x_halo[0], x_halo[1], nd - 3)
    zm, zp = zero_shifted(field, nd - 2)
    if y_halo is None:
        ym, yp = zero_shifted(field, nd - 1)
    else:
        ym, yp = shifted_pair(field, y_halo[0], y_halo[1], nd - 1)
    moved = (xm, xp, zm, zp, ym, yp)
    result = faces[0] * moved[0]
    for one_face, one_moved in zip(faces[1:], moved[1:]):
        result = result + one_face * one_moved
    return result


def face_halos(conductivity, age_field):
    count = lax.axis_size("space")
    width = conductivity.shape[0]
    last = jnp.concatenate([conductivity[width - 1 :][None], age_field[:, width - 1 :]], axis=0)
    first = jnp.concatenate([conductivity[:1][None], age_field[:, :1]], axis=0)
    index = lax.axis_index("space")
    last = jnp.where(index == count - 1, jnp.zeros_like(last), last)
    first = jnp.where(index == 0, jnp.zeros_like(first), first)
    before = lax.ppermute(last, "space", ring_pairs(count, 1))
    after = lax.ppermute(first, "space", ring_pairs(count, -1))
    return (before[0], after[0]), (before[1:], after[1:])


def phase_tables(products, count):
    angles = 2.0 * math.pi / count * (products % count).astype(jnp.float32)
    return jnp.cos(angles), jnp.sin(angles)


def shards(age_field, source_term, conductivity, memory_weights, eigenvalues):
    groups = lax.axis_size("tm")
    position = lax.axis_index("tm")
    steps_local, width_x, depth_z, length_y = age_field.shape
    total_steps = steps_local * groups

    cond_halo, age_halo = face_halos(conductivity, age_field)

    c_low, c_high = shifted_pair(conductivity, cond_halo[0], cond_halo[1], 0)
    z_low, z_high = zero_shifted(conductivity, 1)
    y_low, y_high = zero_shifted(conductivity, 2)
    faces = tuple(0.5 * (conductivity + other) for other in (c_low, c_high, z_low, z_high, y_low, y_high))
    face_total = faces[0]
    for one_face in faces[1:]:
        face_total = face_total + one_face

    spread = neighbour_sum(age_field, faces, age_halo, None) - face_total * age_field
    partial = source_term + spread
    stacked = jnp.stack([partial, age_field])

    frequency = jnp.arange(total_steps, dtype=jnp.int32)
    lag = jnp.arange(total_steps, dtype=jnp.int32)
    cos_w, sin_w = phase_tables(frequency[:, None] * lag[None, :], total_steps)
    weight_real = jnp.sum(memory_weights[None, :] * cos_w, axis=1)[:, None, None]
    weight_imag = -jnp.sum(memory_weights[None, :] * sin_w, axis=1)[:, None, None]
    piece = jnp.arange(groups, dtype=jnp.int32)[None, :, None]
    local = jnp.arange(steps_local, dtype=jnp.int32)[None, None, :]
    step_of = ((position - piece) % groups) * steps_local + local
    cos_f, sin_f = phase_tables(frequency[:, None, None] * step_of, total_steps)
    forward = (
        (cos_f, -sin_f),
        (-(weight_real * cos_f + weight_imag * sin_f), weight_real * sin_f - weight_imag * cos_f),
    )
    step_to = ((position + piece[0, :, :, None]) % groups) * steps_local + local[0, :, :, None]
    cos_i, sin_i = phase_tables(step_to * frequency[None, None, :], total_steps)
    inverse = jnp.stack([cos_i, -sin_i], axis=2) / total_steps

    common = (stacked, forward, inverse, faces, face_total, eigenvalues, age_field)
    if depth_z % groups == 0:
        return z_split(*common)
    return y_split(*common)


def z_split(stacked, forward, inverse, faces, face_total, eigenvalues, age_field):
    groups = lax.axis_size("tm")
    position = lax.axis_index("tm")
    _, steps_local, width_x, depth_z, length_y = stacked.shape
    total_steps = steps_local * groups
    rows = depth_z // groups

    pieces = []
    for step in range(groups):
        target = (position + step) % groups
        piece = lax.dynamic_slice_in_dim(stacked, target * rows, rows, axis=3)
        if step > 0:
            piece = lax.ppermute(piece, "tm", ring_pairs(groups, step))
        pieces.append(piece)

    halves = []
    for part in range(2):
        total = None
        for step in range(groups):
            for field in range(2):
                for local in range(steps_local):
                    weight = forward[field][part][:, step, local][None, None, :, None]
                    term = weight * pieces[step][field, local][:, :, None, :]
                    total = term if total is None else total + term
        halves.append(total)
    spectrum = jnp.stack(halves)

    start = position * rows
    faces_z = tuple(lax.dynamic_slice_in_dim(one_face, start, rows, axis=1)[:, :, None, :] for one_face in faces)
    total_z = lax.dynamic_slice_in_dim(face_total, start, rows, axis=1)[:, :, None, :]
    shifted_real = eigenvalues[0][None, None, :, None] + total_z
    eigen_imag = eigenvalues[1][None, None, :, None]
    squared = shifted_real * shifted_real + eigen_imag * eigen_imag
    ratio_real, ratio_imag = lax.optimization_barrier((shifted_real / squared, eigen_imag / squared))

    summed = spectrum
    correction = None
    for sweep_number in range(SWEEPS):
        if sweep_number > 0:
            x_low, x_high = halos(correction, "space", 1, parts=2)
            z_low, z_high = halos(correction, "tm", 2)
            xm, xp = shifted_pair(correction, x_low, x_high, 1)
            zm, zp = shifted_pair(correction, z_low, z_high, 2)
            ym, yp = zero_shifted(correction, 4)
            moved = (xm, xp, zm, zp, ym, yp)
            total = faces_z[0] * moved[0]
            for one_face, one_moved in zip(faces_z[1:], moved[1:]):
                total = total + one_face * one_moved
            summed = spectrum + total
        correction = jnp.stack(
            [
                summed[0] * ratio_real + summed[1] * ratio_imag,
                summed[1] * ratio_real - summed[0] * ratio_imag,
            ]
        )

    back = []
    for step in range(groups):
        target = (position + step) % groups
        piece = jnp.einsum("lfk,fxzky->lxzy", inverse[step], correction, precision=HIGHEST_PRECISION)
        if step > 0:
            piece = lax.ppermute(piece, "tm", ring_pairs(groups, step))
        back.append(piece)
    arrived = jnp.stack(back)
    update = jnp.concatenate(
        [lax.dynamic_index_in_dim(arrived, (position - j) % groups, axis=0, keepdims=False) for j in range(groups)],
        axis=2,
    )
    return age_field + update


def y_split(stacked, forward, inverse, faces, face_total, eigenvalues, age_field):
    groups = lax.axis_size("tm")
    position = lax.axis_index("tm")
    _, steps_local, width_x, depth_z, length_y = stacked.shape
    total_steps = steps_local * groups
    chunk = length_y // groups

    pieces = []
    for step in range(groups):
        target = (position + step) % groups
        piece = lax.dynamic_slice_in_dim(stacked, target * chunk, chunk, axis=4)
        if step > 0:
            piece = lax.ppermute(piece, "tm", ring_pairs(groups, step))
        pieces.append(piece)

    halves = []
    for part in range(2):
        total = None
        for step in range(groups):
            for field in range(2):
                for local in range(steps_local):
                    weight = forward[field][part][:, step, local][:, None, None, None]
                    term = weight * pieces[step][field, local][None]
                    total = term if total is None else total + term
        halves.append(total)
    spectrum = jnp.stack(halves)


    start = position * chunk
    faces_y = tuple(lax.dynamic_slice_in_dim(one_face, start, chunk, axis=2) for one_face in faces)
    total_y = lax.dynamic_slice_in_dim(face_total, start, chunk, axis=2)
    shifted_real = eigenvalues[0][:, None, None, None] + total_y[None]
    eigen_imag = eigenvalues[1][:, None, None, None]
    squared = shifted_real * shifted_real + eigen_imag * eigen_imag
    ratio_real, ratio_imag = lax.optimization_barrier((shifted_real / squared, eigen_imag / squared))

    summed = spectrum
    correction = None
    for sweep_number in range(SWEEPS):
        if sweep_number > 0:
            x_halo = halos(correction, "space", 2)
            y_halo = column_halos(correction, "tm")
            summed = spectrum + neighbour_sum(correction, faces_y, x_halo, y_halo)
        correction = jnp.stack(
            [
                summed[0] * ratio_real + summed[1] * ratio_imag,
                summed[1] * ratio_real - summed[0] * ratio_imag,
            ]
        )

    back = []
    for step in range(groups):
        target = (position + step) % groups
        piece = jnp.einsum("lfk,fkxzy->lxzy", inverse[step], correction, precision=HIGHEST_PRECISION)
        if step > 0:
            piece = lax.ppermute(piece, "tm", ring_pairs(groups, step))
        back.append(piece)
    arrived = jnp.stack(back)
    update = jnp.concatenate(
        [lax.dynamic_index_in_dim(arrived, (position - j) % groups, axis=0, keepdims=False) for j in range(groups)],
        axis=3,
    )
    return age_field + update


def solution(mesh):
    in_specs = (
        P("tm", "space", None, None),
        P("tm", "space", None, None),
        P("space", None, None),
        P(),
        P(),
    )
    out_specs = P("tm", "space", None, None)
    return jax.shard_map(shards, mesh=mesh, in_specs=in_specs, out_specs=out_specs, check_vma=False)
```

```python
import math

import jax
import jax.numpy as jnp
from jax import lax
from jax.sharding import PartitionSpec as P

SWEEPS = 4


HIGHEST_PRECISION = lax.Precision.HIGHEST


def shift_pairs(count, step):
    return [(i, i + step) for i in range(count) if 0 <= i + step < count]


def halos(array, axis, dim, parts=1):
    count = lax.axis_size(axis)
    index = lax.axis_index(axis)
    length = array.shape[dim]
    last = lax.slice_in_dim(array, length - 1, length, axis=dim)
    first = lax.slice_in_dim(array, 0, 1, axis=dim)
    last = jnp.where(index == count - 1, jnp.zeros_like(last), last)
    first = jnp.where(index == 0, jnp.zeros_like(first), first)
    size = array.shape[0] // parts
    before = [lax.ppermute(last[i * size : (i + 1) * size], axis, ring_pairs(count, 1)) for i in range(parts)]
    after = [lax.ppermute(first[i * size : (i + 1) * size], axis, ring_pairs(count, -1)) for i in range(parts)]
    if parts == 1:
        return before[0], after[0]
    return jnp.concatenate(before, axis=0), jnp.concatenate(after, axis=0)


def column_halos(array, axis):
    count = lax.axis_size(axis)
    before = lax.ppermute(array[..., -1], axis, shift_pairs(count, 1))
    after = lax.ppermute(array[..., 0], axis, shift_pairs(count, -1))
    return before[..., None], after[..., None]


def ring_pairs(count, step):
    return [(i, (i + step) % count) for i in range(count)]


def shifted_pair(field, before, after, dim):
    length = field.shape[dim]
    low = jnp.concatenate([before, lax.slice_in_dim(field, 0, length - 1, axis=dim)], axis=dim)
    high = jnp.concatenate([lax.slice_in_dim(field, 1, length, axis=dim), after], axis=dim)
    return low, high


def zero_shifted(field, dim):
    edge_shape = list(field.shape)
    edge_shape[dim] = 1
    zero = jnp.zeros(edge_shape, field.dtype)
    return shifted_pair(field, zero, zero, dim)


def neighbour_sum(field, faces, x_halo, y_halo):
    nd = field.ndim
    xm, xp = shifted_pair(field, x_halo[0], x_halo[1], nd - 3)
    zm, zp = zero_shifted(field, nd - 2)
    if y_halo is None:
        ym, yp = zero_shifted(field, nd - 1)
    else:
        ym, yp = shifted_pair(field, y_halo[0], y_halo[1], nd - 1)
    moved = (xm, xp, zm, zp, ym, yp)
    result = faces[0] * moved[0]
    for one_face, one_moved in zip(faces[1:], moved[1:]):
        result = result + one_face * one_moved
    return result


def face_halos(conductivity, age_field):
    count = lax.axis_size("space")
    width = conductivity.shape[0]
    last = jnp.concatenate([conductivity[width - 1 :][None], age_field[:, width - 1 :]], axis=0)
    first = jnp.concatenate([conductivity[:1][None], age_field[:, :1]], axis=0)
    index = lax.axis_index("space")
    last = jnp.where(index == count - 1, jnp.zeros_like(last), last)
    first = jnp.where(index == 0, jnp.zeros_like(first), first)
    before = lax.ppermute(last, "space", ring_pairs(count, 1))
    after = lax.ppermute(first, "space", ring_pairs(count, -1))
    return (before[0], after[0]), (before[1:], after[1:])


def phase_tables(products, count):
    angles = 2.0 * math.pi / count * (products % count).astype(jnp.float32)
    return jnp.cos(angles), jnp.sin(angles)


def shards(age_field, source_term, conductivity, memory_weights, eigenvalues):
    groups = lax.axis_size("tm")
    position = lax.axis_index("tm")
    steps_local, width_x, depth_z, length_y = age_field.shape
    total_steps = steps_local * groups

    cond_halo, age_halo = face_halos(conductivity, age_field)

    c_low, c_high = shifted_pair(conductivity, cond_halo[0], cond_halo[1], 0)
    z_low, z_high = zero_shifted(conductivity, 1)
    y_low, y_high = zero_shifted(conductivity, 2)
    faces = tuple(0.5 * (conductivity + other) for other in (c_low, c_high, z_low, z_high, y_low, y_high))
    face_total = faces[0]
    for one_face in faces[1:]:
        face_total = face_total + one_face

    spread = neighbour_sum(age_field, faces, age_halo, None) - face_total * age_field
    partial = source_term + spread
    stacked = jnp.stack([partial, age_field])

    frequency = jnp.arange(total_steps, dtype=jnp.int32)
    lag = jnp.arange(total_steps, dtype=jnp.int32)
    cos_w, sin_w = phase_tables(frequency[:, None] * lag[None, :], total_steps)
    weight_real = jnp.sum(memory_weights[None, :] * cos_w, axis=1)[:, None, None]
    weight_imag = -jnp.sum(memory_weights[None, :] * sin_w, axis=1)[:, None, None]
    piece = jnp.arange(groups, dtype=jnp.int32)[None, :, None]
    local = jnp.arange(steps_local, dtype=jnp.int32)[None, None, :]
    step_of = ((position - piece) % groups) * steps_local + local
    cos_f, sin_f = phase_tables(frequency[:, None, None] * step_of, total_steps)
    forward = (
        (cos_f, -sin_f),
        (-(weight_real * cos_f + weight_imag * sin_f), weight_real * sin_f - weight_imag * cos_f),
    )
    step_to = ((position + piece[0, :, :, None]) % groups) * steps_local + local[0, :, :, None]
    cos_i, sin_i = phase_tables(step_to * frequency[None, None, :], total_steps)
    inverse = jnp.stack([cos_i, -sin_i], axis=2) / total_steps

    common = (stacked, forward, inverse, faces, face_total, eigenvalues, age_field)
    if depth_z % groups == 0:
        return z_split(*common)
    return y_split(*common)


def z_split(stacked, forward, inverse, faces, face_total, eigenvalues, age_field):
    groups = lax.axis_size("tm")
    position = lax.axis_index("tm")
    _, steps_local, width_x, depth_z, length_y = stacked.shape
    total_steps = steps_local * groups
    rows = depth_z // groups

    pieces = []
    for step in range(groups):
        target = (position + step) % groups
        piece = lax.dynamic_slice_in_dim(stacked, target * rows, rows, axis=3)
        if step > 0:
            piece = lax.ppermute(piece, "tm", ring_pairs(groups, step))
        pieces.append(piece)

    halves = []
    for part in range(2):
        total = None
        for step in range(groups):
            for field in range(2):
                for local in range(steps_local):
                    weight = forward[field][part][:, step, local][None, None, :, None]
                    term = weight * pieces[step][field, local][:, :, None, :]
                    total = term if total is None else total + term
        halves.append(total)
    spectrum = jnp.stack(halves)

    start = position * rows
    faces_z = tuple(lax.dynamic_slice_in_dim(one_face, start, rows, axis=1)[:, :, None, :] for one_face in faces)
    total_z = lax.dynamic_slice_in_dim(face_total, start, rows, axis=1)[:, :, None, :]
    shifted_real = eigenvalues[0][None, None, :, None] + total_z
    eigen_imag = eigenvalues[1][None, None, :, None]
    squared = shifted_real * shifted_real + eigen_imag * eigen_imag
    ratio_real, ratio_imag = lax.optimization_barrier((shifted_real / squared, eigen_imag / squared))

    summed = spectrum
    correction = None
    for sweep_number in range(SWEEPS):
        if sweep_number > 0:
            x_low, x_high = halos(correction, "space", 1)
            z_low, z_high = halos(correction, "tm", 2)
            xm, xp = shifted_pair(correction, x_low, x_high, 1)
            zm, zp = shifted_pair(correction, z_low, z_high, 2)
            ym, yp = zero_shifted(correction, 4)
            moved = (xm, xp, zm, zp, ym, yp)
            total = faces_z[0] * moved[0]
            for one_face, one_moved in zip(faces_z[1:], moved[1:]):
                total = total + one_face * one_moved
            summed = spectrum + total
        correction = jnp.stack(
            [
                summed[0] * ratio_real + summed[1] * ratio_imag,
                summed[1] * ratio_real - summed[0] * ratio_imag,
            ]
        )

    back = []
    for step in range(groups):
        target = (position + step) % groups
        piece = jnp.einsum("lfk,fxzky->lxzy", inverse[step], correction, precision=HIGHEST_PRECISION)
        if step > 0:
            piece = lax.ppermute(piece, "tm", ring_pairs(groups, step))
        back.append(piece)
    arrived = jnp.stack(back)
    update = jnp.concatenate(
        [lax.dynamic_index_in_dim(arrived, (position - j) % groups, axis=0, keepdims=False) for j in range(groups)],
        axis=2,
    )
    return age_field + update


def y_split(stacked, forward, inverse, faces, face_total, eigenvalues, age_field):
    groups = lax.axis_size("tm")
    position = lax.axis_index("tm")
    _, steps_local, width_x, depth_z, length_y = stacked.shape
    total_steps = steps_local * groups
    chunk = length_y // groups

    pieces = []
    for step in range(groups):
        target = (position + step) % groups
        piece = lax.dynamic_slice_in_dim(stacked, target * chunk, chunk, axis=4)
        if step > 0:
            piece = lax.ppermute(piece, "tm", ring_pairs(groups, step))
        pieces.append(piece)

    halves = []
    for part in range(2):
        total = None
        for step in range(groups):
            for field in range(2):
                for local in range(steps_local):
                    weight = forward[field][part][:, step, local][:, None, None, None]
                    term = weight * pieces[step][field, local][None]
                    total = term if total is None else total + term
        halves.append(total)
    spectrum = jnp.stack(halves)


    start = position * chunk
    faces_y = tuple(lax.dynamic_slice_in_dim(one_face, start, chunk, axis=2) for one_face in faces)
    total_y = lax.dynamic_slice_in_dim(face_total, start, chunk, axis=2)
    shifted_real = eigenvalues[0][:, None, None, None] + total_y[None]
    eigen_imag = eigenvalues[1][:, None, None, None]
    squared = shifted_real * shifted_real + eigen_imag * eigen_imag
    ratio_real, ratio_imag = lax.optimization_barrier((shifted_real / squared, eigen_imag / squared))

    summed = spectrum
    correction = None
    for sweep_number in range(SWEEPS):
        if sweep_number > 0:
            x_halo = halos(correction, "space", 2)
            y_halo = column_halos(correction, "tm")
            summed = spectrum + neighbour_sum(correction, faces_y, x_halo, y_halo)
        correction = jnp.stack(
            [
                summed[0] * ratio_real + summed[1] * ratio_imag,
                summed[1] * ratio_real - summed[0] * ratio_imag,
            ]
        )

    back = []
    for step in range(groups):
        target = (position + step) % groups
        piece = jnp.einsum("lfk,fkxzy->lxzy", inverse[step], correction, precision=HIGHEST_PRECISION)
        if step > 0:
            piece = lax.ppermute(piece, "tm", ring_pairs(groups, step))
        back.append(piece)
    arrived = jnp.stack(back)
    update = jnp.concatenate(
        [lax.dynamic_index_in_dim(arrived, (position - j) % groups, axis=0, keepdims=False) for j in range(groups)],
        axis=3,
    )
    return age_field + update


def solution(mesh):
    in_specs = (
        P("tm", "space", None, None),
        P("tm", "space", None, None),
        P("space", None, None),
        P(),
        P(),
    )
    out_specs = P("tm", "space", None, None)
    return jax.shard_map(shards, mesh=mesh, in_specs=in_specs, out_specs=out_specs, check_vma=False)
```

```python
import math

import jax
import jax.numpy as jnp
from jax import lax
from jax.sharding import PartitionSpec as P

SWEEPS = 4


HIGHEST_PRECISION = lax.Precision.HIGHEST


def shift_pairs(count, step):
    return [(i, i + step) for i in range(count) if 0 <= i + step < count]


def halos(array, axis, dim, parts=1):
    count = lax.axis_size(axis)
    index = lax.axis_index(axis)
    length = array.shape[dim]
    last = lax.slice_in_dim(array, length - 1, length, axis=dim)
    first = lax.slice_in_dim(array, 0, 1, axis=dim)
    last = jnp.where(index == count - 1, jnp.zeros_like(last), last)
    first = jnp.where(index == 0, jnp.zeros_like(first), first)
    size = array.shape[0] // parts
    before = [lax.ppermute(last[i * size : (i + 1) * size], axis, ring_pairs(count, 1)) for i in range(parts)]
    after = [lax.ppermute(first[i * size : (i + 1) * size], axis, ring_pairs(count, -1)) for i in range(parts)]
    if parts == 1:
        return before[0], after[0]
    return jnp.concatenate(before, axis=0), jnp.concatenate(after, axis=0)


def column_halos(array, axis):
    count = lax.axis_size(axis)
    before = lax.ppermute(array[..., -1], axis, shift_pairs(count, 1))
    after = lax.ppermute(array[..., 0], axis, shift_pairs(count, -1))
    return before[..., None], after[..., None]


def ring_pairs(count, step):
    return [(i, (i + step) % count) for i in range(count)]


def shifted_pair(field, before, after, dim):
    length = field.shape[dim]
    low = jnp.concatenate([before, lax.slice_in_dim(field, 0, length - 1, axis=dim)], axis=dim)
    high = jnp.concatenate([lax.slice_in_dim(field, 1, length, axis=dim), after], axis=dim)
    return low, high


def zero_shifted(field, dim):
    edge_shape = list(field.shape)
    edge_shape[dim] = 1
    zero = jnp.zeros(edge_shape, field.dtype)
    return shifted_pair(field, zero, zero, dim)


def neighbour_sum(field, faces, x_halo, y_halo):
    nd = field.ndim
    xm, xp = shifted_pair(field, x_halo[0], x_halo[1], nd - 3)
    zm, zp = zero_shifted(field, nd - 2)
    if y_halo is None:
        ym, yp = zero_shifted(field, nd - 1)
    else:
        ym, yp = shifted_pair(field, y_halo[0], y_halo[1], nd - 1)
    moved = (xm, xp, zm, zp, ym, yp)
    result = faces[0] * moved[0]
    for one_face, one_moved in zip(faces[1:], moved[1:]):
        result = result + one_face * one_moved
    return result


def face_halos(conductivity, age_field):
    count = lax.axis_size("space")
    width = conductivity.shape[0]
    last = jnp.concatenate([conductivity[width - 1 :][None], age_field[:, width - 1 :]], axis=0)
    first = jnp.concatenate([conductivity[:1][None], age_field[:, :1]], axis=0)
    index = lax.axis_index("space")
    last = jnp.where(index == count - 1, jnp.zeros_like(last), last)
    first = jnp.where(index == 0, jnp.zeros_like(first), first)
    before = lax.ppermute(last, "space", ring_pairs(count, 1))
    after = lax.ppermute(first, "space", ring_pairs(count, -1))
    return (before[0], after[0]), (before[1:], after[1:])


def phase_tables(products, count):
    angles = 2.0 * math.pi / count * (products % count).astype(jnp.float32)
    return jnp.cos(angles), jnp.sin(angles)


def shards(age_field, source_term, conductivity, memory_weights, eigenvalues):
    groups = lax.axis_size("tm")
    position = lax.axis_index("tm")
    steps_local, width_x, depth_z, length_y = age_field.shape
    total_steps = steps_local * groups

    cond_halo, age_halo = face_halos(conductivity, age_field)

    c_low, c_high = shifted_pair(conductivity, cond_halo[0], cond_halo[1], 0)
    z_low, z_high = zero_shifted(conductivity, 1)
    y_low, y_high = zero_shifted(conductivity, 2)
    faces = tuple(0.5 * (conductivity + other) for other in (c_low, c_high, z_low, z_high, y_low, y_high))
    face_total = faces[0]
    for one_face in faces[1:]:
        face_total = face_total + one_face

    spread = neighbour_sum(age_field, faces, age_halo, None) - face_total * age_field
    partial = source_term + spread

    frequency = jnp.arange(total_steps, dtype=jnp.int32)
    lag = jnp.arange(total_steps, dtype=jnp.int32)
    cos_w, sin_w = phase_tables(frequency[:, None] * lag[None, :], total_steps)
    weight_real = jnp.sum(memory_weights[None, :] * cos_w, axis=1)[:, None, None]
    weight_imag = -jnp.sum(memory_weights[None, :] * sin_w, axis=1)[:, None, None]
    piece = jnp.arange(groups, dtype=jnp.int32)[None, :, None]
    local = jnp.arange(steps_local, dtype=jnp.int32)[None, None, :]
    step_of = ((position - piece) % groups) * steps_local + local
    cos_f, sin_f = phase_tables(frequency[:, None, None] * step_of, total_steps)
    forward = (
        (cos_f, -sin_f),
        (-(weight_real * cos_f + weight_imag * sin_f), weight_real * sin_f - weight_imag * cos_f),
    )
    step_to = ((position + piece[0, :, :, None]) % groups) * steps_local + local[0, :, :, None]
    cos_i, sin_i = phase_tables(step_to * frequency[None, None, :], total_steps)
    inverse = jnp.stack([cos_i, -sin_i], axis=2) / total_steps

    if depth_z % groups == 0:
        return z_split(partial, forward, inverse, faces, face_total, eigenvalues, age_field)
    stacked = jnp.stack([partial, age_field])
    return y_split(stacked, forward, inverse, faces, face_total, eigenvalues, age_field)


def z_split(partial, forward, inverse, faces, face_total, eigenvalues, age_field):
    groups = lax.axis_size("tm")
    position = lax.axis_index("tm")
    steps_local, width_x, depth_z, length_y = age_field.shape
    total_steps = steps_local * groups
    rows = depth_z // groups

    def ring(field):
        pieces = []
        for step in range(groups):
            target = (position + step) % groups
            piece = lax.dynamic_slice_in_dim(field, target * rows, rows, axis=2)
            if step > 0:
                piece = lax.ppermute(piece, "tm", ring_pairs(groups, step))
            pieces.append(piece)
        return pieces

    def transform(pieces, field):
        halves = []
        for part in range(2):
            total = None
            for step in range(groups):
                for local in range(steps_local):
                    weight = forward[field][part][:, step, local][None, None, :, None]
                    term = weight * pieces[step][local][:, :, None, :]
                    total = term if total is None else total + term
            halves.append(total)
        return jnp.stack(halves)

    held = transform(ring(age_field), 1)
    spectrum = transform(ring(partial), 0) + held

    start = position * rows
    faces_z = tuple(lax.dynamic_slice_in_dim(one_face, start, rows, axis=1)[:, :, None, :] for one_face in faces)
    total_z = lax.dynamic_slice_in_dim(face_total, start, rows, axis=1)[:, :, None, :]
    shifted_real = eigenvalues[0][None, None, :, None] + total_z
    eigen_imag = eigenvalues[1][None, None, :, None]
    squared = shifted_real * shifted_real + eigen_imag * eigen_imag
    ratio_real, ratio_imag = lax.optimization_barrier((shifted_real / squared, eigen_imag / squared))

    summed = spectrum
    correction = None
    for sweep_number in range(SWEEPS):
        if sweep_number > 0:
            x_low, x_high = halos(correction, "space", 1)
            z_low, z_high = halos(correction, "tm", 2)
            xm, xp = shifted_pair(correction, x_low, x_high, 1)
            zm, zp = shifted_pair(correction, z_low, z_high, 2)
            ym, yp = zero_shifted(correction, 4)
            moved = (xm, xp, zm, zp, ym, yp)
            total = faces_z[0] * moved[0]
            for one_face, one_moved in zip(faces_z[1:], moved[1:]):
                total = total + one_face * one_moved
            summed = spectrum + total
        correction = jnp.stack(
            [
                summed[0] * ratio_real + summed[1] * ratio_imag,
                summed[1] * ratio_real - summed[0] * ratio_imag,
            ]
        )

    back = []
    for step in range(groups):
        target = (position + step) % groups
        piece = jnp.einsum("lfk,fxzky->lxzy", inverse[step], correction, precision=HIGHEST_PRECISION)
        if step > 0:
            piece = lax.ppermute(piece, "tm", ring_pairs(groups, step))
        back.append(piece)
    arrived = jnp.stack(back)
    update = jnp.concatenate(
        [lax.dynamic_index_in_dim(arrived, (position - j) % groups, axis=0, keepdims=False) for j in range(groups)],
        axis=2,
    )
    return age_field + update


def y_split(stacked, forward, inverse, faces, face_total, eigenvalues, age_field):
    groups = lax.axis_size("tm")
    position = lax.axis_index("tm")
    _, steps_local, width_x, depth_z, length_y = stacked.shape
    total_steps = steps_local * groups
    chunk = length_y // groups

    pieces = []
    for step in range(groups):
        target = (position + step) % groups
        piece = lax.dynamic_slice_in_dim(stacked, target * chunk, chunk, axis=4)
        if step > 0:
            piece = lax.ppermute(piece, "tm", ring_pairs(groups, step))
        pieces.append(piece)

    halves = []
    for part in range(2):
        total = None
        for step in range(groups):
            for field in range(2):
                for local in range(steps_local):
                    weight = forward[field][part][:, step, local][:, None, None, None]
                    term = weight * pieces[step][field, local][None]
                    total = term if total is None else total + term
        halves.append(total)
    spectrum = jnp.stack(halves)


    start = position * chunk
    faces_y = tuple(lax.dynamic_slice_in_dim(one_face, start, chunk, axis=2) for one_face in faces)
    total_y = lax.dynamic_slice_in_dim(face_total, start, chunk, axis=2)
    shifted_real = eigenvalues[0][:, None, None, None] + total_y[None]
    eigen_imag = eigenvalues[1][:, None, None, None]
    squared = shifted_real * shifted_real + eigen_imag * eigen_imag
    ratio_real, ratio_imag = lax.optimization_barrier((shifted_real / squared, eigen_imag / squared))

    summed = spectrum
    correction = None
    for sweep_number in range(SWEEPS):
        if sweep_number > 0:
            x_halo = halos(correction, "space", 2)
            y_halo = column_halos(correction, "tm")
            summed = spectrum + neighbour_sum(correction, faces_y, x_halo, y_halo)
        correction = jnp.stack(
            [
                summed[0] * ratio_real + summed[1] * ratio_imag,
                summed[1] * ratio_real - summed[0] * ratio_imag,
            ]
        )

    back = []
    for step in range(groups):
        target = (position + step) % groups
        piece = jnp.einsum("lfk,fkxzy->lxzy", inverse[step], correction, precision=HIGHEST_PRECISION)
        if step > 0:
            piece = lax.ppermute(piece, "tm", ring_pairs(groups, step))
        back.append(piece)
    arrived = jnp.stack(back)
    update = jnp.concatenate(
        [lax.dynamic_index_in_dim(arrived, (position - j) % groups, axis=0, keepdims=False) for j in range(groups)],
        axis=3,
    )
    return age_field + update


def solution(mesh):
    in_specs = (
        P("tm", "space", None, None),
        P("tm", "space", None, None),
        P("space", None, None),
        P(),
        P(),
    )
    out_specs = P("tm", "space", None, None)
    return jax.shard_map(shards, mesh=mesh, in_specs=in_specs, out_specs=out_specs, check_vma=False)
```

```python
import math

import jax
import jax.numpy as jnp
from jax import lax
from jax.sharding import PartitionSpec as P

SWEEPS = 4


HIGHEST_PRECISION = lax.Precision.HIGHEST


def shift_pairs(count, step):
    return [(i, i + step) for i in range(count) if 0 <= i + step < count]


def halos(array, axis, dim, parts=1):
    count = lax.axis_size(axis)
    index = lax.axis_index(axis)
    length = array.shape[dim]
    last = lax.slice_in_dim(array, length - 1, length, axis=dim)
    first = lax.slice_in_dim(array, 0, 1, axis=dim)
    last = jnp.where(index == count - 1, jnp.zeros_like(last), last)
    first = jnp.where(index == 0, jnp.zeros_like(first), first)
    size = array.shape[0] // parts
    before = [lax.ppermute(last[i * size : (i + 1) * size], axis, ring_pairs(count, 1)) for i in range(parts)]
    after = [lax.ppermute(first[i * size : (i + 1) * size], axis, ring_pairs(count, -1)) for i in range(parts)]
    if parts == 1:
        return before[0], after[0]
    return jnp.concatenate(before, axis=0), jnp.concatenate(after, axis=0)


def column_halos(array, axis):
    count = lax.axis_size(axis)
    before = lax.ppermute(array[..., -1], axis, shift_pairs(count, 1))
    after = lax.ppermute(array[..., 0], axis, shift_pairs(count, -1))
    return before[..., None], after[..., None]


def ring_pairs(count, step):
    return [(i, (i + step) % count) for i in range(count)]


def shifted_pair(field, before, after, dim):
    length = field.shape[dim]
    low = jnp.concatenate([before, lax.slice_in_dim(field, 0, length - 1, axis=dim)], axis=dim)
    high = jnp.concatenate([lax.slice_in_dim(field, 1, length, axis=dim), after], axis=dim)
    return low, high


def zero_shifted(field, dim):
    edge_shape = list(field.shape)
    edge_shape[dim] = 1
    zero = jnp.zeros(edge_shape, field.dtype)
    return shifted_pair(field, zero, zero, dim)


def neighbour_sum(field, faces, x_halo, y_halo):
    nd = field.ndim
    xm, xp = shifted_pair(field, x_halo[0], x_halo[1], nd - 3)
    zm, zp = zero_shifted(field, nd - 2)
    if y_halo is None:
        ym, yp = zero_shifted(field, nd - 1)
    else:
        ym, yp = shifted_pair(field, y_halo[0], y_halo[1], nd - 1)
    moved = (xm, xp, zm, zp, ym, yp)
    result = faces[0] * moved[0]
    for one_face, one_moved in zip(faces[1:], moved[1:]):
        result = result + one_face * one_moved
    return result


def face_halos(conductivity, age_field):
    count = lax.axis_size("space")
    width = conductivity.shape[0]
    last = jnp.concatenate([conductivity[width - 1 :][None], age_field[:, width - 1 :]], axis=0)
    first = jnp.concatenate([conductivity[:1][None], age_field[:, :1]], axis=0)
    index = lax.axis_index("space")
    last = jnp.where(index == count - 1, jnp.zeros_like(last), last)
    first = jnp.where(index == 0, jnp.zeros_like(first), first)
    before = lax.ppermute(last, "space", ring_pairs(count, 1))
    after = lax.ppermute(first, "space", ring_pairs(count, -1))
    return (before[0], after[0]), (before[1:], after[1:])


def phase_tables(products, count):
    angles = 2.0 * math.pi / count * (products % count).astype(jnp.float32)
    return jnp.cos(angles), jnp.sin(angles)


def shards(age_field, source_term, conductivity, memory_weights, eigenvalues):
    groups = lax.axis_size("tm")
    position = lax.axis_index("tm")
    steps_local, width_x, depth_z, length_y = age_field.shape
    total_steps = steps_local * groups

    cond_halo, age_halo = face_halos(conductivity, age_field)

    c_low, c_high = shifted_pair(conductivity, cond_halo[0], cond_halo[1], 0)
    z_low, z_high = zero_shifted(conductivity, 1)
    y_low, y_high = zero_shifted(conductivity, 2)
    faces = tuple(0.5 * (conductivity + other) for other in (c_low, c_high, z_low, z_high, y_low, y_high))
    face_total = faces[0]
    for one_face in faces[1:]:
        face_total = face_total + one_face

    spread = neighbour_sum(age_field, faces, age_halo, None) - face_total * age_field
    partial = source_term + spread

    frequency = jnp.arange(total_steps, dtype=jnp.int32)
    lag = jnp.arange(total_steps, dtype=jnp.int32)
    cos_w, sin_w = phase_tables(frequency[:, None] * lag[None, :], total_steps)
    weight_real = jnp.sum(memory_weights[None, :] * cos_w, axis=1)[:, None, None]
    weight_imag = -jnp.sum(memory_weights[None, :] * sin_w, axis=1)[:, None, None]
    piece = jnp.arange(groups, dtype=jnp.int32)[None, :, None]
    local = jnp.arange(steps_local, dtype=jnp.int32)[None, None, :]
    step_of = ((position - piece) % groups) * steps_local + local
    cos_f, sin_f = phase_tables(frequency[:, None, None] * step_of, total_steps)
    forward = (
        (cos_f, -sin_f),
        (-(weight_real * cos_f + weight_imag * sin_f), weight_real * sin_f - weight_imag * cos_f),
    )
    step_to = ((position + piece[0, :, :, None]) % groups) * steps_local + local[0, :, :, None]
    cos_i, sin_i = phase_tables(step_to * frequency[None, None, :], total_steps)
    inverse = jnp.stack([cos_i, -sin_i], axis=2) / total_steps

    if depth_z % groups == 0:
        return z_split(partial, forward, inverse, faces, face_total, eigenvalues, age_field)
    stacked = jnp.stack([partial, age_field])
    return y_split(stacked, forward, inverse, faces, face_total, eigenvalues, age_field)


def z_split(partial, forward, inverse, faces, face_total, eigenvalues, age_field):
    groups = lax.axis_size("tm")
    position = lax.axis_index("tm")
    steps_local, width_x, depth_z, length_y = age_field.shape
    total_steps = steps_local * groups
    rows = depth_z // groups

    def ring(field):
        pieces = []
        for step in range(groups):
            target = (position + step) % groups
            piece = lax.dynamic_slice_in_dim(field, target * rows, rows, axis=2)
            if step > 0:
                piece = lax.ppermute(piece, "tm", ring_pairs(groups, step))
            pieces.append(piece)
        return pieces

    def transform(pieces, field):
        weights = jnp.stack([jnp.transpose(forward[field][part], (1, 2, 0)) for part in range(2)])
        total = None
        for step in range(groups):
            term = jnp.sum(
                weights[:, step][:, :, None, None, :, None] * pieces[step][None, :, :, :, None, :], axis=1
            )
            total = term if total is None else total + term
        return total

    held = transform(ring(age_field), 1)
    spectrum = transform(ring(partial), 0) + held

    start = position * rows
    faces_z = tuple(lax.dynamic_slice_in_dim(one_face, start, rows, axis=1)[:, :, None, :] for one_face in faces)
    total_z = lax.dynamic_slice_in_dim(face_total, start, rows, axis=1)[:, :, None, :]
    shifted_real = eigenvalues[0][None, None, :, None] + total_z
    eigen_imag = eigenvalues[1][None, None, :, None]
    squared = shifted_real * shifted_real + eigen_imag * eigen_imag
    ratio_real, ratio_imag = lax.optimization_barrier((shifted_real / squared, eigen_imag / squared))

    summed = spectrum
    correction = None
    for sweep_number in range(SWEEPS):
        if sweep_number > 0:
            x_low, x_high = halos(correction, "space", 1)
            z_low, z_high = halos(correction, "tm", 2)
            xm, xp = shifted_pair(correction, x_low, x_high, 1)
            zm, zp = shifted_pair(correction, z_low, z_high, 2)
            ym, yp = zero_shifted(correction, 4)
            moved = (xm, xp, zm, zp, ym, yp)
            total = faces_z[0] * moved[0]
            for one_face, one_moved in zip(faces_z[1:], moved[1:]):
                total = total + one_face * one_moved
            summed = spectrum + total
        correction = jnp.stack(
            [
                summed[0] * ratio_real + summed[1] * ratio_imag,
                summed[1] * ratio_real - summed[0] * ratio_imag,
            ]
        )

    back = []
    for step in range(groups):
        target = (position + step) % groups
        piece = jnp.einsum("lfk,fxzky->lxzy", inverse[step], correction, precision=HIGHEST_PRECISION)
        if step > 0:
            piece = lax.ppermute(piece, "tm", ring_pairs(groups, step))
        back.append(piece)
    arrived = jnp.stack(back)
    update = jnp.concatenate(
        [lax.dynamic_index_in_dim(arrived, (position - j) % groups, axis=0, keepdims=False) for j in range(groups)],
        axis=2,
    )
    return age_field + update


def y_split(stacked, forward, inverse, faces, face_total, eigenvalues, age_field):
    groups = lax.axis_size("tm")
    position = lax.axis_index("tm")
    _, steps_local, width_x, depth_z, length_y = stacked.shape
    total_steps = steps_local * groups
    chunk = length_y // groups

    pieces = []
    for step in range(groups):
        target = (position + step) % groups
        piece = lax.dynamic_slice_in_dim(stacked, target * chunk, chunk, axis=4)
        if step > 0:
            piece = lax.ppermute(piece, "tm", ring_pairs(groups, step))
        pieces.append(piece)

    halves = []
    for part in range(2):
        total = None
        for step in range(groups):
            for field in range(2):
                for local in range(steps_local):
                    weight = forward[field][part][:, step, local][:, None, None, None]
                    term = weight * pieces[step][field, local][None]
                    total = term if total is None else total + term
        halves.append(total)
    spectrum = jnp.stack(halves)


    start = position * chunk
    faces_y = tuple(lax.dynamic_slice_in_dim(one_face, start, chunk, axis=2) for one_face in faces)
    total_y = lax.dynamic_slice_in_dim(face_total, start, chunk, axis=2)
    shifted_real = eigenvalues[0][:, None, None, None] + total_y[None]
    eigen_imag = eigenvalues[1][:, None, None, None]
    squared = shifted_real * shifted_real + eigen_imag * eigen_imag
    ratio_real, ratio_imag = lax.optimization_barrier((shifted_real / squared, eigen_imag / squared))

    summed = spectrum
    correction = None
    for sweep_number in range(SWEEPS):
        if sweep_number > 0:
            x_halo = halos(correction, "space", 2)
            y_halo = column_halos(correction, "tm")
            summed = spectrum + neighbour_sum(correction, faces_y, x_halo, y_halo)
        correction = jnp.stack(
            [
                summed[0] * ratio_real + summed[1] * ratio_imag,
                summed[1] * ratio_real - summed[0] * ratio_imag,
            ]
        )

    back = []
    for step in range(groups):
        target = (position + step) % groups
        piece = jnp.einsum("lfk,fkxzy->lxzy", inverse[step], correction, precision=HIGHEST_PRECISION)
        if step > 0:
            piece = lax.ppermute(piece, "tm", ring_pairs(groups, step))
        back.append(piece)
    arrived = jnp.stack(back)
    update = jnp.concatenate(
        [lax.dynamic_index_in_dim(arrived, (position - j) % groups, axis=0, keepdims=False) for j in range(groups)],
        axis=3,
    )
    return age_field + update


def solution(mesh):
    in_specs = (
        P("tm", "space", None, None),
        P("tm", "space", None, None),
        P("space", None, None),
        P(),
        P(),
    )
    out_specs = P("tm", "space", None, None)
    return jax.shard_map(shards, mesh=mesh, in_specs=in_specs, out_specs=out_specs, check_vma=False)
```

```python
import math

import jax
import jax.numpy as jnp
from jax import lax
from jax.sharding import PartitionSpec as P

SWEEPS = 4


HIGHEST_PRECISION = lax.Precision.HIGHEST


def shift_pairs(count, step):
    return [(i, i + step) for i in range(count) if 0 <= i + step < count]


def halos(array, axis, dim, parts=1):
    count = lax.axis_size(axis)
    index = lax.axis_index(axis)
    length = array.shape[dim]
    last = lax.slice_in_dim(array, length - 1, length, axis=dim)
    first = lax.slice_in_dim(array, 0, 1, axis=dim)
    last = jnp.where(index == count - 1, jnp.zeros_like(last), last)
    first = jnp.where(index == 0, jnp.zeros_like(first), first)
    size = array.shape[0] // parts
    before = [lax.ppermute(last[i * size : (i + 1) * size], axis, ring_pairs(count, 1)) for i in range(parts)]
    after = [lax.ppermute(first[i * size : (i + 1) * size], axis, ring_pairs(count, -1)) for i in range(parts)]
    if parts == 1:
        return before[0], after[0]
    return jnp.concatenate(before, axis=0), jnp.concatenate(after, axis=0)


def column_halos(array, axis):
    count = lax.axis_size(axis)
    before = lax.ppermute(array[..., -1], axis, shift_pairs(count, 1))
    after = lax.ppermute(array[..., 0], axis, shift_pairs(count, -1))
    return before[..., None], after[..., None]


def ring_pairs(count, step):
    return [(i, (i + step) % count) for i in range(count)]


def shifted_pair(field, before, after, dim):
    length = field.shape[dim]
    low = jnp.concatenate([before, lax.slice_in_dim(field, 0, length - 1, axis=dim)], axis=dim)
    high = jnp.concatenate([lax.slice_in_dim(field, 1, length, axis=dim), after], axis=dim)
    return low, high


def zero_shifted(field, dim):
    edge_shape = list(field.shape)
    edge_shape[dim] = 1
    zero = jnp.zeros(edge_shape, field.dtype)
    return shifted_pair(field, zero, zero, dim)


def neighbour_sum(field, faces, x_halo, y_halo):
    nd = field.ndim
    xm, xp = shifted_pair(field, x_halo[0], x_halo[1], nd - 3)
    zm, zp = zero_shifted(field, nd - 2)
    if y_halo is None:
        ym, yp = zero_shifted(field, nd - 1)
    else:
        ym, yp = shifted_pair(field, y_halo[0], y_halo[1], nd - 1)
    moved = (xm, xp, zm, zp, ym, yp)
    result = faces[0] * moved[0]
    for one_face, one_moved in zip(faces[1:], moved[1:]):
        result = result + one_face * one_moved
    return result


def face_halos(conductivity, age_field):
    count = lax.axis_size("space")
    width = conductivity.shape[0]
    last = jnp.concatenate([conductivity[width - 1 :][None], age_field[:, width - 1 :]], axis=0)
    first = jnp.concatenate([conductivity[:1][None], age_field[:, :1]], axis=0)
    index = lax.axis_index("space")
    last = jnp.where(index == count - 1, jnp.zeros_like(last), last)
    first = jnp.where(index == 0, jnp.zeros_like(first), first)
    before = lax.ppermute(last, "space", ring_pairs(count, 1))
    after = lax.ppermute(first, "space", ring_pairs(count, -1))
    return (before[0], after[0]), (before[1:], after[1:])


def phase_tables(products, count):
    angles = 2.0 * math.pi / count * (products % count).astype(jnp.float32)
    return jnp.cos(angles), jnp.sin(angles)


def shards(age_field, source_term, conductivity, memory_weights, eigenvalues):
    groups = lax.axis_size("tm")
    position = lax.axis_index("tm")
    steps_local, width_x, depth_z, length_y = age_field.shape
    total_steps = steps_local * groups

    cond_halo, age_halo = face_halos(conductivity, age_field)

    c_low, c_high = shifted_pair(conductivity, cond_halo[0], cond_halo[1], 0)
    z_low, z_high = zero_shifted(conductivity, 1)
    y_low, y_high = zero_shifted(conductivity, 2)
    faces = tuple(0.5 * (conductivity + other) for other in (c_low, c_high, z_low, z_high, y_low, y_high))
    face_total = faces[0]
    for one_face in faces[1:]:
        face_total = face_total + one_face

    spread = neighbour_sum(age_field, faces, age_halo, None) - face_total * age_field
    partial = source_term + spread

    frequency = jnp.arange(total_steps, dtype=jnp.int32)
    lag = jnp.arange(total_steps, dtype=jnp.int32)
    cos_w, sin_w = phase_tables(frequency[:, None] * lag[None, :], total_steps)
    weight_real = jnp.sum(memory_weights[None, :] * cos_w, axis=1)[:, None, None]
    weight_imag = -jnp.sum(memory_weights[None, :] * sin_w, axis=1)[:, None, None]
    piece = jnp.arange(groups, dtype=jnp.int32)[None, :, None]
    local = jnp.arange(steps_local, dtype=jnp.int32)[None, None, :]
    step_of = ((position - piece) % groups) * steps_local + local
    cos_f, sin_f = phase_tables(frequency[:, None, None] * step_of, total_steps)
    forward = (
        (cos_f, -sin_f),
        (-(weight_real * cos_f + weight_imag * sin_f), weight_real * sin_f - weight_imag * cos_f),
    )
    step_to = ((position + piece[0, :, :, None]) % groups) * steps_local + local[0, :, :, None]
    cos_i, sin_i = phase_tables(step_to * frequency[None, None, :], total_steps)
    inverse = jnp.stack([cos_i, -sin_i], axis=2) / total_steps

    if depth_z % groups == 0:
        return z_split(partial, forward, inverse, faces, face_total, eigenvalues, age_field)
    stacked = jnp.stack([partial, age_field])
    return y_split(stacked, forward, inverse, faces, face_total, eigenvalues, age_field)


def z_split(partial, forward, inverse, faces, face_total, eigenvalues, age_field):
    groups = lax.axis_size("tm")
    position = lax.axis_index("tm")
    steps_local, width_x, depth_z, length_y = age_field.shape
    total_steps = steps_local * groups
    rows = depth_z // groups

    def ring(field):
        pieces = []
        for step in range(groups):
            target = (position + step) % groups
            piece = lax.dynamic_slice_in_dim(field, target * rows, rows, axis=2)
            if step > 0:
                piece = lax.ppermute(piece, "tm", ring_pairs(groups, step))
            pieces.append(piece)
        return pieces

    def transform(pieces, field):
        weights = jnp.stack([jnp.transpose(forward[field][part], (1, 2, 0)) for part in range(2)])
        total = None
        for step in range(groups):
            term = jnp.sum(
                weights[:, step][:, :, None, None, :, None] * pieces[step][None, :, :, :, None, :], axis=1
            )
            total = term if total is None else total + term
        return total

    age_pieces, partial = lax.optimization_barrier((ring(age_field), partial))
    sent = ring(partial)
    spectrum = transform(sent, 0) + transform(age_pieces, 1)

    start = position * rows
    faces_z = tuple(lax.dynamic_slice_in_dim(one_face, start, rows, axis=1)[:, :, None, :] for one_face in faces)
    total_z = lax.dynamic_slice_in_dim(face_total, start, rows, axis=1)[:, :, None, :]
    shifted_real = eigenvalues[0][None, None, :, None] + total_z
    eigen_imag = eigenvalues[1][None, None, :, None]
    squared = shifted_real * shifted_real + eigen_imag * eigen_imag
    ratio_real, ratio_imag = lax.optimization_barrier((shifted_real / squared, eigen_imag / squared))

    summed = spectrum
    correction = None
    for sweep_number in range(SWEEPS):
        if sweep_number > 0:
            x_low, x_high = halos(correction, "space", 1)
            z_low, z_high = halos(correction, "tm", 2)
            xm, xp = shifted_pair(correction, x_low, x_high, 1)
            zm, zp = shifted_pair(correction, z_low, z_high, 2)
            ym, yp = zero_shifted(correction, 4)
            moved = (xm, xp, zm, zp, ym, yp)
            total = faces_z[0] * moved[0]
            for one_face, one_moved in zip(faces_z[1:], moved[1:]):
                total = total + one_face * one_moved
            summed = spectrum + total
        correction = jnp.stack(
            [
                summed[0] * ratio_real + summed[1] * ratio_imag,
                summed[1] * ratio_real - summed[0] * ratio_imag,
            ]
        )

    back = []
    for step in range(groups):
        target = (position + step) % groups
        piece = jnp.einsum("lfk,fxzky->lxzy", inverse[step], correction, precision=HIGHEST_PRECISION)
        if step > 0:
            piece = lax.ppermute(piece, "tm", ring_pairs(groups, step))
        back.append(piece)
    arrived = jnp.stack(back)
    update = jnp.concatenate(
        [lax.dynamic_index_in_dim(arrived, (position - j) % groups, axis=0, keepdims=False) for j in range(groups)],
        axis=2,
    )
    return age_field + update


def y_split(stacked, forward, inverse, faces, face_total, eigenvalues, age_field):
    groups = lax.axis_size("tm")
    position = lax.axis_index("tm")
    _, steps_local, width_x, depth_z, length_y = stacked.shape
    total_steps = steps_local * groups
    chunk = length_y // groups

    pieces = []
    for step in range(groups):
        target = (position + step) % groups
        piece = lax.dynamic_slice_in_dim(stacked, target * chunk, chunk, axis=4)
        if step > 0:
            piece = lax.ppermute(piece, "tm", ring_pairs(groups, step))
        pieces.append(piece)

    halves = []
    for part in range(2):
        total = None
        for step in range(groups):
            for field in range(2):
                for local in range(steps_local):
                    weight = forward[field][part][:, step, local][:, None, None, None]
                    term = weight * pieces[step][field, local][None]
                    total = term if total is None else total + term
        halves.append(total)
    spectrum = jnp.stack(halves)


    start = position * chunk
    faces_y = tuple(lax.dynamic_slice_in_dim(one_face, start, chunk, axis=2) for one_face in faces)
    total_y = lax.dynamic_slice_in_dim(face_total, start, chunk, axis=2)
    shifted_real = eigenvalues[0][:, None, None, None] + total_y[None]
    eigen_imag = eigenvalues[1][:, None, None, None]
    squared = shifted_real * shifted_real + eigen_imag * eigen_imag
    ratio_real, ratio_imag = lax.optimization_barrier((shifted_real / squared, eigen_imag / squared))

    summed = spectrum
    correction = None
    for sweep_number in range(SWEEPS):
        if sweep_number > 0:
            x_halo = halos(correction, "space", 2)
            y_halo = column_halos(correction, "tm")
            summed = spectrum + neighbour_sum(correction, faces_y, x_halo, y_halo)
        correction = jnp.stack(
            [
                summed[0] * ratio_real + summed[1] * ratio_imag,
                summed[1] * ratio_real - summed[0] * ratio_imag,
            ]
        )

    back = []
    for step in range(groups):
        target = (position + step) % groups
        piece = jnp.einsum("lfk,fkxzy->lxzy", inverse[step], correction, precision=HIGHEST_PRECISION)
        if step > 0:
            piece = lax.ppermute(piece, "tm", ring_pairs(groups, step))
        back.append(piece)
    arrived = jnp.stack(back)
    update = jnp.concatenate(
        [lax.dynamic_index_in_dim(arrived, (position - j) % groups, axis=0, keepdims=False) for j in range(groups)],
        axis=3,
    )
    return age_field + update


def solution(mesh):
    in_specs = (
        P("tm", "space", None, None),
        P("tm", "space", None, None),
        P("space", None, None),
        P(),
        P(),
    )
    out_specs = P("tm", "space", None, None)
    return jax.shard_map(shards, mesh=mesh, in_specs=in_specs, out_specs=out_specs, check_vma=False)
```

```python
import math

import jax
import jax.numpy as jnp
from jax import lax
from jax.sharding import PartitionSpec as P

SWEEPS = 4


HIGHEST_PRECISION = lax.Precision.HIGHEST


def shift_pairs(count, step):
    return [(i, i + step) for i in range(count) if 0 <= i + step < count]


def halos(array, axis, dim, parts=1):
    count = lax.axis_size(axis)
    index = lax.axis_index(axis)
    length = array.shape[dim]
    last = lax.slice_in_dim(array, length - 1, length, axis=dim)
    first = lax.slice_in_dim(array, 0, 1, axis=dim)
    last = jnp.where(index == count - 1, jnp.zeros_like(last), last)
    first = jnp.where(index == 0, jnp.zeros_like(first), first)
    size = array.shape[0] // parts
    before = [lax.ppermute(last[i * size : (i + 1) * size], axis, ring_pairs(count, 1)) for i in range(parts)]
    after = [lax.ppermute(first[i * size : (i + 1) * size], axis, ring_pairs(count, -1)) for i in range(parts)]
    if parts == 1:
        return before[0], after[0]
    return jnp.concatenate(before, axis=0), jnp.concatenate(after, axis=0)


def column_halos(array, axis):
    count = lax.axis_size(axis)
    before = lax.ppermute(array[..., -1], axis, shift_pairs(count, 1))
    after = lax.ppermute(array[..., 0], axis, shift_pairs(count, -1))
    return before[..., None], after[..., None]


def ring_pairs(count, step):
    return [(i, (i + step) % count) for i in range(count)]


def shifted_pair(field, before, after, dim):
    length = field.shape[dim]
    low = jnp.concatenate([before, lax.slice_in_dim(field, 0, length - 1, axis=dim)], axis=dim)
    high = jnp.concatenate([lax.slice_in_dim(field, 1, length, axis=dim), after], axis=dim)
    return low, high


def zero_shifted(field, dim):
    edge_shape = list(field.shape)
    edge_shape[dim] = 1
    zero = jnp.zeros(edge_shape, field.dtype)
    return shifted_pair(field, zero, zero, dim)


def neighbour_sum(field, faces, x_halo, y_halo):
    nd = field.ndim
    xm, xp = shifted_pair(field, x_halo[0], x_halo[1], nd - 3)
    zm, zp = zero_shifted(field, nd - 2)
    if y_halo is None:
        ym, yp = zero_shifted(field, nd - 1)
    else:
        ym, yp = shifted_pair(field, y_halo[0], y_halo[1], nd - 1)
    moved = (xm, xp, zm, zp, ym, yp)
    result = faces[0] * moved[0]
    for one_face, one_moved in zip(faces[1:], moved[1:]):
        result = result + one_face * one_moved
    return result


def face_halos(conductivity, age_field):
    count = lax.axis_size("space")
    width = conductivity.shape[0]
    index = lax.axis_index("space")
    halves = []
    for field, dim in ((conductivity, 0), (age_field, 1)):
        last = lax.slice_in_dim(field, width - 1, width, axis=dim)
        first = lax.slice_in_dim(field, 0, 1, axis=dim)
        last = jnp.where(index == count - 1, jnp.zeros_like(last), last)
        first = jnp.where(index == 0, jnp.zeros_like(first), first)
        before = lax.ppermute(last, "space", ring_pairs(count, 1))
        after = lax.ppermute(first, "space", ring_pairs(count, -1))
        halves.append((before, after))
    return halves[0], halves[1]


def phase_tables(products, count):
    angles = 2.0 * math.pi / count * (products % count).astype(jnp.float32)
    return jnp.cos(angles), jnp.sin(angles)


def shards(age_field, source_term, conductivity, memory_weights, eigenvalues):
    groups = lax.axis_size("tm")
    position = lax.axis_index("tm")
    steps_local, width_x, depth_z, length_y = age_field.shape
    total_steps = steps_local * groups

    cond_halo, age_halo = face_halos(conductivity, age_field)

    c_low, c_high = shifted_pair(conductivity, cond_halo[0], cond_halo[1], 0)
    z_low, z_high = zero_shifted(conductivity, 1)
    y_low, y_high = zero_shifted(conductivity, 2)
    faces = tuple(0.5 * (conductivity + other) for other in (c_low, c_high, z_low, z_high, y_low, y_high))
    face_total = faces[0]
    for one_face in faces[1:]:
        face_total = face_total + one_face

    spread = neighbour_sum(age_field, faces, age_halo, None) - face_total * age_field
    partial = source_term + spread

    frequency = jnp.arange(total_steps, dtype=jnp.int32)
    lag = jnp.arange(total_steps, dtype=jnp.int32)
    cos_w, sin_w = phase_tables(frequency[:, None] * lag[None, :], total_steps)
    weight_real = jnp.sum(memory_weights[None, :] * cos_w, axis=1)[:, None, None]
    weight_imag = -jnp.sum(memory_weights[None, :] * sin_w, axis=1)[:, None, None]
    piece = jnp.arange(groups, dtype=jnp.int32)[None, :, None]
    local = jnp.arange(steps_local, dtype=jnp.int32)[None, None, :]
    step_of = ((position - piece) % groups) * steps_local + local
    cos_f, sin_f = phase_tables(frequency[:, None, None] * step_of, total_steps)
    forward = (
        (cos_f, -sin_f),
        (-(weight_real * cos_f + weight_imag * sin_f), weight_real * sin_f - weight_imag * cos_f),
    )
    step_to = ((position + piece[0, :, :, None]) % groups) * steps_local + local[0, :, :, None]
    cos_i, sin_i = phase_tables(step_to * frequency[None, None, :], total_steps)
    inverse = jnp.stack([cos_i, -sin_i], axis=2) / total_steps

    if depth_z % groups == 0:
        return z_split(partial, forward, inverse, faces, face_total, eigenvalues, age_field)
    stacked = jnp.stack([partial, age_field])
    return y_split(stacked, forward, inverse, faces, face_total, eigenvalues, age_field)


def z_split(partial, forward, inverse, faces, face_total, eigenvalues, age_field):
    groups = lax.axis_size("tm")
    position = lax.axis_index("tm")
    steps_local, width_x, depth_z, length_y = age_field.shape
    total_steps = steps_local * groups
    rows = depth_z // groups

    def ring(field):
        pieces = []
        for step in range(groups):
            target = (position + step) % groups
            piece = lax.dynamic_slice_in_dim(field, target * rows, rows, axis=2)
            if step > 0:
                piece = lax.ppermute(piece, "tm", ring_pairs(groups, step))
            pieces.append(piece)
        return pieces

    def transform(pieces, field):
        weights = jnp.stack([jnp.transpose(forward[field][part], (1, 2, 0)) for part in range(2)])
        total = None
        for step in range(groups):
            term = jnp.sum(
                weights[:, step][:, :, None, None, :, None] * pieces[step][None, :, :, :, None, :], axis=1
            )
            total = term if total is None else total + term
        return total

    age_pieces, partial = lax.optimization_barrier((ring(age_field), partial))
    sent = ring(partial)
    spectrum = transform(sent, 0) + transform(age_pieces, 1)

    start = position * rows
    faces_z = tuple(lax.dynamic_slice_in_dim(one_face, start, rows, axis=1)[:, :, None, :] for one_face in faces)
    total_z = lax.dynamic_slice_in_dim(face_total, start, rows, axis=1)[:, :, None, :]
    shifted_real = eigenvalues[0][None, None, :, None] + total_z
    eigen_imag = eigenvalues[1][None, None, :, None]
    squared = shifted_real * shifted_real + eigen_imag * eigen_imag
    ratio_real, ratio_imag = lax.optimization_barrier((shifted_real / squared, eigen_imag / squared))

    summed = spectrum
    correction = None
    for sweep_number in range(SWEEPS):
        if sweep_number > 0:
            x_low, x_high = halos(correction, "space", 1)
            z_low, z_high = halos(correction, "tm", 2)
            xm, xp = shifted_pair(correction, x_low, x_high, 1)
            zm, zp = shifted_pair(correction, z_low, z_high, 2)
            ym, yp = zero_shifted(correction, 4)
            moved = (xm, xp, zm, zp, ym, yp)
            total = faces_z[0] * moved[0]
            for one_face, one_moved in zip(faces_z[1:], moved[1:]):
                total = total + one_face * one_moved
            summed = spectrum + total
        correction = jnp.stack(
            [
                summed[0] * ratio_real + summed[1] * ratio_imag,
                summed[1] * ratio_real - summed[0] * ratio_imag,
            ]
        )

    back = []
    for step in range(groups):
        target = (position + step) % groups
        piece = jnp.einsum("lfk,fxzky->lxzy", inverse[step], correction, precision=HIGHEST_PRECISION)
        if step > 0:
            piece = lax.ppermute(piece, "tm", ring_pairs(groups, step))
        back.append(piece)
    arrived = jnp.stack(back)
    update = jnp.concatenate(
        [lax.dynamic_index_in_dim(arrived, (position - j) % groups, axis=0, keepdims=False) for j in range(groups)],
        axis=2,
    )
    return age_field + update


def y_split(stacked, forward, inverse, faces, face_total, eigenvalues, age_field):
    groups = lax.axis_size("tm")
    position = lax.axis_index("tm")
    _, steps_local, width_x, depth_z, length_y = stacked.shape
    total_steps = steps_local * groups
    chunk = length_y // groups

    pieces = []
    for step in range(groups):
        target = (position + step) % groups
        piece = lax.dynamic_slice_in_dim(stacked, target * chunk, chunk, axis=4)
        if step > 0:
            piece = lax.ppermute(piece, "tm", ring_pairs(groups, step))
        pieces.append(piece)

    halves = []
    for part in range(2):
        total = None
        for step in range(groups):
            for field in range(2):
                for local in range(steps_local):
                    weight = forward[field][part][:, step, local][:, None, None, None]
                    term = weight * pieces[step][field, local][None]
                    total = term if total is None else total + term
        halves.append(total)
    spectrum = jnp.stack(halves)


    start = position * chunk
    faces_y = tuple(lax.dynamic_slice_in_dim(one_face, start, chunk, axis=2) for one_face in faces)
    total_y = lax.dynamic_slice_in_dim(face_total, start, chunk, axis=2)
    shifted_real = eigenvalues[0][:, None, None, None] + total_y[None]
    eigen_imag = eigenvalues[1][:, None, None, None]
    squared = shifted_real * shifted_real + eigen_imag * eigen_imag
    ratio_real, ratio_imag = lax.optimization_barrier((shifted_real / squared, eigen_imag / squared))

    summed = spectrum
    correction = None
    for sweep_number in range(SWEEPS):
        if sweep_number > 0:
            x_halo = halos(correction, "space", 2)
            y_halo = column_halos(correction, "tm")
            summed = spectrum + neighbour_sum(correction, faces_y, x_halo, y_halo)
        correction = jnp.stack(
            [
                summed[0] * ratio_real + summed[1] * ratio_imag,
                summed[1] * ratio_real - summed[0] * ratio_imag,
            ]
        )

    back = []
    for step in range(groups):
        target = (position + step) % groups
        piece = jnp.einsum("lfk,fkxzy->lxzy", inverse[step], correction, precision=HIGHEST_PRECISION)
        if step > 0:
            piece = lax.ppermute(piece, "tm", ring_pairs(groups, step))
        back.append(piece)
    arrived = jnp.stack(back)
    update = jnp.concatenate(
        [lax.dynamic_index_in_dim(arrived, (position - j) % groups, axis=0, keepdims=False) for j in range(groups)],
        axis=3,
    )
    return age_field + update


def solution(mesh):
    in_specs = (
        P("tm", "space", None, None),
        P("tm", "space", None, None),
        P("space", None, None),
        P(),
        P(),
    )
    out_specs = P("tm", "space", None, None)
    return jax.shard_map(shards, mesh=mesh, in_specs=in_specs, out_specs=out_specs, check_vma=False)
```

```python
import math

import jax
import jax.numpy as jnp
from jax import lax
from jax.sharding import PartitionSpec as P

SWEEPS = 4


HIGHEST_PRECISION = lax.Precision.HIGHEST


def shift_pairs(count, step):
    return [(i, i + step) for i in range(count) if 0 <= i + step < count]


def halos(array, axis, dim, parts=1):
    count = lax.axis_size(axis)
    index = lax.axis_index(axis)
    length = array.shape[dim]
    last = lax.slice_in_dim(array, length - 1, length, axis=dim)
    first = lax.slice_in_dim(array, 0, 1, axis=dim)
    last = jnp.where(index == count - 1, jnp.zeros_like(last), last)
    first = jnp.where(index == 0, jnp.zeros_like(first), first)
    size = array.shape[0] // parts
    before = [lax.ppermute(last[i * size : (i + 1) * size], axis, ring_pairs(count, 1)) for i in range(parts)]
    after = [lax.ppermute(first[i * size : (i + 1) * size], axis, ring_pairs(count, -1)) for i in range(parts)]
    if parts == 1:
        return before[0], after[0]
    return jnp.concatenate(before, axis=0), jnp.concatenate(after, axis=0)


def column_halos(array, axis):
    count = lax.axis_size(axis)
    before = lax.ppermute(array[..., -1], axis, shift_pairs(count, 1))
    after = lax.ppermute(array[..., 0], axis, shift_pairs(count, -1))
    return before[..., None], after[..., None]


def ring_pairs(count, step):
    return [(i, (i + step) % count) for i in range(count)]


def shifted_pair(field, before, after, dim):
    length = field.shape[dim]
    low = jnp.concatenate([before, lax.slice_in_dim(field, 0, length - 1, axis=dim)], axis=dim)
    high = jnp.concatenate([lax.slice_in_dim(field, 1, length, axis=dim), after], axis=dim)
    return low, high


def zero_shifted(field, dim):
    edge_shape = list(field.shape)
    edge_shape[dim] = 1
    zero = jnp.zeros(edge_shape, field.dtype)
    return shifted_pair(field, zero, zero, dim)


def neighbour_sum(field, faces, x_halo, y_halo):
    nd = field.ndim
    xm, xp = shifted_pair(field, x_halo[0], x_halo[1], nd - 3)
    zm, zp = zero_shifted(field, nd - 2)
    if y_halo is None:
        ym, yp = zero_shifted(field, nd - 1)
    else:
        ym, yp = shifted_pair(field, y_halo[0], y_halo[1], nd - 1)
    moved = (xm, xp, zm, zp, ym, yp)
    result = faces[0] * moved[0]
    for one_face, one_moved in zip(faces[1:], moved[1:]):
        result = result + one_face * one_moved
    return result


def face_halos(conductivity, age_field):
    count = lax.axis_size("space")
    width = conductivity.shape[0]
    last = jnp.concatenate([conductivity[width - 1 :][None], age_field[:, width - 1 :]], axis=0)
    first = jnp.concatenate([conductivity[:1][None], age_field[:, :1]], axis=0)
    index = lax.axis_index("space")
    last = jnp.where(index == count - 1, jnp.zeros_like(last), last)
    first = jnp.where(index == 0, jnp.zeros_like(first), first)
    before = lax.ppermute(last, "space", ring_pairs(count, 1))
    after = lax.ppermute(first, "space", ring_pairs(count, -1))
    return (before[0], after[0]), (before[1:], after[1:])


def phase_tables(products, count):
    angles = 2.0 * math.pi / count * (products % count).astype(jnp.float32)
    return jnp.cos(angles), jnp.sin(angles)


def shards(age_field, source_term, conductivity, memory_weights, eigenvalues):
    groups = lax.axis_size("tm")
    position = lax.axis_index("tm")
    steps_local, width_x, depth_z, length_y = age_field.shape
    total_steps = steps_local * groups

    cond_halo, age_halo = face_halos(conductivity, age_field)

    c_low, c_high = shifted_pair(conductivity, cond_halo[0], cond_halo[1], 0)
    z_low, z_high = zero_shifted(conductivity, 1)
    y_low, y_high = zero_shifted(conductivity, 2)
    faces = tuple(0.5 * (conductivity + other) for other in (c_low, c_high, z_low, z_high, y_low, y_high))
    face_total = faces[0]
    for one_face in faces[1:]:
        face_total = face_total + one_face

    spread = neighbour_sum(age_field, faces, age_halo, None) - face_total * age_field
    partial = source_term + spread
    table_at, memory_weights, _ = lax.optimization_barrier((position, memory_weights, partial))

    frequency = jnp.arange(total_steps, dtype=jnp.int32)
    lag = jnp.arange(total_steps, dtype=jnp.int32)
    cos_w, sin_w = phase_tables(frequency[:, None] * lag[None, :], total_steps)
    weight_real = jnp.sum(memory_weights[None, :] * cos_w, axis=1)[:, None, None]
    weight_imag = -jnp.sum(memory_weights[None, :] * sin_w, axis=1)[:, None, None]
    piece = jnp.arange(groups, dtype=jnp.int32)[None, :, None]
    local = jnp.arange(steps_local, dtype=jnp.int32)[None, None, :]
    step_of = ((table_at - piece) % groups) * steps_local + local
    cos_f, sin_f = phase_tables(frequency[:, None, None] * step_of, total_steps)
    forward = (
        (cos_f, -sin_f),
        (-(weight_real * cos_f + weight_imag * sin_f), weight_real * sin_f - weight_imag * cos_f),
    )
    step_to = ((table_at + piece[0, :, :, None]) % groups) * steps_local + local[0, :, :, None]
    cos_i, sin_i = phase_tables(step_to * frequency[None, None, :], total_steps)
    inverse = jnp.stack([cos_i, -sin_i], axis=2) / total_steps

    if depth_z % groups == 0:
        return z_split(partial, forward, inverse, faces, face_total, eigenvalues, age_field)
    stacked = jnp.stack([partial, age_field])
    return y_split(stacked, forward, inverse, faces, face_total, eigenvalues, age_field)


def z_split(partial, forward, inverse, faces, face_total, eigenvalues, age_field):
    groups = lax.axis_size("tm")
    position = lax.axis_index("tm")
    steps_local, width_x, depth_z, length_y = age_field.shape
    total_steps = steps_local * groups
    rows = depth_z // groups

    def ring(field):
        pieces = []
        for step in range(groups):
            target = (position + step) % groups
            piece = lax.dynamic_slice_in_dim(field, target * rows, rows, axis=2)
            if step > 0:
                piece = lax.ppermute(piece, "tm", ring_pairs(groups, step))
            pieces.append(piece)
        return pieces

    def transform(pieces, field):
        weights = jnp.stack([jnp.transpose(forward[field][part], (1, 2, 0)) for part in range(2)])
        total = None
        for step in range(groups):
            term = jnp.sum(
                weights[:, step][:, :, None, None, :, None] * pieces[step][None, :, :, :, None, :], axis=1
            )
            total = term if total is None else total + term
        return total

    age_pieces, partial = lax.optimization_barrier((ring(age_field), partial))
    sent = ring(partial)
    spectrum = transform(sent, 0) + transform(age_pieces, 1)

    start = position * rows
    faces_z = tuple(lax.dynamic_slice_in_dim(one_face, start, rows, axis=1)[:, :, None, :] for one_face in faces)
    total_z = lax.dynamic_slice_in_dim(face_total, start, rows, axis=1)[:, :, None, :]
    shifted_real = eigenvalues[0][None, None, :, None] + total_z
    eigen_imag = eigenvalues[1][None, None, :, None]
    squared = shifted_real * shifted_real + eigen_imag * eigen_imag
    ratio_real, ratio_imag = lax.optimization_barrier((shifted_real / squared, eigen_imag / squared))

    summed = spectrum
    correction = None
    for sweep_number in range(SWEEPS):
        if sweep_number > 0:
            x_low, x_high = halos(correction, "space", 1)
            z_low, z_high = halos(correction, "tm", 2)
            xm, xp = shifted_pair(correction, x_low, x_high, 1)
            zm, zp = shifted_pair(correction, z_low, z_high, 2)
            ym, yp = zero_shifted(correction, 4)
            moved = (xm, xp, zm, zp, ym, yp)
            total = faces_z[0] * moved[0]
            for one_face, one_moved in zip(faces_z[1:], moved[1:]):
                total = total + one_face * one_moved
            summed = spectrum + total
        correction = jnp.stack(
            [
                summed[0] * ratio_real + summed[1] * ratio_imag,
                summed[1] * ratio_real - summed[0] * ratio_imag,
            ]
        )

    back = []
    for step in range(groups):
        target = (position + step) % groups
        piece = jnp.einsum("lfk,fxzky->lxzy", inverse[step], correction, precision=HIGHEST_PRECISION)
        if step > 0:
            piece = lax.ppermute(piece, "tm", ring_pairs(groups, step))
        back.append(piece)
    arrived = jnp.stack(back)
    update = jnp.concatenate(
        [lax.dynamic_index_in_dim(arrived, (position - j) % groups, axis=0, keepdims=False) for j in range(groups)],
        axis=2,
    )
    return age_field + update


def y_split(stacked, forward, inverse, faces, face_total, eigenvalues, age_field):
    groups = lax.axis_size("tm")
    position = lax.axis_index("tm")
    _, steps_local, width_x, depth_z, length_y = stacked.shape
    total_steps = steps_local * groups
    chunk = length_y // groups

    pieces = []
    for step in range(groups):
        target = (position + step) % groups
        piece = lax.dynamic_slice_in_dim(stacked, target * chunk, chunk, axis=4)
        if step > 0:
            piece = lax.ppermute(piece, "tm", ring_pairs(groups, step))
        pieces.append(piece)

    halves = []
    for part in range(2):
        total = None
        for step in range(groups):
            for field in range(2):
                for local in range(steps_local):
                    weight = forward[field][part][:, step, local][:, None, None, None]
                    term = weight * pieces[step][field, local][None]
                    total = term if total is None else total + term
        halves.append(total)
    spectrum = jnp.stack(halves)


    start = position * chunk
    faces_y = tuple(lax.dynamic_slice_in_dim(one_face, start, chunk, axis=2) for one_face in faces)
    total_y = lax.dynamic_slice_in_dim(face_total, start, chunk, axis=2)
    shifted_real = eigenvalues[0][:, None, None, None] + total_y[None]
    eigen_imag = eigenvalues[1][:, None, None, None]
    squared = shifted_real * shifted_real + eigen_imag * eigen_imag
    ratio_real, ratio_imag = lax.optimization_barrier((shifted_real / squared, eigen_imag / squared))

    summed = spectrum
    correction = None
    for sweep_number in range(SWEEPS):
        if sweep_number > 0:
            x_halo = halos(correction, "space", 2)
            y_halo = column_halos(correction, "tm")
            summed = spectrum + neighbour_sum(correction, faces_y, x_halo, y_halo)
        correction = jnp.stack(
            [
                summed[0] * ratio_real + summed[1] * ratio_imag,
                summed[1] * ratio_real - summed[0] * ratio_imag,
            ]
        )

    back = []
    for step in range(groups):
        target = (position + step) % groups
        piece = jnp.einsum("lfk,fkxzy->lxzy", inverse[step], correction, precision=HIGHEST_PRECISION)
        if step > 0:
            piece = lax.ppermute(piece, "tm", ring_pairs(groups, step))
        back.append(piece)
    arrived = jnp.stack(back)
    update = jnp.concatenate(
        [lax.dynamic_index_in_dim(arrived, (position - j) % groups, axis=0, keepdims=False) for j in range(groups)],
        axis=3,
    )
    return age_field + update


def solution(mesh):
    in_specs = (
        P("tm", "space", None, None),
        P("tm", "space", None, None),
        P("space", None, None),
        P(),
        P(),
    )
    out_specs = P("tm", "space", None, None)
    return jax.shard_map(shards, mesh=mesh, in_specs=in_specs, out_specs=out_specs, check_vma=False)
```

```python
import math

import jax
import jax.numpy as jnp
from jax import lax
from jax.sharding import PartitionSpec as P

SWEEPS = 4


HIGHEST_PRECISION = lax.Precision.HIGHEST


def shift_pairs(count, step):
    return [(i, i + step) for i in range(count) if 0 <= i + step < count]


def halos(array, axis, dim, parts=1):
    count = lax.axis_size(axis)
    index = lax.axis_index(axis)
    length = array.shape[dim]
    last = lax.slice_in_dim(array, length - 1, length, axis=dim)
    first = lax.slice_in_dim(array, 0, 1, axis=dim)
    last = jnp.where(index == count - 1, jnp.zeros_like(last), last)
    first = jnp.where(index == 0, jnp.zeros_like(first), first)
    size = array.shape[0] // parts
    before = [lax.ppermute(last[i * size : (i + 1) * size], axis, ring_pairs(count, 1)) for i in range(parts)]
    after = [lax.ppermute(first[i * size : (i + 1) * size], axis, ring_pairs(count, -1)) for i in range(parts)]
    if parts == 1:
        return before[0], after[0]
    return jnp.concatenate(before, axis=0), jnp.concatenate(after, axis=0)


def column_halos(array, axis):
    count = lax.axis_size(axis)
    before = lax.ppermute(array[..., -1], axis, shift_pairs(count, 1))
    after = lax.ppermute(array[..., 0], axis, shift_pairs(count, -1))
    return before[..., None], after[..., None]


def ring_pairs(count, step):
    return [(i, (i + step) % count) for i in range(count)]


def shifted_pair(field, before, after, dim):
    length = field.shape[dim]
    low = jnp.concatenate([before, lax.slice_in_dim(field, 0, length - 1, axis=dim)], axis=dim)
    high = jnp.concatenate([lax.slice_in_dim(field, 1, length, axis=dim), after], axis=dim)
    return low, high


def zero_shifted(field, dim):
    edge_shape = list(field.shape)
    edge_shape[dim] = 1
    zero = jnp.zeros(edge_shape, field.dtype)
    return shifted_pair(field, zero, zero, dim)


def neighbour_sum(field, faces, x_halo, y_halo):
    nd = field.ndim
    xm, xp = shifted_pair(field, x_halo[0], x_halo[1], nd - 3)
    zm, zp = zero_shifted(field, nd - 2)
    if y_halo is None:
        ym, yp = zero_shifted(field, nd - 1)
    else:
        ym, yp = shifted_pair(field, y_halo[0], y_halo[1], nd - 1)
    moved = (xm, xp, zm, zp, ym, yp)
    result = faces[0] * moved[0]
    for one_face, one_moved in zip(faces[1:], moved[1:]):
        result = result + one_face * one_moved
    return result


def face_halos(conductivity, age_field):
    count = lax.axis_size("space")
    width = conductivity.shape[0]
    last = jnp.concatenate([conductivity[width - 1 :][None], age_field[:, width - 1 :]], axis=0)
    first = jnp.concatenate([conductivity[:1][None], age_field[:, :1]], axis=0)
    index = lax.axis_index("space")
    last = jnp.where(index == count - 1, jnp.zeros_like(last), last)
    first = jnp.where(index == 0, jnp.zeros_like(first), first)
    before = lax.ppermute(last, "space", ring_pairs(count, 1))
    after = lax.ppermute(first, "space", ring_pairs(count, -1))
    return (before[0], after[0]), (before[1:], after[1:])


def phase_tables(products, count):
    angles = 2.0 * math.pi / count * (products % count).astype(jnp.float32)
    return jnp.cos(angles), jnp.sin(angles)


def shards(age_field, source_term, conductivity, memory_weights, eigenvalues):
    groups = lax.axis_size("tm")
    position = lax.axis_index("tm")
    steps_local, width_x, depth_z, length_y = age_field.shape
    total_steps = steps_local * groups

    cond_halo, age_halo = face_halos(conductivity, age_field)

    c_low, c_high = shifted_pair(conductivity, cond_halo[0], cond_halo[1], 0)
    z_low, z_high = zero_shifted(conductivity, 1)
    y_low, y_high = zero_shifted(conductivity, 2)
    faces = tuple(0.5 * (conductivity + other) for other in (c_low, c_high, z_low, z_high, y_low, y_high))
    face_total = faces[0]
    for one_face in faces[1:]:
        face_total = face_total + one_face

    spread = neighbour_sum(age_field, faces, age_halo, None) - face_total * age_field
    partial = source_term + spread
    table_at, memory_weights, _ = lax.optimization_barrier((position, memory_weights, partial))

    frequency = jnp.arange(total_steps, dtype=jnp.int32)
    lag = jnp.arange(total_steps, dtype=jnp.int32)
    cos_w, sin_w = phase_tables(frequency[:, None] * lag[None, :], total_steps)
    weight_real = jnp.sum(memory_weights[None, :] * cos_w, axis=1)[:, None, None]
    weight_imag = -jnp.sum(memory_weights[None, :] * sin_w, axis=1)[:, None, None]
    piece = jnp.arange(groups, dtype=jnp.int32)[None, :, None]
    local = jnp.arange(steps_local, dtype=jnp.int32)[None, None, :]
    step_of = ((table_at - piece) % groups) * steps_local + local
    cos_f, sin_f = phase_tables(frequency[:, None, None] * step_of, total_steps)
    forward = (
        (cos_f, -sin_f),
        (-(weight_real * cos_f + weight_imag * sin_f), weight_real * sin_f - weight_imag * cos_f),
    )
    step_to = ((table_at + piece[0, :, :, None]) % groups) * steps_local + local[0, :, :, None]
    cos_i, sin_i = phase_tables(step_to * frequency[None, None, :], total_steps)
    inverse = jnp.stack([cos_i, -sin_i], axis=2) / total_steps

    if depth_z % groups == 0:
        return z_split(partial, forward, inverse, faces, face_total, eigenvalues, age_field)
    stacked = jnp.stack([partial, age_field])
    return y_split(stacked, forward, inverse, faces, face_total, eigenvalues, age_field)


def z_split(partial, forward, inverse, faces, face_total, eigenvalues, age_field):
    groups = lax.axis_size("tm")
    position = lax.axis_index("tm")
    steps_local, width_x, depth_z, length_y = age_field.shape
    total_steps = steps_local * groups
    rows = depth_z // groups

    def ring(field):
        pieces = []
        for step in range(groups):
            target = (position + step) % groups
            piece = lax.dynamic_slice_in_dim(field, target * rows, rows, axis=2)
            if step > 0:
                piece = lax.ppermute(piece, "tm", ring_pairs(groups, step))
            pieces.append(piece)
        return pieces

    def transform(pieces, field):
        weights = jnp.stack([jnp.transpose(forward[field][part], (1, 2, 0)) for part in range(2)])
        total = None
        for step in range(groups):
            term = jnp.sum(
                weights[:, step][:, :, None, None, :, None] * pieces[step][None, :, :, :, None, :], axis=1
            )
            total = term if total is None else total + term
        return total

    age_pieces, partial = lax.optimization_barrier((ring(age_field), partial))
    sent = ring(partial)
    spectrum = transform(sent, 0) + transform(age_pieces, 1)

    start = position * rows
    faces_z = tuple(lax.dynamic_slice_in_dim(one_face, start, rows, axis=1)[:, :, None, :] for one_face in faces)
    total_z = lax.dynamic_slice_in_dim(face_total, start, rows, axis=1)[:, :, None, :]
    shifted_real = eigenvalues[0][None, None, :, None] + total_z
    eigen_imag = eigenvalues[1][None, None, :, None]
    squared = shifted_real * shifted_real + eigen_imag * eigen_imag
    ratio_real, ratio_imag = lax.optimization_barrier((shifted_real / squared, eigen_imag / squared))

    summed = spectrum
    correction = None
    for sweep_number in range(SWEEPS):
        if sweep_number > 0:
            x_low, x_high = halos(correction, "space", 1)
            z_low, z_high = halos(correction, "tm", 2)
            xm, xp = shifted_pair(correction, x_low, x_high, 1)
            zm, zp = shifted_pair(correction, z_low, z_high, 2)
            ym, yp = zero_shifted(correction, 4)
            moved = (xm, xp, zm, zp, ym, yp)
            total = faces_z[0] * moved[0]
            for one_face, one_moved in zip(faces_z[1:], moved[1:]):
                total = total + one_face * one_moved
            summed = spectrum + total
        correction = jnp.stack(
            [
                summed[0] * ratio_real + summed[1] * ratio_imag,
                summed[1] * ratio_real - summed[0] * ratio_imag,
            ]
        )

    back = []
    for step in range(groups):
        target = (position + step) % groups
        weights = inverse[step][:, :, None, None, :, None]
        piece = jnp.sum(weights * correction[None], axis=(1, 4))
        if step > 0:
            piece = lax.ppermute(piece, "tm", ring_pairs(groups, step))
        back.append(piece)
    arrived = jnp.stack(back)
    update = jnp.concatenate(
        [lax.dynamic_index_in_dim(arrived, (position - j) % groups, axis=0, keepdims=False) for j in range(groups)],
        axis=2,
    )
    return age_field + update


def y_split(stacked, forward, inverse, faces, face_total, eigenvalues, age_field):
    groups = lax.axis_size("tm")
    position = lax.axis_index("tm")
    _, steps_local, width_x, depth_z, length_y = stacked.shape
    total_steps = steps_local * groups
    chunk = length_y // groups

    pieces = []
    for step in range(groups):
        target = (position + step) % groups
        piece = lax.dynamic_slice_in_dim(stacked, target * chunk, chunk, axis=4)
        if step > 0:
            piece = lax.ppermute(piece, "tm", ring_pairs(groups, step))
        pieces.append(piece)

    halves = []
    for part in range(2):
        total = None
        for step in range(groups):
            for field in range(2):
                for local in range(steps_local):
                    weight = forward[field][part][:, step, local][:, None, None, None]
                    term = weight * pieces[step][field, local][None]
                    total = term if total is None else total + term
        halves.append(total)
    spectrum = jnp.stack(halves)


    start = position * chunk
    faces_y = tuple(lax.dynamic_slice_in_dim(one_face, start, chunk, axis=2) for one_face in faces)
    total_y = lax.dynamic_slice_in_dim(face_total, start, chunk, axis=2)
    shifted_real = eigenvalues[0][:, None, None, None] + total_y[None]
    eigen_imag = eigenvalues[1][:, None, None, None]
    squared = shifted_real * shifted_real + eigen_imag * eigen_imag
    ratio_real, ratio_imag = lax.optimization_barrier((shifted_real / squared, eigen_imag / squared))

    summed = spectrum
    correction = None
    for sweep_number in range(SWEEPS):
        if sweep_number > 0:
            x_halo = halos(correction, "space", 2)
            y_halo = column_halos(correction, "tm")
            summed = spectrum + neighbour_sum(correction, faces_y, x_halo, y_halo)
        correction = jnp.stack(
            [
                summed[0] * ratio_real + summed[1] * ratio_imag,
                summed[1] * ratio_real - summed[0] * ratio_imag,
            ]
        )

    back = []
    for step in range(groups):
        target = (position + step) % groups
        piece = jnp.einsum("lfk,fkxzy->lxzy", inverse[step], correction, precision=HIGHEST_PRECISION)
        if step > 0:
            piece = lax.ppermute(piece, "tm", ring_pairs(groups, step))
        back.append(piece)
    arrived = jnp.stack(back)
    update = jnp.concatenate(
        [lax.dynamic_index_in_dim(arrived, (position - j) % groups, axis=0, keepdims=False) for j in range(groups)],
        axis=3,
    )
    return age_field + update


def solution(mesh):
    in_specs = (
        P("tm", "space", None, None),
        P("tm", "space", None, None),
        P("space", None, None),
        P(),
        P(),
    )
    out_specs = P("tm", "space", None, None)
    return jax.shard_map(shards, mesh=mesh, in_specs=in_specs, out_specs=out_specs, check_vma=False)
```

```python
import math

import jax
import jax.numpy as jnp
from jax import lax
from jax.experimental import pallas as pl
from jax.experimental.pallas import tpu as pltpu
from jax.sharding import PartitionSpec as P

SWEEPS = 4


HIGHEST_PRECISION = lax.Precision.HIGHEST


def shift_pairs(count, step):
    return [(i, i + step) for i in range(count) if 0 <= i + step < count]


def halos(array, axis, dim, parts=1):
    count = lax.axis_size(axis)
    index = lax.axis_index(axis)
    length = array.shape[dim]
    last = lax.slice_in_dim(array, length - 1, length, axis=dim)
    first = lax.slice_in_dim(array, 0, 1, axis=dim)
    last = jnp.where(index == count - 1, jnp.zeros_like(last), last)
    first = jnp.where(index == 0, jnp.zeros_like(first), first)
    size = array.shape[0] // parts
    before = [lax.ppermute(last[i * size : (i + 1) * size], axis, ring_pairs(count, 1)) for i in range(parts)]
    after = [lax.ppermute(first[i * size : (i + 1) * size], axis, ring_pairs(count, -1)) for i in range(parts)]
    if parts == 1:
        return before[0], after[0]
    return jnp.concatenate(before, axis=0), jnp.concatenate(after, axis=0)


def column_halos(array, axis):
    count = lax.axis_size(axis)
    before = lax.ppermute(array[..., -1], axis, shift_pairs(count, 1))
    after = lax.ppermute(array[..., 0], axis, shift_pairs(count, -1))
    return before[..., None], after[..., None]


def ring_pairs(count, step):
    return [(i, (i + step) % count) for i in range(count)]


def shifted_pair(field, before, after, dim):
    length = field.shape[dim]
    low = jnp.concatenate([before, lax.slice_in_dim(field, 0, length - 1, axis=dim)], axis=dim)
    high = jnp.concatenate([lax.slice_in_dim(field, 1, length, axis=dim), after], axis=dim)
    return low, high


def zero_shifted(field, dim):
    edge_shape = list(field.shape)
    edge_shape[dim] = 1
    zero = jnp.zeros(edge_shape, field.dtype)
    return shifted_pair(field, zero, zero, dim)


def neighbour_sum(field, faces, x_halo, y_halo):
    nd = field.ndim
    xm, xp = shifted_pair(field, x_halo[0], x_halo[1], nd - 3)
    zm, zp = zero_shifted(field, nd - 2)
    if y_halo is None:
        ym, yp = zero_shifted(field, nd - 1)
    else:
        ym, yp = shifted_pair(field, y_halo[0], y_halo[1], nd - 1)
    moved = (xm, xp, zm, zp, ym, yp)
    result = faces[0] * moved[0]
    for one_face, one_moved in zip(faces[1:], moved[1:]):
        result = result + one_face * one_moved
    return result


def face_halos(conductivity, age_field):
    count = lax.axis_size("space")
    width = conductivity.shape[0]
    last = jnp.concatenate([conductivity[width - 1 :][None], age_field[:, width - 1 :]], axis=0)
    first = jnp.concatenate([conductivity[:1][None], age_field[:, :1]], axis=0)
    index = lax.axis_index("space")
    last = jnp.where(index == count - 1, jnp.zeros_like(last), last)
    first = jnp.where(index == 0, jnp.zeros_like(first), first)
    before = lax.ppermute(last, "space", ring_pairs(count, 1))
    after = lax.ppermute(first, "space", ring_pairs(count, -1))
    return before, after


def faces_of(conductivity, cond_halo):
    c_low, c_high = shifted_pair(conductivity, cond_halo[0], cond_halo[1], 0)
    z_low, z_high = zero_shifted(conductivity, 1)
    y_low, y_high = zero_shifted(conductivity, 2)
    faces = tuple(0.5 * (conductivity + other) for other in (c_low, c_high, z_low, z_high, y_low, y_high))
    face_total = faces[0]
    for one_face in faces[1:]:
        face_total = face_total + one_face
    return faces, face_total


def spread_kernel(age_ref, source_ref, cond_ref, before_ref, after_ref, out_ref):
    steps, width = age_ref.shape[0], age_ref.shape[1]
    rows, lanes = cond_ref.shape[1], cond_ref.shape[2]
    shape = (rows, lanes)
    moves = []
    for axis, count in ((0, rows), (1, lanes)):
        index = lax.broadcasted_iota(jnp.int32, shape, axis)
        for shift in (1, count - 1):
            moved = pltpu.roll(index, shift, axis)
            moves.append((axis, shift, jnp.abs(moved - index) == 1))

    def neighbours(value):
        return [jnp.where(ok, pltpu.roll(value, shift, axis), 0.0) for axis, shift, ok in moves]

    for x in range(width):
        centre = cond_ref[x]
        low = cond_ref[x - 1] if x > 0 else before_ref[0, 0]
        high = cond_ref[x + 1] if x < width - 1 else after_ref[0, 0]
        faces = [0.5 * (centre + other) for other in [low, high] + neighbours(centre)]
        face_total = faces[0]
        for one_face in faces[1:]:
            face_total = face_total + one_face
        for step in range(steps):
            value = age_ref[step, x]
            low = age_ref[step, x - 1] if x > 0 else before_ref[1 + step, 0]
            high = age_ref[step, x + 1] if x < width - 1 else after_ref[1 + step, 0]
            moved = [low, high] + neighbours(value)
            total = faces[0] * moved[0]
            for one_face, one_moved in zip(faces[1:], moved[1:]):
                total = total + one_face * one_moved
            out_ref[step, x] = source_ref[step, x] + (total - face_total * value)


def phase_tables(products, count):
    angles = 2.0 * math.pi / count * (products % count).astype(jnp.float32)
    return jnp.cos(angles), jnp.sin(angles)


def shards(age_field, source_term, conductivity, memory_weights, eigenvalues):
    groups = lax.axis_size("tm")
    position = lax.axis_index("tm")
    steps_local, width_x, depth_z, length_y = age_field.shape
    total_steps = steps_local * groups

    before, after = face_halos(conductivity, age_field)
    partial = pl.pallas_call(spread_kernel, out_shape=jax.ShapeDtypeStruct(age_field.shape, jnp.float32))(
        age_field, source_term, conductivity, before, after
    )
    table_at, memory_weights, before, after, _ = lax.optimization_barrier(
        (position, memory_weights, before, after, partial)
    )
    faces, face_total = faces_of(conductivity, (before[0], after[0]))

    frequency = jnp.arange(total_steps, dtype=jnp.int32)
    lag = jnp.arange(total_steps, dtype=jnp.int32)
    cos_w, sin_w = phase_tables(frequency[:, None] * lag[None, :], total_steps)
    weight_real = jnp.sum(memory_weights[None, :] * cos_w, axis=1)[:, None, None]
    weight_imag = -jnp.sum(memory_weights[None, :] * sin_w, axis=1)[:, None, None]
    piece = jnp.arange(groups, dtype=jnp.int32)[None, :, None]
    local = jnp.arange(steps_local, dtype=jnp.int32)[None, None, :]
    step_of = ((table_at - piece) % groups) * steps_local + local
    cos_f, sin_f = phase_tables(frequency[:, None, None] * step_of, total_steps)
    forward = (
        (cos_f, -sin_f),
        (-(weight_real * cos_f + weight_imag * sin_f), weight_real * sin_f - weight_imag * cos_f),
    )
    step_to = ((table_at + piece[0, :, :, None]) % groups) * steps_local + local[0, :, :, None]
    cos_i, sin_i = phase_tables(step_to * frequency[None, None, :], total_steps)
    inverse = jnp.stack([cos_i, -sin_i], axis=2) / total_steps

    if depth_z % groups == 0:
        return z_split(partial, forward, inverse, faces, face_total, eigenvalues, age_field)
    stacked = jnp.stack([partial, age_field])
    return y_split(stacked, forward, inverse, faces, face_total, eigenvalues, age_field)


def z_split(partial, forward, inverse, faces, face_total, eigenvalues, age_field):
    groups = lax.axis_size("tm")
    position = lax.axis_index("tm")
    steps_local, width_x, depth_z, length_y = age_field.shape
    total_steps = steps_local * groups
    rows = depth_z // groups

    def ring(field):
        pieces = []
        for step in range(groups):
            target = (position + step) % groups
            piece = lax.dynamic_slice_in_dim(field, target * rows, rows, axis=2)
            if step > 0:
                piece = lax.ppermute(piece, "tm", ring_pairs(groups, step))
            pieces.append(piece)
        return pieces

    def transform(pieces, field):
        weights = jnp.stack([jnp.transpose(forward[field][part], (1, 2, 0)) for part in range(2)])
        total = None
        for step in range(groups):
            term = jnp.sum(
                weights[:, step][:, :, None, None, :, None] * pieces[step][None, :, :, :, None, :], axis=1
            )
            total = term if total is None else total + term
        return total

    age_pieces, partial = lax.optimization_barrier((ring(age_field), partial))
    sent = ring(partial)
    spectrum = transform(sent, 0) + transform(age_pieces, 1)

    start = position * rows
    faces_z = tuple(lax.dynamic_slice_in_dim(one_face, start, rows, axis=1)[:, :, None, :] for one_face in faces)
    total_z = lax.dynamic_slice_in_dim(face_total, start, rows, axis=1)[:, :, None, :]
    shifted_real = eigenvalues[0][None, None, :, None] + total_z
    eigen_imag = eigenvalues[1][None, None, :, None]
    squared = shifted_real * shifted_real + eigen_imag * eigen_imag
    ratio_real, ratio_imag = lax.optimization_barrier((shifted_real / squared, eigen_imag / squared))

    summed = spectrum
    correction = None
    for sweep_number in range(SWEEPS):
        if sweep_number > 0:
            x_low, x_high = halos(correction, "space", 1)
            z_low, z_high = halos(correction, "tm", 2)
            xm, xp = shifted_pair(correction, x_low, x_high, 1)
            zm, zp = shifted_pair(correction, z_low, z_high, 2)
            ym, yp = zero_shifted(correction, 4)
            moved = (xm, xp, zm, zp, ym, yp)
            total = faces_z[0] * moved[0]
            for one_face, one_moved in zip(faces_z[1:], moved[1:]):
                total = total + one_face * one_moved
            summed = spectrum + total
        correction = jnp.stack(
            [
                summed[0] * ratio_real + summed[1] * ratio_imag,
                summed[1] * ratio_real - summed[0] * ratio_imag,
            ]
        )

    back = []
    for step in range(groups):
        target = (position + step) % groups
        piece = jnp.einsum("lfk,fxzky->lxzy", inverse[step], correction, precision=HIGHEST_PRECISION)
        if step > 0:
            piece = lax.ppermute(piece, "tm", ring_pairs(groups, step))
        back.append(piece)
    arrived = jnp.stack(back)
    update = jnp.concatenate(
        [lax.dynamic_index_in_dim(arrived, (position - j) % groups, axis=0, keepdims=False) for j in range(groups)],
        axis=2,
    )
    return age_field + update


def y_split(stacked, forward, inverse, faces, face_total, eigenvalues, age_field):
    groups = lax.axis_size("tm")
    position = lax.axis_index("tm")
    _, steps_local, width_x, depth_z, length_y = stacked.shape
    total_steps = steps_local * groups
    chunk = length_y // groups

    pieces = []
    for step in range(groups):
        target = (position + step) % groups
        piece = lax.dynamic_slice_in_dim(stacked, target * chunk, chunk, axis=4)
        if step > 0:
            piece = lax.ppermute(piece, "tm", ring_pairs(groups, step))
        pieces.append(piece)

    halves = []
    for part in range(2):
        total = None
        for step in range(groups):
            for field in range(2):
                for local in range(steps_local):
                    weight = forward[field][part][:, step, local][:, None, None, None]
                    term = weight * pieces[step][field, local][None]
                    total = term if total is None else total + term
        halves.append(total)
    spectrum = jnp.stack(halves)


    start = position * chunk
    faces_y = tuple(lax.dynamic_slice_in_dim(one_face, start, chunk, axis=2) for one_face in faces)
    total_y = lax.dynamic_slice_in_dim(face_total, start, chunk, axis=2)
    shifted_real = eigenvalues[0][:, None, None, None] + total_y[None]
    eigen_imag = eigenvalues[1][:, None, None, None]
    squared = shifted_real * shifted_real + eigen_imag * eigen_imag
    ratio_real, ratio_imag = lax.optimization_barrier((shifted_real / squared, eigen_imag / squared))

    summed = spectrum
    correction = None
    for sweep_number in range(SWEEPS):
        if sweep_number > 0:
            x_halo = halos(correction, "space", 2)
            y_halo = column_halos(correction, "tm")
            summed = spectrum + neighbour_sum(correction, faces_y, x_halo, y_halo)
        correction = jnp.stack(
            [
                summed[0] * ratio_real + summed[1] * ratio_imag,
                summed[1] * ratio_real - summed[0] * ratio_imag,
            ]
        )

    back = []
    for step in range(groups):
        target = (position + step) % groups
        piece = jnp.einsum("lfk,fkxzy->lxzy", inverse[step], correction, precision=HIGHEST_PRECISION)
        if step > 0:
            piece = lax.ppermute(piece, "tm", ring_pairs(groups, step))
        back.append(piece)
    arrived = jnp.stack(back)
    update = jnp.concatenate(
        [lax.dynamic_index_in_dim(arrived, (position - j) % groups, axis=0, keepdims=False) for j in range(groups)],
        axis=3,
    )
    return age_field + update


def solution(mesh):
    in_specs = (
        P("tm", "space", None, None),
        P("tm", "space", None, None),
        P("space", None, None),
        P(),
        P(),
    )
    out_specs = P("tm", "space", None, None)
    return jax.shard_map(shards, mesh=mesh, in_specs=in_specs, out_specs=out_specs, check_vma=False)
```

```python
import math

import jax
import jax.numpy as jnp
from jax import lax
from jax.experimental import pallas as pl
from jax.experimental.pallas import tpu as pltpu
from jax.sharding import PartitionSpec as P

SWEEPS = 4


HIGHEST_PRECISION = lax.Precision.HIGHEST


def shift_pairs(count, step):
    return [(i, i + step) for i in range(count) if 0 <= i + step < count]


def halos(array, axis, dim, parts=1):
    count = lax.axis_size(axis)
    index = lax.axis_index(axis)
    length = array.shape[dim]
    last = lax.slice_in_dim(array, length - 1, length, axis=dim)
    first = lax.slice_in_dim(array, 0, 1, axis=dim)
    last = jnp.where(index == count - 1, jnp.zeros_like(last), last)
    first = jnp.where(index == 0, jnp.zeros_like(first), first)
    size = array.shape[0] // parts
    before = [lax.ppermute(last[i * size : (i + 1) * size], axis, ring_pairs(count, 1)) for i in range(parts)]
    after = [lax.ppermute(first[i * size : (i + 1) * size], axis, ring_pairs(count, -1)) for i in range(parts)]
    if parts == 1:
        return before[0], after[0]
    return jnp.concatenate(before, axis=0), jnp.concatenate(after, axis=0)


def column_halos(array, axis):
    count = lax.axis_size(axis)
    before = lax.ppermute(array[..., -1], axis, shift_pairs(count, 1))
    after = lax.ppermute(array[..., 0], axis, shift_pairs(count, -1))
    return before[..., None], after[..., None]


def ring_pairs(count, step):
    return [(i, (i + step) % count) for i in range(count)]


def shifted_pair(field, before, after, dim):
    length = field.shape[dim]
    low = jnp.concatenate([before, lax.slice_in_dim(field, 0, length - 1, axis=dim)], axis=dim)
    high = jnp.concatenate([lax.slice_in_dim(field, 1, length, axis=dim), after], axis=dim)
    return low, high


def zero_shifted(field, dim):
    edge_shape = list(field.shape)
    edge_shape[dim] = 1
    zero = jnp.zeros(edge_shape, field.dtype)
    return shifted_pair(field, zero, zero, dim)


def neighbour_sum(field, faces, x_halo, y_halo):
    nd = field.ndim
    xm, xp = shifted_pair(field, x_halo[0], x_halo[1], nd - 3)
    zm, zp = zero_shifted(field, nd - 2)
    if y_halo is None:
        ym, yp = zero_shifted(field, nd - 1)
    else:
        ym, yp = shifted_pair(field, y_halo[0], y_halo[1], nd - 1)
    moved = (xm, xp, zm, zp, ym, yp)
    result = faces[0] * moved[0]
    for one_face, one_moved in zip(faces[1:], moved[1:]):
        result = result + one_face * one_moved
    return result


def face_halos(conductivity, age_field):
    count = lax.axis_size("space")
    width = conductivity.shape[0]
    last = jnp.concatenate([conductivity[width - 1 :][None], age_field[:, width - 1 :]], axis=0)
    first = jnp.concatenate([conductivity[:1][None], age_field[:, :1]], axis=0)
    index = lax.axis_index("space")
    last = jnp.where(index == count - 1, jnp.zeros_like(last), last)
    first = jnp.where(index == 0, jnp.zeros_like(first), first)
    before = lax.ppermute(last, "space", ring_pairs(count, 1))
    after = lax.ppermute(first, "space", ring_pairs(count, -1))
    age_field, _, _ = lax.optimization_barrier((age_field, last, first))
    return before, after, age_field


def faces_of(conductivity, cond_halo):
    c_low, c_high = shifted_pair(conductivity, cond_halo[0], cond_halo[1], 0)
    z_low, z_high = zero_shifted(conductivity, 1)
    y_low, y_high = zero_shifted(conductivity, 2)
    faces = tuple(0.5 * (conductivity + other) for other in (c_low, c_high, z_low, z_high, y_low, y_high))
    face_total = faces[0]
    for one_face in faces[1:]:
        face_total = face_total + one_face
    return faces, face_total


def spread_kernel(age_ref, source_ref, cond_ref, before_ref, after_ref, out_ref):
    steps, width = age_ref.shape[0], age_ref.shape[1]
    rows, lanes = cond_ref.shape[1], cond_ref.shape[2]
    shape = (rows, lanes)
    moves = []
    for axis, count in ((0, rows), (1, lanes)):
        index = lax.broadcasted_iota(jnp.int32, shape, axis)
        for shift in (1, count - 1):
            moved = pltpu.roll(index, shift, axis)
            moves.append((axis, shift, jnp.abs(moved - index) == 1))

    def neighbours(value):
        return [jnp.where(ok, pltpu.roll(value, shift, axis), 0.0) for axis, shift, ok in moves]

    for x in range(width):
        centre = cond_ref[x]
        low = cond_ref[x - 1] if x > 0 else before_ref[0, 0]
        high = cond_ref[x + 1] if x < width - 1 else after_ref[0, 0]
        faces = [0.5 * (centre + other) for other in [low, high] + neighbours(centre)]
        face_total = faces[0]
        for one_face in faces[1:]:
            face_total = face_total + one_face
        for step in range(steps):
            value = age_ref[step, x]
            low = age_ref[step, x - 1] if x > 0 else before_ref[1 + step, 0]
            high = age_ref[step, x + 1] if x < width - 1 else after_ref[1 + step, 0]
            moved = [low, high] + neighbours(value)
            total = faces[0] * moved[0]
            for one_face, one_moved in zip(faces[1:], moved[1:]):
                total = total + one_face * one_moved
            out_ref[step, x] = source_ref[step, x] + (total - face_total * value)


def phase_tables(products, count):
    angles = 2.0 * math.pi / count * (products % count).astype(jnp.float32)
    return jnp.cos(angles), jnp.sin(angles)


def shards(age_field, source_term, conductivity, memory_weights, eigenvalues):
    groups = lax.axis_size("tm")
    position = lax.axis_index("tm")
    steps_local, width_x, depth_z, length_y = age_field.shape
    total_steps = steps_local * groups

    before, after, age_later = face_halos(conductivity, age_field)
    partial = pl.pallas_call(spread_kernel, out_shape=jax.ShapeDtypeStruct(age_field.shape, jnp.float32))(
        age_field, source_term, conductivity, before, after
    )
    table_at, memory_weights, before, after, _ = lax.optimization_barrier(
        (position, memory_weights, before, after, partial)
    )
    faces, face_total = faces_of(conductivity, (before[0], after[0]))

    frequency = jnp.arange(total_steps, dtype=jnp.int32)
    lag = jnp.arange(total_steps, dtype=jnp.int32)
    cos_w, sin_w = phase_tables(frequency[:, None] * lag[None, :], total_steps)
    weight_real = jnp.sum(memory_weights[None, :] * cos_w, axis=1)[:, None, None]
    weight_imag = -jnp.sum(memory_weights[None, :] * sin_w, axis=1)[:, None, None]
    piece = jnp.arange(groups, dtype=jnp.int32)[None, :, None]
    local = jnp.arange(steps_local, dtype=jnp.int32)[None, None, :]
    step_of = ((table_at - piece) % groups) * steps_local + local
    cos_f, sin_f = phase_tables(frequency[:, None, None] * step_of, total_steps)
    forward = (
        (cos_f, -sin_f),
        (-(weight_real * cos_f + weight_imag * sin_f), weight_real * sin_f - weight_imag * cos_f),
    )
    step_to = ((table_at + piece[0, :, :, None]) % groups) * steps_local + local[0, :, :, None]
    cos_i, sin_i = phase_tables(step_to * frequency[None, None, :], total_steps)
    inverse = jnp.stack([cos_i, -sin_i], axis=2) / total_steps

    if depth_z % groups == 0:
        return z_split(partial, forward, inverse, faces, face_total, eigenvalues, age_field, age_later)
    stacked = jnp.stack([partial, age_field])
    return y_split(stacked, forward, inverse, faces, face_total, eigenvalues, age_field)


def z_split(partial, forward, inverse, faces, face_total, eigenvalues, age_field, age_later):
    groups = lax.axis_size("tm")
    position = lax.axis_index("tm")
    steps_local, width_x, depth_z, length_y = age_field.shape
    total_steps = steps_local * groups
    rows = depth_z // groups

    def ring(field):
        pieces = []
        for step in range(groups):
            target = (position + step) % groups
            piece = lax.dynamic_slice_in_dim(field, target * rows, rows, axis=2)
            if step > 0:
                piece = lax.ppermute(piece, "tm", ring_pairs(groups, step))
            pieces.append(piece)
        return pieces

    def transform(pieces, field):
        weights = jnp.stack([jnp.transpose(forward[field][part], (1, 2, 0)) for part in range(2)])
        total = None
        for step in range(groups):
            term = jnp.sum(
                weights[:, step][:, :, None, None, :, None] * pieces[step][None, :, :, :, None, :], axis=1
            )
            total = term if total is None else total + term
        return total

    age_pieces, partial = lax.optimization_barrier((ring(age_later), partial))
    sent = ring(partial)
    spectrum = transform(sent, 0) + transform(age_pieces, 1)

    start = position * rows
    faces_z = tuple(lax.dynamic_slice_in_dim(one_face, start, rows, axis=1)[:, :, None, :] for one_face in faces)
    total_z = lax.dynamic_slice_in_dim(face_total, start, rows, axis=1)[:, :, None, :]
    shifted_real = eigenvalues[0][None, None, :, None] + total_z
    eigen_imag = eigenvalues[1][None, None, :, None]
    squared = shifted_real * shifted_real + eigen_imag * eigen_imag
    ratio_real, ratio_imag = lax.optimization_barrier((shifted_real / squared, eigen_imag / squared))

    summed = spectrum
    correction = None
    for sweep_number in range(SWEEPS):
        if sweep_number > 0:
            x_low, x_high = halos(correction, "space", 1)
            z_low, z_high = halos(correction, "tm", 2)
            xm, xp = shifted_pair(correction, x_low, x_high, 1)
            zm, zp = shifted_pair(correction, z_low, z_high, 2)
            ym, yp = zero_shifted(correction, 4)
            moved = (xm, xp, zm, zp, ym, yp)
            total = faces_z[0] * moved[0]
            for one_face, one_moved in zip(faces_z[1:], moved[1:]):
                total = total + one_face * one_moved
            summed = spectrum + total
        correction = jnp.stack(
            [
                summed[0] * ratio_real + summed[1] * ratio_imag,
                summed[1] * ratio_real - summed[0] * ratio_imag,
            ]
        )

    back = []
    for step in range(groups):
        target = (position + step) % groups
        piece = jnp.einsum("lfk,fxzky->lxzy", inverse[step], correction, precision=HIGHEST_PRECISION)
        if step > 0:
            piece = lax.ppermute(piece, "tm", ring_pairs(groups, step))
        back.append(piece)
    arrived = jnp.stack(back)
    update = jnp.concatenate(
        [lax.dynamic_index_in_dim(arrived, (position - j) % groups, axis=0, keepdims=False) for j in range(groups)],
        axis=2,
    )
    return age_field + update


def y_split(stacked, forward, inverse, faces, face_total, eigenvalues, age_field):
    groups = lax.axis_size("tm")
    position = lax.axis_index("tm")
    _, steps_local, width_x, depth_z, length_y = stacked.shape
    total_steps = steps_local * groups
    chunk = length_y // groups

    pieces = []
    for step in range(groups):
        target = (position + step) % groups
        piece = lax.dynamic_slice_in_dim(stacked, target * chunk, chunk, axis=4)
        if step > 0:
            piece = lax.ppermute(piece, "tm", ring_pairs(groups, step))
        pieces.append(piece)

    halves = []
    for part in range(2):
        total = None
        for step in range(groups):
            for field in range(2):
                for local in range(steps_local):
                    weight = forward[field][part][:, step, local][:, None, None, None]
                    term = weight * pieces[step][field, local][None]
                    total = term if total is None else total + term
        halves.append(total)
    spectrum = jnp.stack(halves)


    start = position * chunk
    faces_y = tuple(lax.dynamic_slice_in_dim(one_face, start, chunk, axis=2) for one_face in faces)
    total_y = lax.dynamic_slice_in_dim(face_total, start, chunk, axis=2)
    shifted_real = eigenvalues[0][:, None, None, None] + total_y[None]
    eigen_imag = eigenvalues[1][:, None, None, None]
    squared = shifted_real * shifted_real + eigen_imag * eigen_imag
    ratio_real, ratio_imag = lax.optimization_barrier((shifted_real / squared, eigen_imag / squared))

    summed = spectrum
    correction = None
    for sweep_number in range(SWEEPS):
        if sweep_number > 0:
            x_halo = halos(correction, "space", 2)
            y_halo = column_halos(correction, "tm")
            summed = spectrum + neighbour_sum(correction, faces_y, x_halo, y_halo)
        correction = jnp.stack(
            [
                summed[0] * ratio_real + summed[1] * ratio_imag,
                summed[1] * ratio_real - summed[0] * ratio_imag,
            ]
        )

    back = []
    for step in range(groups):
        target = (position + step) % groups
        piece = jnp.einsum("lfk,fkxzy->lxzy", inverse[step], correction, precision=HIGHEST_PRECISION)
        if step > 0:
            piece = lax.ppermute(piece, "tm", ring_pairs(groups, step))
        back.append(piece)
    arrived = jnp.stack(back)
    update = jnp.concatenate(
        [lax.dynamic_index_in_dim(arrived, (position - j) % groups, axis=0, keepdims=False) for j in range(groups)],
        axis=3,
    )
    return age_field + update


def solution(mesh):
    in_specs = (
        P("tm", "space", None, None),
        P("tm", "space", None, None),
        P("space", None, None),
        P(),
        P(),
    )
    out_specs = P("tm", "space", None, None)
    return jax.shard_map(shards, mesh=mesh, in_specs=in_specs, out_specs=out_specs, check_vma=False)
```

```python
import functools
import math

import jax
import jax.numpy as jnp
from jax import lax
from jax.experimental import pallas as pl
from jax.experimental.pallas import tpu as pltpu
from jax.sharding import PartitionSpec as P

SWEEPS = 4


HIGHEST_PRECISION = lax.Precision.HIGHEST


def shift_pairs(count, step):
    return [(i, i + step) for i in range(count) if 0 <= i + step < count]


def halos(array, axis, dim, parts=1):
    count = lax.axis_size(axis)
    index = lax.axis_index(axis)
    length = array.shape[dim]
    last = lax.slice_in_dim(array, length - 1, length, axis=dim)
    first = lax.slice_in_dim(array, 0, 1, axis=dim)
    last = jnp.where(index == count - 1, jnp.zeros_like(last), last)
    first = jnp.where(index == 0, jnp.zeros_like(first), first)
    size = array.shape[0] // parts
    before = [lax.ppermute(last[i * size : (i + 1) * size], axis, ring_pairs(count, 1)) for i in range(parts)]
    after = [lax.ppermute(first[i * size : (i + 1) * size], axis, ring_pairs(count, -1)) for i in range(parts)]
    if parts == 1:
        return before[0], after[0]
    return jnp.concatenate(before, axis=0), jnp.concatenate(after, axis=0)


def column_halos(array, axis):
    count = lax.axis_size(axis)
    before = lax.ppermute(array[..., -1], axis, shift_pairs(count, 1))
    after = lax.ppermute(array[..., 0], axis, shift_pairs(count, -1))
    return before[..., None], after[..., None]


def ring_pairs(count, step):
    return [(i, (i + step) % count) for i in range(count)]


def shifted_pair(field, before, after, dim):
    length = field.shape[dim]
    low = jnp.concatenate([before, lax.slice_in_dim(field, 0, length - 1, axis=dim)], axis=dim)
    high = jnp.concatenate([lax.slice_in_dim(field, 1, length, axis=dim), after], axis=dim)
    return low, high


def zero_shifted(field, dim):
    edge_shape = list(field.shape)
    edge_shape[dim] = 1
    zero = jnp.zeros(edge_shape, field.dtype)
    return shifted_pair(field, zero, zero, dim)


def neighbour_sum(field, faces, x_halo, y_halo):
    nd = field.ndim
    xm, xp = shifted_pair(field, x_halo[0], x_halo[1], nd - 3)
    zm, zp = zero_shifted(field, nd - 2)
    if y_halo is None:
        ym, yp = zero_shifted(field, nd - 1)
    else:
        ym, yp = shifted_pair(field, y_halo[0], y_halo[1], nd - 1)
    moved = (xm, xp, zm, zp, ym, yp)
    result = faces[0] * moved[0]
    for one_face, one_moved in zip(faces[1:], moved[1:]):
        result = result + one_face * one_moved
    return result


def face_halos(conductivity, age_field):
    count = lax.axis_size("space")
    width = conductivity.shape[0]
    last = jnp.concatenate([conductivity[width - 1 :][None], age_field[:, width - 1 :]], axis=0)
    first = jnp.concatenate([conductivity[:1][None], age_field[:, :1]], axis=0)
    index = lax.axis_index("space")
    last = jnp.where(index == count - 1, jnp.zeros_like(last), last)
    first = jnp.where(index == 0, jnp.zeros_like(first), first)
    before = lax.ppermute(last, "space", ring_pairs(count, 1))
    after = lax.ppermute(first, "space", ring_pairs(count, -1))
    age_field, _, _ = lax.optimization_barrier((age_field, last, first))
    return before, after, age_field


def faces_of(conductivity, cond_halo):
    c_low, c_high = shifted_pair(conductivity, cond_halo[0], cond_halo[1], 0)
    z_low, z_high = zero_shifted(conductivity, 1)
    y_low, y_high = zero_shifted(conductivity, 2)
    faces = tuple(0.5 * (conductivity + other) for other in (c_low, c_high, z_low, z_high, y_low, y_high))
    face_total = faces[0]
    for one_face in faces[1:]:
        face_total = face_total + one_face
    return faces, face_total


def spread_kernel(age_ref, source_ref, cond_ref, before_ref, after_ref, out_ref, chunks=0):
    steps, width = age_ref.shape[0], age_ref.shape[1]
    rows, lanes = cond_ref.shape[1], cond_ref.shape[2]
    shape = (rows, lanes)
    moves = []
    for axis, count in ((0, rows), (1, lanes)):
        index = lax.broadcasted_iota(jnp.int32, shape, axis)
        for shift in (1, count - 1):
            moved = pltpu.roll(index, shift, axis)
            moves.append((axis, shift, jnp.abs(moved - index) == 1))

    def neighbours(value):
        return [jnp.where(ok, pltpu.roll(value, shift, axis), 0.0) for axis, shift, ok in moves]

    for x in range(width):
        centre = cond_ref[x]
        low = cond_ref[x - 1] if x > 0 else before_ref[0, 0]
        high = cond_ref[x + 1] if x < width - 1 else after_ref[0, 0]
        faces = [0.5 * (centre + other) for other in [low, high] + neighbours(centre)]
        face_total = faces[0]
        for one_face in faces[1:]:
            face_total = face_total + one_face
        for step in range(steps):
            value = age_ref[step, x]
            low = age_ref[step, x - 1] if x > 0 else before_ref[1 + step, 0]
            high = age_ref[step, x + 1] if x < width - 1 else after_ref[1 + step, 0]
            moved = [low, high] + neighbours(value)
            total = faces[0] * moved[0]
            for one_face, one_moved in zip(faces[1:], moved[1:]):
                total = total + one_face * one_moved
            result = source_ref[step, x] + (total - face_total * value)
            if chunks:
                size = rows // chunks
                for chunk in range(chunks):
                    out_ref[chunk, step, x] = result[chunk * size : (chunk + 1) * size]
            else:
                out_ref[step, x] = result


def phase_tables(products, count):
    angles = 2.0 * math.pi / count * (products % count).astype(jnp.float32)
    return jnp.cos(angles), jnp.sin(angles)


def shards(age_field, source_term, conductivity, memory_weights, eigenvalues):
    groups = lax.axis_size("tm")
    position = lax.axis_index("tm")
    steps_local, width_x, depth_z, length_y = age_field.shape
    total_steps = steps_local * groups

    before, after, age_later = face_halos(conductivity, age_field)
    chunks = groups if depth_z % groups == 0 else 0
    out_shape = age_field.shape
    if chunks:
        out_shape = (groups, steps_local, width_x, depth_z // groups, length_y)
    partial = pl.pallas_call(
        functools.partial(spread_kernel, chunks=chunks), out_shape=jax.ShapeDtypeStruct(out_shape, jnp.float32)
    )(age_field, source_term, conductivity, before, after)
    table_at, memory_weights, before, after, _ = lax.optimization_barrier(
        (position, memory_weights, before, after, partial)
    )
    faces, face_total = faces_of(conductivity, (before[0], after[0]))

    frequency = jnp.arange(total_steps, dtype=jnp.int32)
    lag = jnp.arange(total_steps, dtype=jnp.int32)
    cos_w, sin_w = phase_tables(frequency[:, None] * lag[None, :], total_steps)
    weight_real = jnp.sum(memory_weights[None, :] * cos_w, axis=1)[:, None, None]
    weight_imag = -jnp.sum(memory_weights[None, :] * sin_w, axis=1)[:, None, None]
    piece = jnp.arange(groups, dtype=jnp.int32)[None, :, None]
    local = jnp.arange(steps_local, dtype=jnp.int32)[None, None, :]
    step_of = ((table_at - piece) % groups) * steps_local + local
    cos_f, sin_f = phase_tables(frequency[:, None, None] * step_of, total_steps)
    forward = (
        (cos_f, -sin_f),
        (-(weight_real * cos_f + weight_imag * sin_f), weight_real * sin_f - weight_imag * cos_f),
    )
    step_to = ((table_at + piece[0, :, :, None]) % groups) * steps_local + local[0, :, :, None]
    cos_i, sin_i = phase_tables(step_to * frequency[None, None, :], total_steps)
    inverse = jnp.stack([cos_i, -sin_i], axis=2) / total_steps

    if depth_z % groups == 0:
        return z_split(partial, forward, inverse, faces, face_total, eigenvalues, age_field, age_later)
    stacked = jnp.stack([partial, age_field])
    return y_split(stacked, forward, inverse, faces, face_total, eigenvalues, age_field)


def z_split(partial, forward, inverse, faces, face_total, eigenvalues, age_field, age_later):
    groups = lax.axis_size("tm")
    position = lax.axis_index("tm")
    steps_local, width_x, depth_z, length_y = age_field.shape
    total_steps = steps_local * groups
    rows = depth_z // groups

    def ring(field, chunked=False):
        pieces = []
        for step in range(groups):
            target = (position + step) % groups
            if chunked:
                piece = lax.dynamic_index_in_dim(field, target, axis=0, keepdims=False)
            else:
                piece = lax.dynamic_slice_in_dim(field, target * rows, rows, axis=2)
            if step > 0:
                piece = lax.ppermute(piece, "tm", ring_pairs(groups, step))
            pieces.append(piece)
        return pieces

    def transform(pieces, field):
        weights = jnp.stack([jnp.transpose(forward[field][part], (1, 2, 0)) for part in range(2)])
        total = None
        for step in range(groups):
            term = jnp.sum(
                weights[:, step][:, :, None, None, :, None] * pieces[step][None, :, :, :, None, :], axis=1
            )
            total = term if total is None else total + term
        return total

    age_pieces, partial = lax.optimization_barrier((ring(age_later), partial))
    sent = ring(partial, chunked=True)
    spectrum = transform(sent, 0) + transform(age_pieces, 1)

    start = position * rows
    faces_z = tuple(lax.dynamic_slice_in_dim(one_face, start, rows, axis=1)[:, :, None, :] for one_face in faces)
    total_z = lax.dynamic_slice_in_dim(face_total, start, rows, axis=1)[:, :, None, :]
    shifted_real = eigenvalues[0][None, None, :, None] + total_z
    eigen_imag = eigenvalues[1][None, None, :, None]
    squared = shifted_real * shifted_real + eigen_imag * eigen_imag
    ratio_real, ratio_imag = lax.optimization_barrier((shifted_real / squared, eigen_imag / squared))

    summed = spectrum
    correction = None
    for sweep_number in range(SWEEPS):
        if sweep_number > 0:
            x_low, x_high = halos(correction, "space", 1)
            z_low, z_high = halos(correction, "tm", 2)
            xm, xp = shifted_pair(correction, x_low, x_high, 1)
            zm, zp = shifted_pair(correction, z_low, z_high, 2)
            ym, yp = zero_shifted(correction, 4)
            moved = (xm, xp, zm, zp, ym, yp)
            total = faces_z[0] * moved[0]
            for one_face, one_moved in zip(faces_z[1:], moved[1:]):
                total = total + one_face * one_moved
            summed = spectrum + total
        correction = jnp.stack(
            [
                summed[0] * ratio_real + summed[1] * ratio_imag,
                summed[1] * ratio_real - summed[0] * ratio_imag,
            ]
        )

    back = []
    for step in range(groups):
        target = (position + step) % groups
        piece = jnp.einsum("lfk,fxzky->lxzy", inverse[step], correction, precision=HIGHEST_PRECISION)
        if step > 0:
            piece = lax.ppermute(piece, "tm", ring_pairs(groups, step))
        back.append(piece)
    arrived = jnp.stack(back)
    update = jnp.concatenate(
        [lax.dynamic_index_in_dim(arrived, (position - j) % groups, axis=0, keepdims=False) for j in range(groups)],
        axis=2,
    )
    return age_field + update


def y_split(stacked, forward, inverse, faces, face_total, eigenvalues, age_field):
    groups = lax.axis_size("tm")
    position = lax.axis_index("tm")
    _, steps_local, width_x, depth_z, length_y = stacked.shape
    total_steps = steps_local * groups
    chunk = length_y // groups

    pieces = []
    for step in range(groups):
        target = (position + step) % groups
        piece = lax.dynamic_slice_in_dim(stacked, target * chunk, chunk, axis=4)
        if step > 0:
            piece = lax.ppermute(piece, "tm", ring_pairs(groups, step))
        pieces.append(piece)

    halves = []
    for part in range(2):
        total = None
        for step in range(groups):
            for field in range(2):
                for local in range(steps_local):
                    weight = forward[field][part][:, step, local][:, None, None, None]
                    term = weight * pieces[step][field, local][None]
                    total = term if total is None else total + term
        halves.append(total)
    spectrum = jnp.stack(halves)


    start = position * chunk
    faces_y = tuple(lax.dynamic_slice_in_dim(one_face, start, chunk, axis=2) for one_face in faces)
    total_y = lax.dynamic_slice_in_dim(face_total, start, chunk, axis=2)
    shifted_real = eigenvalues[0][:, None, None, None] + total_y[None]
    eigen_imag = eigenvalues[1][:, None, None, None]
    squared = shifted_real * shifted_real + eigen_imag * eigen_imag
    ratio_real, ratio_imag = lax.optimization_barrier((shifted_real / squared, eigen_imag / squared))

    summed = spectrum
    correction = None
    for sweep_number in range(SWEEPS):
        if sweep_number > 0:
            x_halo = halos(correction, "space", 2)
            y_halo = column_halos(correction, "tm")
            summed = spectrum + neighbour_sum(correction, faces_y, x_halo, y_halo)
        correction = jnp.stack(
            [
                summed[0] * ratio_real + summed[1] * ratio_imag,
                summed[1] * ratio_real - summed[0] * ratio_imag,
            ]
        )

    back = []
    for step in range(groups):
        target = (position + step) % groups
        piece = jnp.einsum("lfk,fkxzy->lxzy", inverse[step], correction, precision=HIGHEST_PRECISION)
        if step > 0:
            piece = lax.ppermute(piece, "tm", ring_pairs(groups, step))
        back.append(piece)
    arrived = jnp.stack(back)
    update = jnp.concatenate(
        [lax.dynamic_index_in_dim(arrived, (position - j) % groups, axis=0, keepdims=False) for j in range(groups)],
        axis=3,
    )
    return age_field + update


def solution(mesh):
    in_specs = (
        P("tm", "space", None, None),
        P("tm", "space", None, None),
        P("space", None, None),
        P(),
        P(),
    )
    out_specs = P("tm", "space", None, None)
    return jax.shard_map(shards, mesh=mesh, in_specs=in_specs, out_specs=out_specs, check_vma=False)
```

```python
import functools
import math

import jax
import jax.numpy as jnp
from jax import lax
from jax.experimental import pallas as pl
from jax.experimental.pallas import tpu as pltpu
from jax.sharding import PartitionSpec as P

SWEEPS = 4


HIGHEST_PRECISION = lax.Precision.HIGHEST


def shift_pairs(count, step):
    return [(i, i + step) for i in range(count) if 0 <= i + step < count]


def halos(array, axis, dim, parts=1):
    count = lax.axis_size(axis)
    index = lax.axis_index(axis)
    length = array.shape[dim]
    last = lax.slice_in_dim(array, length - 1, length, axis=dim)
    first = lax.slice_in_dim(array, 0, 1, axis=dim)
    last = jnp.where(index == count - 1, jnp.zeros_like(last), last)
    first = jnp.where(index == 0, jnp.zeros_like(first), first)
    size = array.shape[0] // parts
    before = [lax.ppermute(last[i * size : (i + 1) * size], axis, ring_pairs(count, 1)) for i in range(parts)]
    after = [lax.ppermute(first[i * size : (i + 1) * size], axis, ring_pairs(count, -1)) for i in range(parts)]
    if parts == 1:
        return before[0], after[0]
    return jnp.concatenate(before, axis=0), jnp.concatenate(after, axis=0)


def column_halos(array, axis):
    count = lax.axis_size(axis)
    before = lax.ppermute(array[..., -1], axis, shift_pairs(count, 1))
    after = lax.ppermute(array[..., 0], axis, shift_pairs(count, -1))
    return before[..., None], after[..., None]


def ring_pairs(count, step):
    return [(i, (i + step) % count) for i in range(count)]


def shifted_pair(field, before, after, dim):
    length = field.shape[dim]
    low = jnp.concatenate([before, lax.slice_in_dim(field, 0, length - 1, axis=dim)], axis=dim)
    high = jnp.concatenate([lax.slice_in_dim(field, 1, length, axis=dim), after], axis=dim)
    return low, high


def zero_shifted(field, dim):
    edge_shape = list(field.shape)
    edge_shape[dim] = 1
    zero = jnp.zeros(edge_shape, field.dtype)
    return shifted_pair(field, zero, zero, dim)


def neighbour_sum(field, faces, x_halo, y_halo):
    nd = field.ndim
    xm, xp = shifted_pair(field, x_halo[0], x_halo[1], nd - 3)
    zm, zp = zero_shifted(field, nd - 2)
    if y_halo is None:
        ym, yp = zero_shifted(field, nd - 1)
    else:
        ym, yp = shifted_pair(field, y_halo[0], y_halo[1], nd - 1)
    moved = (xm, xp, zm, zp, ym, yp)
    result = faces[0] * moved[0]
    for one_face, one_moved in zip(faces[1:], moved[1:]):
        result = result + one_face * one_moved
    return result


def face_halos(conductivity, age_field):
    count = lax.axis_size("space")
    width = conductivity.shape[0]
    last = jnp.concatenate([conductivity[width - 1 :][None], age_field[:, width - 1 :]], axis=0)
    first = jnp.concatenate([conductivity[:1][None], age_field[:, :1]], axis=0)
    index = lax.axis_index("space")
    last = jnp.where(index == count - 1, jnp.zeros_like(last), last)
    first = jnp.where(index == 0, jnp.zeros_like(first), first)
    before = lax.ppermute(last, "space", ring_pairs(count, 1))
    after = lax.ppermute(first, "space", ring_pairs(count, -1))
    age_field, _, _ = lax.optimization_barrier((age_field, last, first))
    return before, after, age_field


def faces_of(conductivity, cond_halo):
    c_low, c_high = shifted_pair(conductivity, cond_halo[0], cond_halo[1], 0)
    z_low, z_high = zero_shifted(conductivity, 1)
    y_low, y_high = zero_shifted(conductivity, 2)
    faces = tuple(0.5 * (conductivity + other) for other in (c_low, c_high, z_low, z_high, y_low, y_high))
    face_total = faces[0]
    for one_face in faces[1:]:
        face_total = face_total + one_face
    return faces, face_total


def spread_kernel(age_ref, source_ref, cond_ref, before_ref, after_ref, out_ref, chunks=0):
    steps, width = age_ref.shape[0], age_ref.shape[1]
    rows, lanes = cond_ref.shape[1], cond_ref.shape[2]
    shape = (rows, lanes)
    moves = []
    for axis, count in ((0, rows), (1, lanes)):
        index = lax.broadcasted_iota(jnp.int32, shape, axis)
        for shift in (1, count - 1):
            moved = pltpu.roll(index, shift, axis)
            moves.append((axis, shift, jnp.abs(moved - index) == 1))

    def neighbours(value):
        return [jnp.where(ok, pltpu.roll(value, shift, axis), 0.0) for axis, shift, ok in moves]

    for x in range(width):
        centre = cond_ref[x]
        low = cond_ref[x - 1] if x > 0 else before_ref[0, 0]
        high = cond_ref[x + 1] if x < width - 1 else after_ref[0, 0]
        faces = [0.5 * (centre + other) for other in [low, high] + neighbours(centre)]
        face_total = faces[0]
        for one_face in faces[1:]:
            face_total = face_total + one_face
        for step in range(steps):
            value = age_ref[step, x]
            low = age_ref[step, x - 1] if x > 0 else before_ref[1 + step, 0]
            high = age_ref[step, x + 1] if x < width - 1 else after_ref[1 + step, 0]
            moved = [low, high] + neighbours(value)
            total = faces[0] * moved[0]
            for one_face, one_moved in zip(faces[1:], moved[1:]):
                total = total + one_face * one_moved
            result = source_ref[step, x] + (total - face_total * value)
            if chunks:
                size = rows // chunks
                position = lax.axis_index("tm")
                for chunk in range(chunks):
                    out_ref[(chunk - position) % chunks, step, x] = result[chunk * size : (chunk + 1) * size]
            else:
                out_ref[step, x] = result


def phase_tables(products, count):
    angles = 2.0 * math.pi / count * (products % count).astype(jnp.float32)
    return jnp.cos(angles), jnp.sin(angles)


def shards(age_field, source_term, conductivity, memory_weights, eigenvalues):
    groups = lax.axis_size("tm")
    position = lax.axis_index("tm")
    steps_local, width_x, depth_z, length_y = age_field.shape
    total_steps = steps_local * groups

    before, after, age_later = face_halos(conductivity, age_field)
    chunks = groups if depth_z % groups == 0 else 0
    out_shape = age_field.shape
    if chunks:
        out_shape = (groups, steps_local, width_x, depth_z // groups, length_y)
    partial = pl.pallas_call(
        functools.partial(spread_kernel, chunks=chunks), out_shape=jax.ShapeDtypeStruct(out_shape, jnp.float32)
    )(age_field, source_term, conductivity, before, after)
    table_at, memory_weights, before, after, _ = lax.optimization_barrier(
        (position, memory_weights, before, after, partial)
    )
    faces, face_total = faces_of(conductivity, (before[0], after[0]))

    frequency = jnp.arange(total_steps, dtype=jnp.int32)
    lag = jnp.arange(total_steps, dtype=jnp.int32)
    cos_w, sin_w = phase_tables(frequency[:, None] * lag[None, :], total_steps)
    weight_real = jnp.sum(memory_weights[None, :] * cos_w, axis=1)[:, None, None]
    weight_imag = -jnp.sum(memory_weights[None, :] * sin_w, axis=1)[:, None, None]
    piece = jnp.arange(groups, dtype=jnp.int32)[None, :, None]
    local = jnp.arange(steps_local, dtype=jnp.int32)[None, None, :]
    step_of = ((table_at - piece) % groups) * steps_local + local
    cos_f, sin_f = phase_tables(frequency[:, None, None] * step_of, total_steps)
    forward = (
        (cos_f, -sin_f),
        (-(weight_real * cos_f + weight_imag * sin_f), weight_real * sin_f - weight_imag * cos_f),
    )
    step_to = ((table_at + piece[0, :, :, None]) % groups) * steps_local + local[0, :, :, None]
    cos_i, sin_i = phase_tables(step_to * frequency[None, None, :], total_steps)
    inverse = jnp.stack([cos_i, -sin_i], axis=2) / total_steps

    if depth_z % groups == 0:
        return z_split(partial, forward, inverse, faces, face_total, eigenvalues, age_field, age_later)
    stacked = jnp.stack([partial, age_field])
    return y_split(stacked, forward, inverse, faces, face_total, eigenvalues, age_field)


def z_split(partial, forward, inverse, faces, face_total, eigenvalues, age_field, age_later):
    groups = lax.axis_size("tm")
    position = lax.axis_index("tm")
    steps_local, width_x, depth_z, length_y = age_field.shape
    total_steps = steps_local * groups
    rows = depth_z // groups

    def ring(field, chunked=False):
        pieces = []
        for step in range(groups):
            target = (position + step) % groups
            if chunked:
                piece = field[step]
            else:
                piece = lax.dynamic_slice_in_dim(field, target * rows, rows, axis=2)
            if step > 0:
                piece = lax.ppermute(piece, "tm", ring_pairs(groups, step))
            pieces.append(piece)
        return pieces

    def transform(pieces, field):
        weights = jnp.stack([jnp.transpose(forward[field][part], (1, 2, 0)) for part in range(2)])
        total = None
        for step in range(groups):
            term = jnp.sum(
                weights[:, step][:, :, None, None, :, None] * pieces[step][None, :, :, :, None, :], axis=1
            )
            total = term if total is None else total + term
        return total

    age_pieces, partial = lax.optimization_barrier((ring(age_later), partial))
    sent = ring(partial, chunked=True)
    spectrum = transform(sent, 0) + transform(age_pieces, 1)

    start = position * rows
    faces_z = tuple(lax.dynamic_slice_in_dim(one_face, start, rows, axis=1)[:, :, None, :] for one_face in faces)
    total_z = lax.dynamic_slice_in_dim(face_total, start, rows, axis=1)[:, :, None, :]
    shifted_real = eigenvalues[0][None, None, :, None] + total_z
    eigen_imag = eigenvalues[1][None, None, :, None]
    squared = shifted_real * shifted_real + eigen_imag * eigen_imag
    ratio_real, ratio_imag = lax.optimization_barrier((shifted_real / squared, eigen_imag / squared))

    summed = spectrum
    correction = None
    for sweep_number in range(SWEEPS):
        if sweep_number > 0:
            x_low, x_high = halos(correction, "space", 1)
            z_low, z_high = halos(correction, "tm", 2)
            xm, xp = shifted_pair(correction, x_low, x_high, 1)
            zm, zp = shifted_pair(correction, z_low, z_high, 2)
            ym, yp = zero_shifted(correction, 4)
            moved = (xm, xp, zm, zp, ym, yp)
            total = faces_z[0] * moved[0]
            for one_face, one_moved in zip(faces_z[1:], moved[1:]):
                total = total + one_face * one_moved
            summed = spectrum + total
        correction = jnp.stack(
            [
                summed[0] * ratio_real + summed[1] * ratio_imag,
                summed[1] * ratio_real - summed[0] * ratio_imag,
            ]
        )

    back = []
    for step in range(groups):
        target = (position + step) % groups
        piece = jnp.einsum("lfk,fxzky->lxzy", inverse[step], correction, precision=HIGHEST_PRECISION)
        if step > 0:
            piece = lax.ppermute(piece, "tm", ring_pairs(groups, step))
        back.append(piece)
    arrived = jnp.stack(back)
    update = jnp.concatenate(
        [lax.dynamic_index_in_dim(arrived, (position - j) % groups, axis=0, keepdims=False) for j in range(groups)],
        axis=2,
    )
    return age_field + update


def y_split(stacked, forward, inverse, faces, face_total, eigenvalues, age_field):
    groups = lax.axis_size("tm")
    position = lax.axis_index("tm")
    _, steps_local, width_x, depth_z, length_y = stacked.shape
    total_steps = steps_local * groups
    chunk = length_y // groups

    pieces = []
    for step in range(groups):
        target = (position + step) % groups
        piece = lax.dynamic_slice_in_dim(stacked, target * chunk, chunk, axis=4)
        if step > 0:
            piece = lax.ppermute(piece, "tm", ring_pairs(groups, step))
        pieces.append(piece)

    halves = []
    for part in range(2):
        total = None
        for step in range(groups):
            for field in range(2):
                for local in range(steps_local):
                    weight = forward[field][part][:, step, local][:, None, None, None]
                    term = weight * pieces[step][field, local][None]
                    total = term if total is None else total + term
        halves.append(total)
    spectrum = jnp.stack(halves)


    start = position * chunk
    faces_y = tuple(lax.dynamic_slice_in_dim(one_face, start, chunk, axis=2) for one_face in faces)
    total_y = lax.dynamic_slice_in_dim(face_total, start, chunk, axis=2)
    shifted_real = eigenvalues[0][:, None, None, None] + total_y[None]
    eigen_imag = eigenvalues[1][:, None, None, None]
    squared = shifted_real * shifted_real + eigen_imag * eigen_imag
    ratio_real, ratio_imag = lax.optimization_barrier((shifted_real / squared, eigen_imag / squared))

    summed = spectrum
    correction = None
    for sweep_number in range(SWEEPS):
        if sweep_number > 0:
            x_halo = halos(correction, "space", 2)
            y_halo = column_halos(correction, "tm")
            summed = spectrum + neighbour_sum(correction, faces_y, x_halo, y_halo)
        correction = jnp.stack(
            [
                summed[0] * ratio_real + summed[1] * ratio_imag,
                summed[1] * ratio_real - summed[0] * ratio_imag,
            ]
        )

    back = []
    for step in range(groups):
        target = (position + step) % groups
        piece = jnp.einsum("lfk,fkxzy->lxzy", inverse[step], correction, precision=HIGHEST_PRECISION)
        if step > 0:
            piece = lax.ppermute(piece, "tm", ring_pairs(groups, step))
        back.append(piece)
    arrived = jnp.stack(back)
    update = jnp.concatenate(
        [lax.dynamic_index_in_dim(arrived, (position - j) % groups, axis=0, keepdims=False) for j in range(groups)],
        axis=3,
    )
    return age_field + update


def solution(mesh):
    in_specs = (
        P("tm", "space", None, None),
        P("tm", "space", None, None),
        P("space", None, None),
        P(),
        P(),
    )
    out_specs = P("tm", "space", None, None)
    return jax.shard_map(shards, mesh=mesh, in_specs=in_specs, out_specs=out_specs, check_vma=False)
```

```python
import functools
import math

import jax
import jax.numpy as jnp
from jax import lax
from jax.experimental import pallas as pl
from jax.experimental.pallas import tpu as pltpu
from jax.sharding import PartitionSpec as P

SWEEPS = 4


HIGHEST_PRECISION = lax.Precision.HIGHEST


def shift_pairs(count, step):
    return [(i, i + step) for i in range(count) if 0 <= i + step < count]


def halos(array, axis, dim, parts=1):
    count = lax.axis_size(axis)
    index = lax.axis_index(axis)
    length = array.shape[dim]
    last = lax.slice_in_dim(array, length - 1, length, axis=dim)
    first = lax.slice_in_dim(array, 0, 1, axis=dim)
    last = jnp.where(index == count - 1, jnp.zeros_like(last), last)
    first = jnp.where(index == 0, jnp.zeros_like(first), first)
    size = array.shape[0] // parts
    before = [lax.ppermute(last[i * size : (i + 1) * size], axis, ring_pairs(count, 1)) for i in range(parts)]
    after = [lax.ppermute(first[i * size : (i + 1) * size], axis, ring_pairs(count, -1)) for i in range(parts)]
    if parts == 1:
        return before[0], after[0]
    return jnp.concatenate(before, axis=0), jnp.concatenate(after, axis=0)


def column_halos(array, axis):
    count = lax.axis_size(axis)
    before = lax.ppermute(array[..., -1], axis, shift_pairs(count, 1))
    after = lax.ppermute(array[..., 0], axis, shift_pairs(count, -1))
    return before[..., None], after[..., None]


def ring_pairs(count, step):
    return [(i, (i + step) % count) for i in range(count)]


def shifted_pair(field, before, after, dim):
    length = field.shape[dim]
    low = jnp.concatenate([before, lax.slice_in_dim(field, 0, length - 1, axis=dim)], axis=dim)
    high = jnp.concatenate([lax.slice_in_dim(field, 1, length, axis=dim), after], axis=dim)
    return low, high


def zero_shifted(field, dim):
    edge_shape = list(field.shape)
    edge_shape[dim] = 1
    zero = jnp.zeros(edge_shape, field.dtype)
    return shifted_pair(field, zero, zero, dim)


def neighbour_sum(field, faces, x_halo, y_halo):
    nd = field.ndim
    xm, xp = shifted_pair(field, x_halo[0], x_halo[1], nd - 3)
    zm, zp = zero_shifted(field, nd - 2)
    if y_halo is None:
        ym, yp = zero_shifted(field, nd - 1)
    else:
        ym, yp = shifted_pair(field, y_halo[0], y_halo[1], nd - 1)
    moved = (xm, xp, zm, zp, ym, yp)
    result = faces[0] * moved[0]
    for one_face, one_moved in zip(faces[1:], moved[1:]):
        result = result + one_face * one_moved
    return result


def face_halos(conductivity, age_field):
    count = lax.axis_size("space")
    width = conductivity.shape[0]
    last = jnp.concatenate([conductivity[width - 1 :][None], age_field[:, width - 1 :]], axis=0)
    first = jnp.concatenate([conductivity[:1][None], age_field[:, :1]], axis=0)
    index = lax.axis_index("space")
    last = jnp.where(index == count - 1, jnp.zeros_like(last), last)
    first = jnp.where(index == 0, jnp.zeros_like(first), first)
    before = lax.ppermute(last, "space", ring_pairs(count, 1))
    after = lax.ppermute(first, "space", ring_pairs(count, -1))
    age_field, _, _ = lax.optimization_barrier((age_field, last, first))
    return before, after, age_field


def faces_of(conductivity, cond_halo):
    c_low, c_high = shifted_pair(conductivity, cond_halo[0], cond_halo[1], 0)
    z_low, z_high = zero_shifted(conductivity, 1)
    y_low, y_high = zero_shifted(conductivity, 2)
    faces = tuple(0.5 * (conductivity + other) for other in (c_low, c_high, z_low, z_high, y_low, y_high))
    face_total = faces[0]
    for one_face in faces[1:]:
        face_total = face_total + one_face
    return faces, face_total


def spread_kernel(age_ref, source_ref, cond_ref, before_ref, after_ref, out_ref, chunks=0):
    steps, width = age_ref.shape[0], age_ref.shape[1]
    rows, lanes = cond_ref.shape[1], cond_ref.shape[2]
    shape = (rows, lanes)
    moves = []
    for axis, count in ((0, rows), (1, lanes)):
        index = lax.broadcasted_iota(jnp.int32, shape, axis)
        for shift in (1, count - 1):
            moved = pltpu.roll(index, shift, axis)
            moves.append((axis, shift, jnp.abs(moved - index) == 1))

    def neighbours(value):
        return [jnp.where(ok, pltpu.roll(value, shift, axis), 0.0) for axis, shift, ok in moves]

    for x in range(width):
        centre = cond_ref[x]
        low = cond_ref[x - 1] if x > 0 else before_ref[0, 0]
        high = cond_ref[x + 1] if x < width - 1 else after_ref[0, 0]
        faces = [0.5 * (centre + other) for other in [low, high] + neighbours(centre)]
        face_total = faces[0]
        for one_face in faces[1:]:
            face_total = face_total + one_face
        for step in range(steps):
            value = age_ref[step, x]
            low = age_ref[step, x - 1] if x > 0 else before_ref[1 + step, 0]
            high = age_ref[step, x + 1] if x < width - 1 else after_ref[1 + step, 0]
            moved = [low, high] + neighbours(value)
            total = faces[0] * moved[0]
            for one_face, one_moved in zip(faces[1:], moved[1:]):
                total = total + one_face * one_moved
            result = source_ref[step, x] + (total - face_total * value)
            if chunks:
                size = rows // chunks
                position = lax.axis_index("tm")
                for chunk in range(chunks):
                    out_ref[(chunk - position) % chunks, step, x] = result[chunk * size : (chunk + 1) * size]
            else:
                out_ref[step, x] = result


def phase_tables(products, count):
    angles = 2.0 * math.pi / count * (products % count).astype(jnp.float32)
    return jnp.cos(angles), jnp.sin(angles)


def shards(age_field, source_term, conductivity, memory_weights, eigenvalues):
    groups = lax.axis_size("tm")
    position = lax.axis_index("tm")
    steps_local, width_x, depth_z, length_y = age_field.shape
    total_steps = steps_local * groups

    before, after, age_later = face_halos(conductivity, age_field)
    chunks = groups if depth_z % groups == 0 else 0
    out_shape = age_field.shape
    if chunks:
        out_shape = (groups, steps_local, width_x, depth_z // groups, length_y)
    partial = pl.pallas_call(
        functools.partial(spread_kernel, chunks=chunks), out_shape=jax.ShapeDtypeStruct(out_shape, jnp.float32)
    )(age_field, source_term, conductivity, before, after)
    table_at, memory_weights, before, after, _ = lax.optimization_barrier(
        (position, memory_weights, before, after, partial)
    )
    faces, face_total = faces_of(conductivity, (before[0], after[0]))

    frequency = jnp.arange(total_steps, dtype=jnp.int32)
    lag = jnp.arange(total_steps, dtype=jnp.int32)
    cos_w, sin_w = phase_tables(frequency[:, None] * lag[None, :], total_steps)
    weight_real = jnp.sum(memory_weights[None, :] * cos_w, axis=1)[:, None, None]
    weight_imag = -jnp.sum(memory_weights[None, :] * sin_w, axis=1)[:, None, None]
    piece = jnp.arange(groups, dtype=jnp.int32)[None, :, None]
    local = jnp.arange(steps_local, dtype=jnp.int32)[None, None, :]
    step_of = ((table_at - piece) % groups) * steps_local + local
    cos_f, sin_f = phase_tables(frequency[:, None, None] * step_of, total_steps)
    forward = (
        (cos_f, -sin_f),
        (-(weight_real * cos_f + weight_imag * sin_f), weight_real * sin_f - weight_imag * cos_f),
    )
    step_to = ((table_at + piece[0, :, :, None]) % groups) * steps_local + local[0, :, :, None]
    cos_i, sin_i = phase_tables(step_to * frequency[None, None, :], total_steps)
    inverse = jnp.stack([cos_i, -sin_i], axis=2) / total_steps

    if depth_z % groups == 0:
        return z_split(partial, forward, inverse, faces, face_total, eigenvalues, age_field, age_later)
    stacked = jnp.stack([partial, age_field])
    return y_split(stacked, forward, inverse, faces, face_total, eigenvalues, age_field)


def z_split(partial, forward, inverse, faces, face_total, eigenvalues, age_field, age_later):
    groups = lax.axis_size("tm")
    position = lax.axis_index("tm")
    steps_local, width_x, depth_z, length_y = age_field.shape
    total_steps = steps_local * groups
    rows = depth_z // groups

    def ring(field, chunked=False):
        pieces = []
        for step in range(groups):
            target = (position + step) % groups
            if chunked:
                piece = field[step]
            else:
                piece = lax.dynamic_slice_in_dim(field, target * rows, rows, axis=2)
            if step > 0:
                piece = lax.ppermute(piece, "tm", ring_pairs(groups, step))
            pieces.append(piece)
        return pieces

    def transform(pieces, field):
        weights = jnp.stack([jnp.transpose(forward[field][part], (1, 2, 0)) for part in range(2)])
        total = None
        for step in range(groups):
            term = jnp.sum(
                weights[:, step][:, :, None, None, :, None] * pieces[step][None, :, :, :, None, :], axis=1
            )
            total = term if total is None else total + term
        return total

    age_pieces, partial = lax.optimization_barrier((ring(age_later), partial))
    sent = ring(partial, chunked=True)
    spectrum = transform(sent, 0) + transform(age_pieces, 1)

    start = position * rows
    faces_z = tuple(lax.dynamic_slice_in_dim(one_face, start, rows, axis=1)[:, :, None, :] for one_face in faces)
    total_z = lax.dynamic_slice_in_dim(face_total, start, rows, axis=1)[:, :, None, :]
    shifted_real = eigenvalues[0][None, None, :, None] + total_z
    eigen_imag = eigenvalues[1][None, None, :, None]
    squared = shifted_real * shifted_real + eigen_imag * eigen_imag
    ratio_real, ratio_imag = shifted_real / squared, eigen_imag / squared

    summed = spectrum
    correction = None
    for sweep_number in range(SWEEPS):
        if sweep_number > 0:
            x_low, x_high = halos(correction, "space", 1)
            z_low, z_high = halos(correction, "tm", 2)
            xm, xp = shifted_pair(correction, x_low, x_high, 1)
            zm, zp = shifted_pair(correction, z_low, z_high, 2)
            ym, yp = zero_shifted(correction, 4)
            moved = (xm, xp, zm, zp, ym, yp)
            total = faces_z[0] * moved[0]
            for one_face, one_moved in zip(faces_z[1:], moved[1:]):
                total = total + one_face * one_moved
            summed = spectrum + total
        correction = jnp.stack(
            [
                summed[0] * ratio_real + summed[1] * ratio_imag,
                summed[1] * ratio_real - summed[0] * ratio_imag,
            ]
        )

    back = []
    for step in range(groups):
        target = (position + step) % groups
        piece = jnp.einsum("lfk,fxzky->lxzy", inverse[step], correction, precision=HIGHEST_PRECISION)
        if step > 0:
            piece = lax.ppermute(piece, "tm", ring_pairs(groups, step))
        back.append(piece)
    arrived = jnp.stack(back)
    update = jnp.concatenate(
        [lax.dynamic_index_in_dim(arrived, (position - j) % groups, axis=0, keepdims=False) for j in range(groups)],
        axis=2,
    )
    return age_field + update


def y_split(stacked, forward, inverse, faces, face_total, eigenvalues, age_field):
    groups = lax.axis_size("tm")
    position = lax.axis_index("tm")
    _, steps_local, width_x, depth_z, length_y = stacked.shape
    total_steps = steps_local * groups
    chunk = length_y // groups

    pieces = []
    for step in range(groups):
        target = (position + step) % groups
        piece = lax.dynamic_slice_in_dim(stacked, target * chunk, chunk, axis=4)
        if step > 0:
            piece = lax.ppermute(piece, "tm", ring_pairs(groups, step))
        pieces.append(piece)

    halves = []
    for part in range(2):
        total = None
        for step in range(groups):
            for field in range(2):
                for local in range(steps_local):
                    weight = forward[field][part][:, step, local][:, None, None, None]
                    term = weight * pieces[step][field, local][None]
                    total = term if total is None else total + term
        halves.append(total)
    spectrum = jnp.stack(halves)


    start = position * chunk
    faces_y = tuple(lax.dynamic_slice_in_dim(one_face, start, chunk, axis=2) for one_face in faces)
    total_y = lax.dynamic_slice_in_dim(face_total, start, chunk, axis=2)
    shifted_real = eigenvalues[0][:, None, None, None] + total_y[None]
    eigen_imag = eigenvalues[1][:, None, None, None]
    squared = shifted_real * shifted_real + eigen_imag * eigen_imag
    ratio_real, ratio_imag = lax.optimization_barrier((shifted_real / squared, eigen_imag / squared))

    summed = spectrum
    correction = None
    for sweep_number in range(SWEEPS):
        if sweep_number > 0:
            x_halo = halos(correction, "space", 2)
            y_halo = column_halos(correction, "tm")
            summed = spectrum + neighbour_sum(correction, faces_y, x_halo, y_halo)
        correction = jnp.stack(
            [
                summed[0] * ratio_real + summed[1] * ratio_imag,
                summed[1] * ratio_real - summed[0] * ratio_imag,
            ]
        )

    back = []
    for step in range(groups):
        target = (position + step) % groups
        piece = jnp.einsum("lfk,fkxzy->lxzy", inverse[step], correction, precision=HIGHEST_PRECISION)
        if step > 0:
            piece = lax.ppermute(piece, "tm", ring_pairs(groups, step))
        back.append(piece)
    arrived = jnp.stack(back)
    update = jnp.concatenate(
        [lax.dynamic_index_in_dim(arrived, (position - j) % groups, axis=0, keepdims=False) for j in range(groups)],
        axis=3,
    )
    return age_field + update


def solution(mesh):
    in_specs = (
        P("tm", "space", None, None),
        P("tm", "space", None, None),
        P("space", None, None),
        P(),
        P(),
    )
    out_specs = P("tm", "space", None, None)
    return jax.shard_map(shards, mesh=mesh, in_specs=in_specs, out_specs=out_specs, check_vma=False)
```
